256 devices in a mesh: gx: 16 (over x, y), gy: 8 (over z), mode: 2 (over core).
Axes of the slice: x: 4, y: 4, z: 8, core: 2. Of those that a mesh axis runs over, the one named last changes fastest.
Arguments:
- state: float32 [4, 64, 512, 2048], P(None, None, 'gx', ('gy', 'mode')), may hold values from -6 to 6
- depth_class: int32 [512, 2048], P('gx', ('gy', 'mode')), may hold values from 0 to 4
- vertical_inverse: float32 [4, 64, 64], replicated, as said below
- height: float32 [512, 2048], P('gx', ('gy', 'mode')), may hold values from -4 to 4
- transport: float32 [2, 512, 2048], P(None, 'gx', ('gy', 'mode')), may hold values from -4 to 4
Outputs:
- state_next: float32 [4, 64, 512, 2048], P(None, None, 'gx', ('gy', 'mode'))
- height_next: float32 [512, 2048], P('gx', ('gy', 'mode'))
- transport_next: float32 [2, 512, 2048], P(None, 'gx', ('gy', 'mode'))
The draws below stay inside these ranges and needn't reach their ends.
Inputs may be any that keep to these rules, and one draw needn't show every extreme that they name: `depth_class`: 0 marks land; a column of class c has its top c * 16 levels active. `vertical_inverse`: entry c is used for columns of class c + 1 and acts on all 64 levels.
All inputs are finite; a program needn't handle non-finite values.
Results may differ from the reference program's by a relative error of at most 0.0003.
Values sent between devices are 32-bit elements; how exact they have to be, the bound alone decides.
No kernel may reach another device: no remote copies, remote signals or barrier semaphores. Data moves between devices by JAX's collectives and lax.ppermute only.
A program may use at most 128 MiB of HBM per device.

```python
import jax
import jax.numpy as jnp
from jax import lax

L = 64
NCLS = 4
SUB = 32
NX = 512
NY = 2048


def draw_vertical_inverse(key, part):
    first_key, second_key = jax.random.split(jax.random.fold_in(key, 11))
    diagonal = jax.random.uniform(first_key, (NCLS, L), jnp.float32, 0.6, 1.0)
    spread = 0.06
    offdiag = spread * jax.random.normal(second_key, (NCLS, L, L), jnp.float32)
    return offdiag + jnp.eye(L, dtype=jnp.float32)[None] * diagonal[:, :, None]


def touch_ends(result, own_key, least, top_value):
    index_at = [jax.random.randint(jax.random.fold_in(own_key, axis), (), 0, length) for axis, length in enumerate(result.shape)]
    main_axis = result.shape.index(max(result.shape))
    beside = index_at[:main_axis] + [(index_at[main_axis] + 1) % result.shape[main_axis]] + index_at[main_axis + 1:]
    return result.at[tuple(index_at)].set(least).at[tuple(beside)].set(top_value)


def block_levels(own_key, shape, pieces, least, largest):
    def one(dim, shards_of):
        draws = jax.random.uniform(jax.random.fold_in(jax.random.fold_in(own_key, 6), dim), (shards_of,), jnp.float32, least / len(pieces), largest / len(pieces))
        return jnp.repeat(jnp.exp(draws), shape[dim] // shards_of).reshape((-1,) + (1,) * (len(shape) - dim - 1))

    level = one(*pieces[0])
    for cut in pieces[1:]:
        level = level * one(*cut)
    return level


def centred(key, extent, deviation, reach, pieces=(), held_as=jnp.bfloat16):
    gain = block_levels(key, extent, pieces, -0.22, 0.18) if pieces else 1.0
    array = jax.random.normal(key, extent, jnp.float32) * deviation * gain
    return jnp.minimum(jnp.maximum(array, -reach), reach).astype(held_as)


def setup_inputs(seed: int = 0) -> dict:
    streams_of = jax.random.split(jax.random.key(seed), 6)
    state = centred(streams_of[0], (4, L, NX, NY), 1.0, 6.0, ((2, 16), (3, 16)), jnp.float32)
    depth_class = touch_ends(jax.random.randint(streams_of[1], (NX, NY), 0, NCLS + 1), jax.random.fold_in(streams_of[1], 1), 0, NCLS).astype(jnp.int32)
    vertical_inverse = draw_vertical_inverse(jax.random.fold_in(streams_of[5], 71), 0)
    height = centred(streams_of[3], (NX, NY), 0.5, 4.0, ((0, 16), (1, 16)), jnp.float32)
    transport = centred(streams_of[4], (2, NX, NY), 0.5, 4.0, ((1, 16), (2, 16)), jnp.float32)
    return dict(state=state, depth_class=depth_class, vertical_inverse=vertical_inverse, height=height, transport=transport)


THERMAL = 0.8
HALINE = 0.6
PRESSURE_SCALE = 4.0
VISCOSITY = 0.1
STEP_TIME = 0.05
WAVE_STEP = 0.5
GRAVITY = 1.0
BOTTOM_DRAG = 0.05
CORIOLIS_BASE = 0.3
CORIOLIS_SLOPE = 0.4


def x_fourth(values):
    return (8.0 * (values[..., 3:-1, 2:-2] - values[..., 1:-3, 2:-2]) - (values[..., 4:, 2:-2] - values[..., :-4, 2:-2])) / 12.0


def y_fourth(values):
    return (8.0 * (values[..., 2:-2, 3:-1] - values[..., 2:-2, 1:-3]) - (values[..., 2:-2, 4:] - values[..., 2:-2, :-4])) / 12.0


def laplace(values):
    center = values[..., 2:-2, 2:-2]
    return values[..., 3:-1, 2:-2] + values[..., 1:-3, 2:-2] + values[..., 2:-2, 3:-1] + values[..., 2:-2, 1:-3] - 4.0 * center


def coriolis_row(anchor, number, total):
    position = (anchor + lax.broadcasted_iota(jnp.int32, (number,), 0)).astype(jnp.float32)
    return (CORIOLIS_BASE + CORIOLIS_SLOPE * (position + 0.5) / total)[None, :]


def baroclinic(state, padded, pressure, active, depth_class, inverse, coriolis):
    levels = state.shape[1]
    center = padded[:, :, 2:-2, 2:-2]
    east_vel = center[2]
    north_vel = center[3]
    tendency = -(east_vel * x_fourth(padded) + north_vel * y_fourth(padded)) + VISCOSITY * laplace(padded)
    zeros_field = jnp.zeros_like(east_vel)
    extra = jnp.stack([zeros_field, zeros_field, -x_fourth(pressure) + coriolis * north_vel, -y_fourth(pressure) - coriolis * east_vel])
    tendency = tendency + extra
    provisional = active * (center + STEP_TIME * tendency)
    solved = jnp.zeros_like(provisional)
    for class_index in range(inverse.shape[0]):
        chosen = (depth_class == class_index + 1).astype(jnp.float32)
        solved = solved + chosen * jnp.einsum('kl,flxy->fkxy', inverse[class_index], provisional, precision=lax.Precision.HIGHEST)
    updated = active * solved + (1.0 - active) * state
    forcing = jnp.sum(active * tendency[2:4], axis=1) / levels
    return updated, forcing


def shrink(values):
    return values[..., 1:-1, 1:-1]


def x_slope(values):
    return (values[2:, 1:-1] - values[:-2, 1:-1]) * 0.5


def y_slope(values):
    return (values[1:-1, 2:] - values[1:-1, :-2]) * 0.5


def substep(moving, fixed_fields, coriolis):
    surface, east_flow, north_flow = moving[0], moving[1], moving[2]
    column_depth = fixed_fields[2]
    sea_mask = (column_depth > 0.0).astype(jnp.float32)
    surface_mid = shrink(sea_mask) * (shrink(surface) - WAVE_STEP * (x_slope(east_flow) + y_slope(north_flow)))
    sea_inner = shrink(shrink(sea_mask))
    depth_inner = shrink(shrink(column_depth))
    force_east = shrink(shrink(fixed_fields[0]))
    force_north = shrink(shrink(fixed_fields[1]))
    coriolis_inner = coriolis[:, 2:-2]
    east_old = shrink(shrink(east_flow))
    north_old = shrink(shrink(north_flow))
    east_new = sea_inner * (east_old + WAVE_STEP * (-GRAVITY * depth_inner * x_slope(surface_mid) + coriolis_inner * north_old + force_east - BOTTOM_DRAG * east_old))
    north_new = sea_inner * (north_old + WAVE_STEP * (-GRAVITY * depth_inner * y_slope(surface_mid) - coriolis_inner * east_new + force_north - BOTTOM_DRAG * north_old))
    return jnp.stack([shrink(surface_mid), east_new, north_new])


def finish(updated, waves, active, depth_class, level_block, levels):
    counted = jnp.maximum(depth_class * level_block, 1).astype(jnp.float32)
    safe_depth = jnp.maximum(depth_class, 1).astype(jnp.float32) * level_block / levels
    column_means = jnp.sum(active * updated[2:4], axis=1) / counted
    carried = waves[1:3] / safe_depth
    velocity = updated[2:4] + active * (carried - column_means)[:, None]
    return jnp.concatenate([updated[0:2], velocity], axis=0)


def reference(state, depth_class, vertical_inverse, height, transport):
    levels = L
    level_block = L // NCLS
    level_ids = lax.broadcasted_iota(jnp.int32, (levels, 1, 1), 0)
    active = (level_ids < depth_class[None] * level_block).astype(jnp.float32)
    masked = state * active[None]
    padded = jnp.pad(masked, ((0, 0), (0, 0), (2, 2), (2, 2)))
    density = -THERMAL * padded[0] + HALINE * padded[1]
    pressure = (PRESSURE_SCALE / levels) * jnp.cumsum(density, axis=0)
    coriolis = coriolis_row(0, NY, NY)[0]
    updated, forcing = baroclinic(state, padded, pressure, active, depth_class, vertical_inverse, coriolis)
    column_depth = depth_class.astype(jnp.float32) * level_block / levels
    sea_mask = (depth_class > 0).astype(jnp.float32)
    moving = jnp.stack([height, transport[0], transport[1]]) * sea_mask
    fixed_fields = jnp.pad(jnp.stack([forcing[0], forcing[1], column_depth]), ((0, 0), (2, 2), (2, 2)))
    coriolis_wide = coriolis_row(-2, NY + 4, NY)

    def turn(index, current):
        return substep(jnp.pad(current, ((0, 0), (2, 2), (2, 2))), fixed_fields, coriolis_wide)

    waves = lax.fori_loop(0, SUB, turn, moving)
    state_next = finish(updated, waves, active, depth_class, level_block, levels)
    return state_next, waves[0], waves[1:3]
```

```python
import jax
import jax.numpy as jnp
from jax import lax
from jax.sharding import PartitionSpec as P

SUB = 32


THERMAL = 0.8
HALINE = 0.6
PRESSURE_SCALE = 4.0
VISCOSITY = 0.1
STEP_TIME = 0.05
WAVE_STEP = 0.5
GRAVITY = 1.0
BOTTOM_DRAG = 0.05
CORIOLIS_BASE = 0.3
CORIOLIS_SLOPE = 0.4


def with_halo(cells, sides, width):
    for axis, dim in sides:
        count = lax.axis_size(axis)
        ends = count - 1
        head = lax.slice_in_dim(cells, 0, width, axis=dim)
        tail = lax.slice_in_dim(cells, cells.shape[dim] - width, cells.shape[dim], axis=dim)
        cells = jnp.concatenate(
            [
                lax.ppermute(tail, axis, [(i, (i + 1) % count) for i in range(ends)]),
                cells,
                lax.ppermute(head, axis, [((i + 1) % count, i) for i in range(ends)]),
            ],
            axis=dim,
        )
    return cells


def x_fourth(values):
    return (
        8.0 * (values[..., 3:-1, 2:-2] - values[..., 1:-3, 2:-2])
        - (values[..., 4:, 2:-2] - values[..., :-4, 2:-2])
    ) / 12.0


def y_fourth(values):
    return (
        8.0 * (values[..., 2:-2, 3:-1] - values[..., 2:-2, 1:-3])
        - (values[..., 2:-2, 4:] - values[..., 2:-2, :-4])
    ) / 12.0


def laplace(values):
    center = values[..., 2:-2, 2:-2]
    return (
        values[..., 3:-1, 2:-2]
        + values[..., 1:-3, 2:-2]
        + values[..., 2:-2, 3:-1]
        + values[..., 2:-2, 1:-3]
        - 4.0 * center
    )


def coriolis_row(anchor, number, total):
    position = (anchor + lax.broadcasted_iota(jnp.int32, (number,), 0)).astype(jnp.float32)
    return (CORIOLIS_BASE + CORIOLIS_SLOPE * (position + 0.5) / total)[None, :]


def baroclinic(state, padded, pressure, active, depth_class, inverse, coriolis):
    levels = state.shape[1]
    center = padded[:, :, 2:-2, 2:-2]
    east_vel = center[2]
    north_vel = center[3]
    tendency = -(east_vel * x_fourth(padded) + north_vel * y_fourth(padded)) + VISCOSITY * laplace(
        padded
    )
    zeros_field = jnp.zeros_like(east_vel)
    extra = jnp.stack(
        [
            zeros_field,
            zeros_field,
            -x_fourth(pressure) + coriolis * north_vel,
            -y_fourth(pressure) - coriolis * east_vel,
        ]
    )
    tendency = tendency + extra
    provisional = active * (center + STEP_TIME * tendency)
    solved = jnp.zeros_like(provisional)
    for class_index in range(inverse.shape[0]):
        chosen = (depth_class == class_index + 1).astype(jnp.float32)
        solved = solved + chosen * jnp.einsum(
            "kl,flxy->fkxy", inverse[class_index], provisional, precision=lax.Precision.HIGHEST
        )
    updated = active * solved + (1.0 - active) * state
    forcing = jnp.sum(active * tendency[2:4], axis=1) / levels
    return (updated, forcing)


def shrink(values):
    return values[..., 1:-1, 1:-1]


def x_slope(values):
    return (values[2:, 1:-1] - values[:-2, 1:-1]) * 0.5


def y_slope(values):
    return (values[1:-1, 2:] - values[1:-1, :-2]) * 0.5


def substep(moving, fixed_fields, coriolis):
    surface, east_flow, north_flow = (moving[0], moving[1], moving[2])
    column_depth = fixed_fields[2]
    sea_mask = (column_depth > 0.0).astype(jnp.float32)
    surface_mid = shrink(sea_mask) * (
        shrink(surface) - WAVE_STEP * (x_slope(east_flow) + y_slope(north_flow))
    )
    sea_inner = shrink(shrink(sea_mask))
    depth_inner = shrink(shrink(column_depth))
    force_east = shrink(shrink(fixed_fields[0]))
    force_north = shrink(shrink(fixed_fields[1]))
    coriolis_inner = coriolis[:, 2:-2]
    east_old = shrink(shrink(east_flow))
    north_old = shrink(shrink(north_flow))
    east_new = sea_inner * (
        east_old
        + WAVE_STEP
        * (
            -GRAVITY * depth_inner * x_slope(surface_mid)
            + coriolis_inner * north_old
            + force_east
            - BOTTOM_DRAG * east_old
        )
    )
    north_new = sea_inner * (
        north_old
        + WAVE_STEP
        * (
            -GRAVITY * depth_inner * y_slope(surface_mid)
            - coriolis_inner * east_new
            + force_north
            - BOTTOM_DRAG * north_old
        )
    )
    return jnp.stack([shrink(surface_mid), east_new, north_new])


def finish(updated, waves, active, depth_class, level_block, levels):
    counted = jnp.maximum(depth_class * level_block, 1).astype(jnp.float32)
    safe_depth = jnp.maximum(depth_class, 1).astype(jnp.float32) * level_block / levels
    column_means = jnp.sum(active * updated[2:4], axis=1) / counted
    carried = waves[1:3] / safe_depth
    velocity = updated[2:4] + active * (carried - column_means)[:, None]
    return jnp.concatenate([updated[0:2], velocity], axis=0)


def wide_halo(cells, axis, dim, width):
    count = lax.axis_size(axis)
    size = cells.shape[dim]
    before, after = [], []
    remaining, hop = width, 1
    while remaining > 0:
        take = min(size, remaining)
        tail = lax.slice_in_dim(cells, size - take, size, axis=dim)
        head = lax.slice_in_dim(cells, 0, take, axis=dim)
        if hop < count:
            from_before = lax.ppermute(tail, axis, [(i, i + hop) for i in range(count - hop)])
            from_after = lax.ppermute(head, axis, [(i + hop, i) for i in range(count - hop)])
        else:
            from_before = jnp.zeros_like(tail)
            from_after = jnp.zeros_like(head)
        before.insert(0, from_before)
        after.append(from_after)
        remaining -= take
        hop += 1
    return jnp.concatenate(before + [cells] + after, axis=dim)


def body(state, depth_class, vertical_inverse, height, transport):
    levels = state.shape[1]
    level_block = levels // vertical_inverse.shape[0]
    y_cells = depth_class.shape[1]
    level_ids = lax.broadcasted_iota(jnp.int32, (levels, 1, 1), 0)
    active = (level_ids < depth_class[None] * level_block).astype(jnp.float32)
    masked = state * active[None]
    padded = with_halo(masked, (("gx", 2), (("gy", "mode"), 3)), 2)
    column_blocks = lax.axis_size(("gy", "mode"))
    anchor = lax.axis_index(("gy", "mode")) * y_cells
    coriolis = coriolis_row(anchor, y_cells, y_cells * column_blocks)[0]
    density = -THERMAL * padded[0] + HALINE * padded[1]
    row_ids = lax.broadcasted_iota(jnp.int32, (levels, levels), 0)
    col_ids = lax.broadcasted_iota(jnp.int32, (levels, levels), 1)
    lower_ones = (row_ids >= col_ids).astype(jnp.float32)
    pressure = (
        PRESSURE_SCALE
        / levels
        * jnp.einsum("kl,lxy->kxy", lower_ones, density, precision=lax.Precision.HIGHEST)
    )
    updated, forcing = baroclinic(
        state, padded, pressure, active, depth_class, vertical_inverse, coriolis
    )
    column_depth = depth_class.astype(jnp.float32) * level_block / levels
    sea_mask = (depth_class > 0).astype(jnp.float32)
    moving = jnp.stack([height, transport[0], transport[1]]) * sea_mask
    fields = jnp.stack([moving[0], moving[1], moving[2], forcing[0], forcing[1], column_depth])
    rim = 2 * SUB
    fields = wide_halo(fields, "gx", 1, rim)
    fields = wide_halo(fields, ("gy", "mode"), 2, rim)
    moving_wide = fields[0:3]
    fixed_wide = jnp.pad(fields[3:6], ((0, 0), (2, 2), (2, 2)))
    coriolis_wide = coriolis_row(
        anchor - rim - 2, y_cells + 2 * rim + 4, y_cells * column_blocks
    )

    def turn(index, current):
        return substep(jnp.pad(current, ((0, 0), (2, 2), (2, 2))), fixed_wide, coriolis_wide)

    waves_wide = lax.fori_loop(0, SUB, turn, moving_wide)
    x_cells = depth_class.shape[0]
    waves = waves_wide[:, rim : rim + x_cells, rim : rim + y_cells]
    state_next = finish(updated, waves, active, depth_class, level_block, levels)
    return (state_next, waves[0], waves[1:3])


def solution(mesh):
    placed = (
        P(None, None, "gx", ("gy", "mode")),
        P("gx", ("gy", "mode")),
        P(),
        P("gx", ("gy", "mode")),
        P(None, "gx", ("gy", "mode")),
    )
    return jax.shard_map(
        body,
        mesh=mesh,
        in_specs=placed,
        out_specs=(
            P(None, None, "gx", ("gy", "mode")),
            P("gx", ("gy", "mode")),
            P(None, "gx", ("gy", "mode")),
        ),
        check_vma=False,
    )
```

```python
import jax
import jax.numpy as jnp
from jax import lax
from jax.experimental import pallas as pl
from jax.experimental.pallas import tpu as pltpu
from jax.sharding import PartitionSpec as P

SUB = 32


THERMAL = 0.8
HALINE = 0.6
PRESSURE_SCALE = 4.0
VISCOSITY = 0.1
STEP_TIME = 0.05
WAVE_STEP = 0.5
GRAVITY = 1.0
BOTTOM_DRAG = 0.05
CORIOLIS_BASE = 0.3
CORIOLIS_SLOPE = 0.4


def with_halo(cells, sides, width):
    for axis, dim in sides:
        count = lax.axis_size(axis)
        ends = count - 1
        head = lax.slice_in_dim(cells, 0, width, axis=dim)
        tail = lax.slice_in_dim(cells, cells.shape[dim] - width, cells.shape[dim], axis=dim)
        cells = jnp.concatenate(
            [
                lax.ppermute(tail, axis, [(i, (i + 1) % count) for i in range(ends)]),
                cells,
                lax.ppermute(head, axis, [((i + 1) % count, i) for i in range(ends)]),
            ],
            axis=dim,
        )
    return cells


def x_fourth(values):
    return (
        8.0 * (values[..., 3:-1, 2:-2] - values[..., 1:-3, 2:-2])
        - (values[..., 4:, 2:-2] - values[..., :-4, 2:-2])
    ) / 12.0


def y_fourth(values):
    return (
        8.0 * (values[..., 2:-2, 3:-1] - values[..., 2:-2, 1:-3])
        - (values[..., 2:-2, 4:] - values[..., 2:-2, :-4])
    ) / 12.0


def laplace(values):
    center = values[..., 2:-2, 2:-2]
    return (
        values[..., 3:-1, 2:-2]
        + values[..., 1:-3, 2:-2]
        + values[..., 2:-2, 3:-1]
        + values[..., 2:-2, 1:-3]
        - 4.0 * center
    )


def coriolis_row(anchor, number, total):
    position = (anchor + lax.broadcasted_iota(jnp.int32, (number,), 0)).astype(jnp.float32)
    return (CORIOLIS_BASE + CORIOLIS_SLOPE * (position + 0.5) / total)[None, :]


def baroclinic(state, padded, pressure, active, depth_class, inverse, coriolis):
    levels = state.shape[1]
    center = padded[:, :, 2:-2, 2:-2]
    east_vel = center[2]
    north_vel = center[3]
    tendency = -(east_vel * x_fourth(padded) + north_vel * y_fourth(padded)) + VISCOSITY * laplace(
        padded
    )
    zeros_field = jnp.zeros_like(east_vel)
    extra = jnp.stack(
        [
            zeros_field,
            zeros_field,
            -x_fourth(pressure) + coriolis * north_vel,
            -y_fourth(pressure) - coriolis * east_vel,
        ]
    )
    tendency = tendency + extra
    provisional = active * (center + STEP_TIME * tendency)
    solved = jnp.zeros_like(provisional)
    for class_index in range(inverse.shape[0]):
        chosen = (depth_class == class_index + 1).astype(jnp.float32)
        solved = solved + chosen * jnp.einsum(
            "kl,flxy->fkxy", inverse[class_index], provisional, precision=lax.Precision.HIGHEST
        )
    updated = active * solved + (1.0 - active) * state
    forcing = jnp.sum(active * tendency[2:4], axis=1) / levels
    return (updated, forcing)


def shrink(values):
    return values[..., 1:-1, 1:-1]


def x_slope(values):
    return (values[2:, 1:-1] - values[:-2, 1:-1]) * 0.5


def y_slope(values):
    return (values[1:-1, 2:] - values[1:-1, :-2]) * 0.5


def substep(moving, fixed_fields, coriolis):
    surface, east_flow, north_flow = (moving[0], moving[1], moving[2])
    column_depth = fixed_fields[2]
    sea_mask = (column_depth > 0.0).astype(jnp.float32)
    surface_mid = shrink(sea_mask) * (
        shrink(surface) - WAVE_STEP * (x_slope(east_flow) + y_slope(north_flow))
    )
    sea_inner = shrink(shrink(sea_mask))
    depth_inner = shrink(shrink(column_depth))
    force_east = shrink(shrink(fixed_fields[0]))
    force_north = shrink(shrink(fixed_fields[1]))
    coriolis_inner = coriolis[:, 2:-2]
    east_old = shrink(shrink(east_flow))
    north_old = shrink(shrink(north_flow))
    east_new = sea_inner * (
        east_old
        + WAVE_STEP
        * (
            -GRAVITY * depth_inner * x_slope(surface_mid)
            + coriolis_inner * north_old
            + force_east
            - BOTTOM_DRAG * east_old
        )
    )
    north_new = sea_inner * (
        north_old
        + WAVE_STEP
        * (
            -GRAVITY * depth_inner * y_slope(surface_mid)
            - coriolis_inner * east_new
            + force_north
            - BOTTOM_DRAG * north_old
        )
    )
    return jnp.stack([shrink(surface_mid), east_new, north_new])


def finish(updated, waves, active, depth_class, level_block, levels):
    counted = jnp.maximum(depth_class * level_block, 1).astype(jnp.float32)
    safe_depth = jnp.maximum(depth_class, 1).astype(jnp.float32) * level_block / levels
    column_means = jnp.sum(active * updated[2:4], axis=1) / counted
    carried = waves[1:3] / safe_depth
    velocity = updated[2:4] + active * (carried - column_means)[:, None]
    return jnp.concatenate([updated[0:2], velocity], axis=0)


def wide_halo(cells, axis, dim, width):
    count = lax.axis_size(axis)
    size = cells.shape[dim]
    before, after = [], []
    remaining, hop = width, 1
    while remaining > 0:
        take = min(size, remaining)
        tail = lax.slice_in_dim(cells, size - take, size, axis=dim)
        head = lax.slice_in_dim(cells, 0, take, axis=dim)
        if hop < count:
            from_before = lax.ppermute(tail, axis, [(i, i + hop) for i in range(count - hop)])
            from_after = lax.ppermute(head, axis, [(i + hop, i) for i in range(count - hop)])
        else:
            from_before = jnp.zeros_like(tail)
            from_after = jnp.zeros_like(head)
        before.insert(0, from_before)
        after.append(from_after)
        remaining -= take
        hop += 1
    return jnp.concatenate(before + [cells] + after, axis=dim)


def wave_kernel(moving_ref, fixed_ref, coriolis_ref, out_ref):
    rows, cols = moving_ref.shape[1], moving_ref.shape[2]
    column_depth = fixed_ref[2]
    sea_mask = (column_depth > 0.0).astype(jnp.float32)
    force_east = fixed_ref[0]
    force_north = fixed_ref[1]
    coriolis = jnp.broadcast_to(coriolis_ref[0:1, :], (rows, cols))

    def x_slope_rolled(values):
        return (pltpu.roll(values, rows - 1, 0) - pltpu.roll(values, 1, 0)) * 0.5

    def y_slope_rolled(values):
        return (pltpu.roll(values, cols - 1, 1) - pltpu.roll(values, 1, 1)) * 0.5

    out_ref[...] = moving_ref[...]

    def step(index, carry):
        surface = out_ref[0]
        east_old = out_ref[1]
        north_old = out_ref[2]
        surface_mid = sea_mask * (
            surface - WAVE_STEP * (x_slope_rolled(east_old) + y_slope_rolled(north_old))
        )
        east_new = sea_mask * (
            east_old
            + WAVE_STEP
            * (
                -GRAVITY * column_depth * x_slope_rolled(surface_mid)
                + coriolis * north_old
                + force_east
                - BOTTOM_DRAG * east_old
            )
        )
        north_new = sea_mask * (
            north_old
            + WAVE_STEP
            * (
                -GRAVITY * column_depth * y_slope_rolled(surface_mid)
                - coriolis * east_new
                + force_north
                - BOTTOM_DRAG * north_old
            )
        )
        out_ref[0] = surface_mid
        out_ref[1] = east_new
        out_ref[2] = north_new
        return carry

    lax.fori_loop(0, SUB, step, 0)


def local_waves(moving, fixed, coriolis):
    rows, cols = moving.shape[1], moving.shape[2]
    elements = rows * cols
    return pl.pallas_call(
        wave_kernel,
        out_shape=jax.ShapeDtypeStruct(moving.shape, jnp.float32),
        in_specs=[pl.BlockSpec(memory_space=pltpu.VMEM)] * 3,
        out_specs=pl.BlockSpec(memory_space=pltpu.VMEM),
        cost_estimate=pl.CostEstimate(
            flops=SUB * 40 * elements, transcendentals=0, bytes_accessed=4 * 9 * elements
        ),
    )(moving, fixed, coriolis)


def body(state, depth_class, vertical_inverse, height, transport):
    levels = state.shape[1]
    level_block = levels // vertical_inverse.shape[0]
    y_cells = depth_class.shape[1]
    level_ids = lax.broadcasted_iota(jnp.int32, (levels, 1, 1), 0)
    active = (level_ids < depth_class[None] * level_block).astype(jnp.float32)
    masked = state * active[None]
    padded = with_halo(masked, (("gx", 2), (("gy", "mode"), 3)), 2)
    column_blocks = lax.axis_size(("gy", "mode"))
    anchor = lax.axis_index(("gy", "mode")) * y_cells
    coriolis = coriolis_row(anchor, y_cells, y_cells * column_blocks)[0]
    density = -THERMAL * padded[0] + HALINE * padded[1]
    row_ids = lax.broadcasted_iota(jnp.int32, (levels, levels), 0)
    col_ids = lax.broadcasted_iota(jnp.int32, (levels, levels), 1)
    lower_ones = (row_ids >= col_ids).astype(jnp.float32)
    pressure = (
        PRESSURE_SCALE
        / levels
        * jnp.einsum("kl,lxy->kxy", lower_ones, density, precision=lax.Precision.HIGHEST)
    )
    updated, forcing = baroclinic(
        state, padded, pressure, active, depth_class, vertical_inverse, coriolis
    )
    column_depth = depth_class.astype(jnp.float32) * level_block / levels
    sea_mask = (depth_class > 0).astype(jnp.float32)
    moving = jnp.stack([height, transport[0], transport[1]]) * sea_mask
    fields = jnp.stack([moving[0], moving[1], moving[2], forcing[0], forcing[1], column_depth])
    rim = 2 * SUB
    fields = wide_halo(fields, "gx", 1, rim)
    fields = wide_halo(fields, ("gy", "mode"), 2, rim)
    coriolis_wide = jnp.broadcast_to(
        coriolis_row(anchor - rim, y_cells + 2 * rim, y_cells * column_blocks), (8, y_cells + 2 * rim)
    )
    waves_wide = local_waves(fields[0:3], fields[3:6], coriolis_wide)
    x_cells = depth_class.shape[0]
    waves = waves_wide[:, rim : rim + x_cells, rim : rim + y_cells]
    state_next = finish(updated, waves, active, depth_class, level_block, levels)
    return (state_next, waves[0], waves[1:3])


def solution(mesh):
    placed = (
        P(None, None, "gx", ("gy", "mode")),
        P("gx", ("gy", "mode")),
        P(),
        P("gx", ("gy", "mode")),
        P(None, "gx", ("gy", "mode")),
    )
    return jax.shard_map(
        body,
        mesh=mesh,
        in_specs=placed,
        out_specs=(
            P(None, None, "gx", ("gy", "mode")),
            P("gx", ("gy", "mode")),
            P(None, "gx", ("gy", "mode")),
        ),
        check_vma=False,
    )
```

```python
import jax
import jax.numpy as jnp
from jax import lax
from jax.experimental import pallas as pl
from jax.experimental.pallas import tpu as pltpu
from jax.sharding import PartitionSpec as P

SUB = 32


THERMAL = 0.8
HALINE = 0.6
PRESSURE_SCALE = 4.0
VISCOSITY = 0.1
STEP_TIME = 0.05
WAVE_STEP = 0.5
GRAVITY = 1.0
BOTTOM_DRAG = 0.05
CORIOLIS_BASE = 0.3
CORIOLIS_SLOPE = 0.4


def with_halo(cells, sides, width):
    for axis, dim in sides:
        count = lax.axis_size(axis)
        ends = count - 1
        head = lax.slice_in_dim(cells, 0, width, axis=dim)
        tail = lax.slice_in_dim(cells, cells.shape[dim] - width, cells.shape[dim], axis=dim)
        cells = jnp.concatenate(
            [
                lax.ppermute(tail, axis, [(i, (i + 1) % count) for i in range(ends)]),
                cells,
                lax.ppermute(head, axis, [((i + 1) % count, i) for i in range(ends)]),
            ],
            axis=dim,
        )
    return cells


def cross_halo(cells, x_axis, x_dim, y_axis, y_dim, width):
    pieces = []
    for axis, dim in ((x_axis, x_dim), (y_axis, y_dim)):
        count = lax.axis_size(axis)
        ends = count - 1
        head = lax.slice_in_dim(cells, 0, width, axis=dim)
        tail = lax.slice_in_dim(cells, cells.shape[dim] - width, cells.shape[dim], axis=dim)
        pieces.append(
            (
                lax.ppermute(tail, axis, [(i, (i + 1) % count) for i in range(ends)]),
                lax.ppermute(head, axis, [((i + 1) % count, i) for i in range(ends)]),
            )
        )
    (west, east), (south, north) = pieces
    cells = jnp.concatenate([west, cells, east], axis=x_dim)
    rim = [(0, 0)] * cells.ndim
    rim[x_dim] = (width, width)
    south = jnp.pad(south, rim)
    north = jnp.pad(north, rim)
    return jnp.concatenate([south, cells, north], axis=y_dim)


def x_fourth(values):
    return (
        8.0 * (values[..., 3:-1, 2:-2] - values[..., 1:-3, 2:-2])
        - (values[..., 4:, 2:-2] - values[..., :-4, 2:-2])
    ) / 12.0


def y_fourth(values):
    return (
        8.0 * (values[..., 2:-2, 3:-1] - values[..., 2:-2, 1:-3])
        - (values[..., 2:-2, 4:] - values[..., 2:-2, :-4])
    ) / 12.0


def laplace(values):
    center = values[..., 2:-2, 2:-2]
    return (
        values[..., 3:-1, 2:-2]
        + values[..., 1:-3, 2:-2]
        + values[..., 2:-2, 3:-1]
        + values[..., 2:-2, 1:-3]
        - 4.0 * center
    )


def coriolis_row(anchor, number, total):
    position = (anchor + lax.broadcasted_iota(jnp.int32, (number,), 0)).astype(jnp.float32)
    return (CORIOLIS_BASE + CORIOLIS_SLOPE * (position + 0.5) / total)[None, :]


def baroclinic(state, padded, pressure, active, depth_class, inverse, coriolis):
    levels = state.shape[1]
    center = padded[:, :, 2:-2, 2:-2]
    east_vel = center[2]
    north_vel = center[3]
    tendency = -(east_vel * x_fourth(padded) + north_vel * y_fourth(padded)) + VISCOSITY * laplace(
        padded
    )
    zeros_field = jnp.zeros_like(east_vel)
    extra = jnp.stack(
        [
            zeros_field,
            zeros_field,
            -x_fourth(pressure) + coriolis * north_vel,
            -y_fourth(pressure) - coriolis * east_vel,
        ]
    )
    tendency = tendency + extra
    provisional = active * (center + STEP_TIME * tendency)
    classes = inverse.shape[0]
    levels_out = inverse.shape[1]
    stacked = inverse.reshape(classes * levels_out, inverse.shape[2])
    every = jnp.einsum(
        "kl,flxy->fkxy", stacked, provisional, precision=lax.Precision.HIGHEST
    )
    solved = jnp.zeros_like(provisional)
    for class_index in range(classes):
        chosen = (depth_class == class_index + 1).astype(jnp.float32)
        solved = solved + chosen * every[:, class_index * levels_out : (class_index + 1) * levels_out]
    updated = active * solved + (1.0 - active) * state
    forcing = jnp.sum(active * tendency[2:4], axis=1) / levels
    return (updated, forcing)


def shrink(values):
    return values[..., 1:-1, 1:-1]


def x_slope(values):
    return (values[2:, 1:-1] - values[:-2, 1:-1]) * 0.5


def y_slope(values):
    return (values[1:-1, 2:] - values[1:-1, :-2]) * 0.5


def substep(moving, fixed_fields, coriolis):
    surface, east_flow, north_flow = (moving[0], moving[1], moving[2])
    column_depth = fixed_fields[2]
    sea_mask = (column_depth > 0.0).astype(jnp.float32)
    surface_mid = shrink(sea_mask) * (
        shrink(surface) - WAVE_STEP * (x_slope(east_flow) + y_slope(north_flow))
    )
    sea_inner = shrink(shrink(sea_mask))
    depth_inner = shrink(shrink(column_depth))
    force_east = shrink(shrink(fixed_fields[0]))
    force_north = shrink(shrink(fixed_fields[1]))
    coriolis_inner = coriolis[:, 2:-2]
    east_old = shrink(shrink(east_flow))
    north_old = shrink(shrink(north_flow))
    east_new = sea_inner * (
        east_old
        + WAVE_STEP
        * (
            -GRAVITY * depth_inner * x_slope(surface_mid)
            + coriolis_inner * north_old
            + force_east
            - BOTTOM_DRAG * east_old
        )
    )
    north_new = sea_inner * (
        north_old
        + WAVE_STEP
        * (
            -GRAVITY * depth_inner * y_slope(surface_mid)
            - coriolis_inner * east_new
            + force_north
            - BOTTOM_DRAG * north_old
        )
    )
    return jnp.stack([shrink(surface_mid), east_new, north_new])


def finish(updated, waves, active, depth_class, level_block, levels):
    counted = jnp.maximum(depth_class * level_block, 1).astype(jnp.float32)
    safe_depth = jnp.maximum(depth_class, 1).astype(jnp.float32) * level_block / levels
    column_means = jnp.sum(active * updated[2:4], axis=1) / counted
    carried = waves[1:3] / safe_depth
    velocity = updated[2:4] + active * (carried - column_means)[:, None]
    return jnp.concatenate([updated[0:2], velocity], axis=0)


def wide_halo(cells, axis, dim, width):
    count = lax.axis_size(axis)
    size = cells.shape[dim]
    before, after = [], []
    remaining, hop = width, 1
    while remaining > 0:
        take = min(size, remaining)
        tail = lax.slice_in_dim(cells, size - take, size, axis=dim)
        head = lax.slice_in_dim(cells, 0, take, axis=dim)
        if hop < count:
            from_before = lax.ppermute(tail, axis, [(i, i + hop) for i in range(count - hop)])
            from_after = lax.ppermute(head, axis, [(i + hop, i) for i in range(count - hop)])
        else:
            from_before = jnp.zeros_like(tail)
            from_after = jnp.zeros_like(head)
        before.insert(0, from_before)
        after.append(from_after)
        remaining -= take
        hop += 1
    return jnp.concatenate(before + [cells] + after, axis=dim)


def wave_kernel(moving_ref, fixed_ref, coriolis_ref, out_ref):
    rows, cols = moving_ref.shape[1], moving_ref.shape[2]
    column_depth = fixed_ref[2]
    sea_mask = (column_depth > 0.0).astype(jnp.float32)
    force_east = fixed_ref[0]
    force_north = fixed_ref[1]
    coriolis = jnp.broadcast_to(coriolis_ref[0:1, :], (rows, cols))

    def x_slope_rolled(values):
        return (pltpu.roll(values, rows - 1, 0) - pltpu.roll(values, 1, 0)) * 0.5

    def y_slope_rolled(values):
        return (pltpu.roll(values, cols - 1, 1) - pltpu.roll(values, 1, 1)) * 0.5

    out_ref[...] = moving_ref[...]

    def step(index, carry):
        surface = out_ref[0]
        east_old = out_ref[1]
        north_old = out_ref[2]
        surface_mid = sea_mask * (
            surface - WAVE_STEP * (x_slope_rolled(east_old) + y_slope_rolled(north_old))
        )
        east_new = sea_mask * (
            east_old
            + WAVE_STEP
            * (
                -GRAVITY * column_depth * x_slope_rolled(surface_mid)
                + coriolis * north_old
                + force_east
                - BOTTOM_DRAG * east_old
            )
        )
        north_new = sea_mask * (
            north_old
            + WAVE_STEP
            * (
                -GRAVITY * column_depth * y_slope_rolled(surface_mid)
                - coriolis * east_new
                + force_north
                - BOTTOM_DRAG * north_old
            )
        )
        out_ref[0] = surface_mid
        out_ref[1] = east_new
        out_ref[2] = north_new
        return carry

    lax.fori_loop(0, SUB, step, 0)


def local_waves(moving, fixed, coriolis):
    rows, cols = moving.shape[1], moving.shape[2]
    elements = rows * cols
    return pl.pallas_call(
        wave_kernel,
        out_shape=jax.ShapeDtypeStruct(moving.shape, jnp.float32),
        in_specs=[pl.BlockSpec(memory_space=pltpu.VMEM)] * 3,
        out_specs=pl.BlockSpec(memory_space=pltpu.VMEM),
        cost_estimate=pl.CostEstimate(
            flops=SUB * 40 * elements, transcendentals=0, bytes_accessed=4 * 9 * elements
        ),
    )(moving, fixed, coriolis)


def body(state, depth_class, vertical_inverse, height, transport):
    levels = state.shape[1]
    level_block = levels // vertical_inverse.shape[0]
    y_cells = depth_class.shape[1]
    level_ids = lax.broadcasted_iota(jnp.int32, (levels, 1, 1), 0)
    active = (level_ids < depth_class[None] * level_block).astype(jnp.float32)
    masked = state * active[None]
    padded = cross_halo(masked, "gx", 2, ("gy", "mode"), 3, 2)
    column_blocks = lax.axis_size(("gy", "mode"))
    anchor = lax.axis_index(("gy", "mode")) * y_cells
    coriolis = coriolis_row(anchor, y_cells, y_cells * column_blocks)[0]
    density = -THERMAL * padded[0] + HALINE * padded[1]
    row_ids = lax.broadcasted_iota(jnp.int32, (levels, levels), 0)
    col_ids = lax.broadcasted_iota(jnp.int32, (levels, levels), 1)
    lower_ones = (row_ids >= col_ids).astype(jnp.float32)
    pressure = (
        PRESSURE_SCALE
        / levels
        * jnp.einsum("kl,lxy->kxy", lower_ones, density, precision=lax.Precision.HIGHEST)
    )
    updated, forcing = baroclinic(
        state, padded, pressure, active, depth_class, vertical_inverse, coriolis
    )
    column_depth = depth_class.astype(jnp.float32) * level_block / levels
    sea_mask = (depth_class > 0).astype(jnp.float32)
    moving = jnp.stack([height, transport[0], transport[1]]) * sea_mask
    fields = jnp.stack([moving[0], moving[1], moving[2], forcing[0], forcing[1], column_depth])
    rim = 2 * SUB
    fields = wide_halo(fields, "gx", 1, rim)
    fields = wide_halo(fields, ("gy", "mode"), 2, rim)
    coriolis_wide = jnp.broadcast_to(
        coriolis_row(anchor - rim, y_cells + 2 * rim, y_cells * column_blocks), (8, y_cells + 2 * rim)
    )
    waves_wide = local_waves(fields[0:3], fields[3:6], coriolis_wide)
    x_cells = depth_class.shape[0]
    waves = waves_wide[:, rim : rim + x_cells, rim : rim + y_cells]
    state_next = finish(updated, waves, active, depth_class, level_block, levels)
    return (state_next, waves[0], waves[1:3])


def solution(mesh):
    placed = (
        P(None, None, "gx", ("gy", "mode")),
        P("gx", ("gy", "mode")),
        P(),
        P("gx", ("gy", "mode")),
        P(None, "gx", ("gy", "mode")),
    )
    return jax.shard_map(
        body,
        mesh=mesh,
        in_specs=placed,
        out_specs=(
            P(None, None, "gx", ("gy", "mode")),
            P("gx", ("gy", "mode")),
            P(None, "gx", ("gy", "mode")),
        ),
        check_vma=False,
    )
```

```python
import jax
import jax.numpy as jnp
from jax import lax
from jax.experimental import pallas as pl
from jax.experimental.pallas import tpu as pltpu
from jax.sharding import PartitionSpec as P

SUB = 32


THERMAL = 0.8
HALINE = 0.6
PRESSURE_SCALE = 4.0
VISCOSITY = 0.1
STEP_TIME = 0.05
WAVE_STEP = 0.5
GRAVITY = 1.0
BOTTOM_DRAG = 0.05
CORIOLIS_BASE = 0.3
CORIOLIS_SLOPE = 0.4


def with_halo(cells, sides, width):
    for axis, dim in sides:
        count = lax.axis_size(axis)
        ends = count - 1
        head = lax.slice_in_dim(cells, 0, width, axis=dim)
        tail = lax.slice_in_dim(cells, cells.shape[dim] - width, cells.shape[dim], axis=dim)
        cells = jnp.concatenate(
            [
                lax.ppermute(tail, axis, [(i, (i + 1) % count) for i in range(ends)]),
                cells,
                lax.ppermute(head, axis, [((i + 1) % count, i) for i in range(ends)]),
            ],
            axis=dim,
        )
    return cells


def cross_halo(cells, x_axis, x_dim, y_axis, y_dim, width):
    pieces = []
    for axis, dim in ((x_axis, x_dim), (y_axis, y_dim)):
        count = lax.axis_size(axis)
        ends = count - 1
        head = lax.slice_in_dim(cells, 0, width, axis=dim)
        tail = lax.slice_in_dim(cells, cells.shape[dim] - width, cells.shape[dim], axis=dim)
        pieces.append(
            (
                lax.ppermute(tail, axis, [(i, (i + 1) % count) for i in range(ends)]),
                lax.ppermute(head, axis, [((i + 1) % count, i) for i in range(ends)]),
            )
        )
    (west, east), (south, north) = pieces
    cells = jnp.concatenate([west, cells, east], axis=x_dim)
    rim = [(0, 0)] * cells.ndim
    rim[x_dim] = (width, width)
    south = jnp.pad(south, rim)
    north = jnp.pad(north, rim)
    return jnp.concatenate([south, cells, north], axis=y_dim)


def x_fourth(values):
    return (
        8.0 * (values[..., 3:-1, 2:-2] - values[..., 1:-3, 2:-2])
        - (values[..., 4:, 2:-2] - values[..., :-4, 2:-2])
    ) / 12.0


def y_fourth(values):
    return (
        8.0 * (values[..., 2:-2, 3:-1] - values[..., 2:-2, 1:-3])
        - (values[..., 2:-2, 4:] - values[..., 2:-2, :-4])
    ) / 12.0


def laplace(values):
    center = values[..., 2:-2, 2:-2]
    return (
        values[..., 3:-1, 2:-2]
        + values[..., 1:-3, 2:-2]
        + values[..., 2:-2, 3:-1]
        + values[..., 2:-2, 1:-3]
        - 4.0 * center
    )


def coriolis_row(anchor, number, total):
    position = (anchor + lax.broadcasted_iota(jnp.int32, (number,), 0)).astype(jnp.float32)
    return (CORIOLIS_BASE + CORIOLIS_SLOPE * (position + 0.5) / total)[None, :]


def baroclinic(state, padded, pressure, active, depth_class, inverse, coriolis):
    levels = state.shape[1]
    center = padded[:, :, 2:-2, 2:-2]
    east_vel = center[2]
    north_vel = center[3]
    tendency = -(east_vel * x_fourth(padded) + north_vel * y_fourth(padded)) + VISCOSITY * laplace(
        padded
    )
    zeros_field = jnp.zeros_like(east_vel)
    extra = jnp.stack(
        [
            zeros_field,
            zeros_field,
            -x_fourth(pressure) + coriolis * north_vel,
            -y_fourth(pressure) - coriolis * east_vel,
        ]
    )
    tendency = tendency + extra
    provisional = active * (center + STEP_TIME * tendency)
    classes = inverse.shape[0]
    band = levels // classes
    stacked = jnp.concatenate(
        [inverse[class_index, : band * (class_index + 1)] for class_index in range(classes)], axis=0
    )
    every = jnp.einsum("kl,flxy->fkxy", stacked, provisional, precision=lax.Precision.HIGH)
    starts = [band * class_index * (class_index + 1) // 2 for class_index in range(classes)]
    chosen = [(depth_class == class_index + 1).astype(jnp.float32) for class_index in range(classes)]
    bands = []
    for level_band in range(classes):
        part = jnp.zeros_like(provisional[:, :band])
        for class_index in range(level_band, classes):
            first = starts[class_index] + level_band * band
            part = part + chosen[class_index] * every[:, first : first + band]
        bands.append(part)
    solved = jnp.concatenate(bands, axis=1)
    updated = active * solved + (1.0 - active) * state
    forcing = jnp.sum(active * tendency[2:4], axis=1) / levels
    return (updated, forcing)


def shrink(values):
    return values[..., 1:-1, 1:-1]


def x_slope(values):
    return (values[2:, 1:-1] - values[:-2, 1:-1]) * 0.5


def y_slope(values):
    return (values[1:-1, 2:] - values[1:-1, :-2]) * 0.5


def substep(moving, fixed_fields, coriolis):
    surface, east_flow, north_flow = (moving[0], moving[1], moving[2])
    column_depth = fixed_fields[2]
    sea_mask = (column_depth > 0.0).astype(jnp.float32)
    surface_mid = shrink(sea_mask) * (
        shrink(surface) - WAVE_STEP * (x_slope(east_flow) + y_slope(north_flow))
    )
    sea_inner = shrink(shrink(sea_mask))
    depth_inner = shrink(shrink(column_depth))
    force_east = shrink(shrink(fixed_fields[0]))
    force_north = shrink(shrink(fixed_fields[1]))
    coriolis_inner = coriolis[:, 2:-2]
    east_old = shrink(shrink(east_flow))
    north_old = shrink(shrink(north_flow))
    east_new = sea_inner * (
        east_old
        + WAVE_STEP
        * (
            -GRAVITY * depth_inner * x_slope(surface_mid)
            + coriolis_inner * north_old
            + force_east
            - BOTTOM_DRAG * east_old
        )
    )
    north_new = sea_inner * (
        north_old
        + WAVE_STEP
        * (
            -GRAVITY * depth_inner * y_slope(surface_mid)
            - coriolis_inner * east_new
            + force_north
            - BOTTOM_DRAG * north_old
        )
    )
    return jnp.stack([shrink(surface_mid), east_new, north_new])


def finish(updated, waves, active, depth_class, level_block, levels):
    counted = jnp.maximum(depth_class * level_block, 1).astype(jnp.float32)
    safe_depth = jnp.maximum(depth_class, 1).astype(jnp.float32) * level_block / levels
    column_means = jnp.sum(active * updated[2:4], axis=1) / counted
    carried = waves[1:3] / safe_depth
    velocity = updated[2:4] + active * (carried - column_means)[:, None]
    return jnp.concatenate([updated[0:2], velocity], axis=0)


def wide_halo(cells, axis, dim, width):
    count = lax.axis_size(axis)
    size = cells.shape[dim]
    before, after = [], []
    remaining, hop = width, 1
    while remaining > 0:
        take = min(size, remaining)
        tail = lax.slice_in_dim(cells, size - take, size, axis=dim)
        head = lax.slice_in_dim(cells, 0, take, axis=dim)
        if hop < count:
            from_before = lax.ppermute(tail, axis, [(i, i + hop) for i in range(count - hop)])
            from_after = lax.ppermute(head, axis, [(i + hop, i) for i in range(count - hop)])
        else:
            from_before = jnp.zeros_like(tail)
            from_after = jnp.zeros_like(head)
        before.insert(0, from_before)
        after.append(from_after)
        remaining -= take
        hop += 1
    return jnp.concatenate(before + [cells] + after, axis=dim)


def wave_kernel(moving_ref, fixed_ref, coriolis_ref, out_ref):
    rows, cols = moving_ref.shape[1], moving_ref.shape[2]
    column_depth = fixed_ref[2]
    sea_mask = (column_depth > 0.0).astype(jnp.float32)
    force_east = fixed_ref[0]
    force_north = fixed_ref[1]
    coriolis = jnp.broadcast_to(coriolis_ref[0:1, :], (rows, cols))

    def x_slope_rolled(values):
        return (pltpu.roll(values, rows - 1, 0) - pltpu.roll(values, 1, 0)) * 0.5

    def y_slope_rolled(values):
        return (pltpu.roll(values, cols - 1, 1) - pltpu.roll(values, 1, 1)) * 0.5

    out_ref[...] = moving_ref[...]

    def step(index, carry):
        surface = out_ref[0]
        east_old = out_ref[1]
        north_old = out_ref[2]
        surface_mid = sea_mask * (
            surface - WAVE_STEP * (x_slope_rolled(east_old) + y_slope_rolled(north_old))
        )
        east_new = sea_mask * (
            east_old
            + WAVE_STEP
            * (
                -GRAVITY * column_depth * x_slope_rolled(surface_mid)
                + coriolis * north_old
                + force_east
                - BOTTOM_DRAG * east_old
            )
        )
        north_new = sea_mask * (
            north_old
            + WAVE_STEP
            * (
                -GRAVITY * column_depth * y_slope_rolled(surface_mid)
                - coriolis * east_new
                + force_north
                - BOTTOM_DRAG * north_old
            )
        )
        out_ref[0] = surface_mid
        out_ref[1] = east_new
        out_ref[2] = north_new
        return carry

    lax.fori_loop(0, SUB, step, 0)


def local_waves(moving, fixed, coriolis):
    rows, cols = moving.shape[1], moving.shape[2]
    elements = rows * cols
    return pl.pallas_call(
        wave_kernel,
        out_shape=jax.ShapeDtypeStruct(moving.shape, jnp.float32),
        in_specs=[pl.BlockSpec(memory_space=pltpu.VMEM)] * 3,
        out_specs=pl.BlockSpec(memory_space=pltpu.VMEM),
        cost_estimate=pl.CostEstimate(
            flops=SUB * 40 * elements, transcendentals=0, bytes_accessed=4 * 9 * elements
        ),
    )(moving, fixed, coriolis)


def body(state, depth_class, vertical_inverse, height, transport):
    levels = state.shape[1]
    level_block = levels // vertical_inverse.shape[0]
    y_cells = depth_class.shape[1]
    level_ids = lax.broadcasted_iota(jnp.int32, (levels, 1, 1), 0)
    active = (level_ids < depth_class[None] * level_block).astype(jnp.float32)
    masked = state * active[None]
    padded = cross_halo(masked, "gx", 2, ("gy", "mode"), 3, 2)
    column_blocks = lax.axis_size(("gy", "mode"))
    anchor = lax.axis_index(("gy", "mode")) * y_cells
    coriolis = coriolis_row(anchor, y_cells, y_cells * column_blocks)[0]
    density = -THERMAL * padded[0] + HALINE * padded[1]
    row_ids = lax.broadcasted_iota(jnp.int32, (levels, levels), 0)
    col_ids = lax.broadcasted_iota(jnp.int32, (levels, levels), 1)
    lower_ones = (row_ids >= col_ids).astype(jnp.float32)
    pressure = (
        PRESSURE_SCALE
        / levels
        * jnp.einsum("kl,lxy->kxy", lower_ones, density, precision=lax.Precision.HIGHEST)
    )
    updated, forcing = baroclinic(
        state, padded, pressure, active, depth_class, vertical_inverse, coriolis
    )
    column_depth = depth_class.astype(jnp.float32) * level_block / levels
    sea_mask = (depth_class > 0).astype(jnp.float32)
    moving = jnp.stack([height, transport[0], transport[1]]) * sea_mask
    fields = jnp.stack([moving[0], moving[1], moving[2], forcing[0], forcing[1], column_depth])
    rim = 2 * SUB
    fields = wide_halo(fields, "gx", 1, rim)
    fields = wide_halo(fields, ("gy", "mode"), 2, rim)
    coriolis_wide = jnp.broadcast_to(
        coriolis_row(anchor - rim, y_cells + 2 * rim, y_cells * column_blocks), (8, y_cells + 2 * rim)
    )
    waves_wide = local_waves(fields[0:3], fields[3:6], coriolis_wide)
    x_cells = depth_class.shape[0]
    waves = waves_wide[:, rim : rim + x_cells, rim : rim + y_cells]
    state_next = finish(updated, waves, active, depth_class, level_block, levels)
    return (state_next, waves[0], waves[1:3])


def solution(mesh):
    placed = (
        P(None, None, "gx", ("gy", "mode")),
        P("gx", ("gy", "mode")),
        P(),
        P("gx", ("gy", "mode")),
        P(None, "gx", ("gy", "mode")),
    )
    return jax.shard_map(
        body,
        mesh=mesh,
        in_specs=placed,
        out_specs=(
            P(None, None, "gx", ("gy", "mode")),
            P("gx", ("gy", "mode")),
            P(None, "gx", ("gy", "mode")),
        ),
        check_vma=False,
    )
```

```python
import jax
import jax.numpy as jnp
from jax import lax
from jax.experimental import pallas as pl
from jax.experimental.pallas import tpu as pltpu
from jax.sharding import PartitionSpec as P

SUB = 32
LEVEL_CHUNK = 8


THERMAL = 0.8
HALINE = 0.6
PRESSURE_SCALE = 4.0
VISCOSITY = 0.1
STEP_TIME = 0.05
WAVE_STEP = 0.5
GRAVITY = 1.0
BOTTOM_DRAG = 0.05
CORIOLIS_BASE = 0.3
CORIOLIS_SLOPE = 0.4


def coriolis_row(anchor, number, total):
    position = (anchor + lax.broadcasted_iota(jnp.int32, (number,), 0)).astype(jnp.float32)
    return (CORIOLIS_BASE + CORIOLIS_SLOPE * (position + 0.5) / total)[None, :]


def vertical_solve(state, provisional, active, depth_class, inverse):
    levels = state.shape[1]
    classes = inverse.shape[0]
    band = levels // classes
    stacked = jnp.concatenate(
        [inverse[class_index, : band * (class_index + 1)] for class_index in range(classes)], axis=0
    )
    every = jnp.einsum("kl,flxy->fkxy", stacked, provisional, precision=lax.Precision.HIGH)
    starts = [band * class_index * (class_index + 1) // 2 for class_index in range(classes)]
    chosen = [(depth_class == class_index + 1).astype(jnp.float32) for class_index in range(classes)]
    bands = []
    for level_band in range(classes):
        part = jnp.zeros_like(provisional[:, :band])
        for class_index in range(level_band, classes):
            first = starts[class_index] + level_band * band
            part = part + chosen[class_index] * every[:, first : first + band]
        bands.append(part)
    solved = jnp.concatenate(bands, axis=1)
    return active * solved + (1.0 - active) * state


def edge_halo(state, active, axis, dim, width):
    count = lax.axis_size(axis)
    ends = count - 1
    size = state.shape[dim]
    head = lax.slice_in_dim(state, 0, width, axis=dim) * lax.slice_in_dim(active, 0, width, axis=dim - 1)
    tail = lax.slice_in_dim(state, size - width, size, axis=dim) * lax.slice_in_dim(
        active, size - width, size, axis=dim - 1
    )
    before = lax.ppermute(tail, axis, [(i, i + 1) for i in range(ends)])
    after = lax.ppermute(head, axis, [(i + 1, i) for i in range(ends)])
    return before, after


def finish(updated, waves, active, depth_class, level_block, levels):
    counted = jnp.maximum(depth_class * level_block, 1).astype(jnp.float32)
    safe_depth = jnp.maximum(depth_class, 1).astype(jnp.float32) * level_block / levels
    column_means = jnp.sum(active * updated[2:4], axis=1) / counted
    carried = waves[1:3] / safe_depth
    velocity = updated[2:4] + active * (carried - column_means)[:, None]
    return jnp.concatenate([updated[0:2], velocity], axis=0)


def wide_halo(cells, axis, dim, width):
    count = lax.axis_size(axis)
    size = cells.shape[dim]
    before, after = [], []
    remaining, hop = width, 1
    while remaining > 0:
        take = min(size, remaining)
        tail = lax.slice_in_dim(cells, size - take, size, axis=dim)
        head = lax.slice_in_dim(cells, 0, take, axis=dim)
        if hop < count:
            from_before = lax.ppermute(tail, axis, [(i, i + hop) for i in range(count - hop)])
            from_after = lax.ppermute(head, axis, [(i + hop, i) for i in range(count - hop)])
        else:
            from_before = jnp.zeros_like(tail)
            from_after = jnp.zeros_like(head)
        before.insert(0, from_before)
        after.append(from_after)
        remaining -= take
        hop += 1
    return jnp.concatenate(before + [cells] + after, axis=dim)


def stencil_kernel(depth_ref, coriolis_ref, state_ref, west_ref, east_ref, side_ref,
                   provisional_ref, forcing_ref, sums_ref):
    chunk = pl.program_id(0)
    fields, depth_levels, rows, cols = state_ref.shape
    levels = depth_levels * pl.num_programs(0)
    block = levels // 4

    @pl.when(chunk == 0)
    def _():
        sums_ref[...] = jnp.zeros_like(sums_ref)

    row = lax.broadcasted_iota(jnp.int32, (rows, cols), 0)
    lane = lax.broadcasted_iota(jnp.int32, (rows, cols), 1)
    reach = depth_ref[...] * block
    coriolis = coriolis_ref[0:1, :]

    def near(values, west, east, side):
        w0 = jnp.broadcast_to(west[0:1], (rows, cols))
        w1 = jnp.broadcast_to(west[1:2], (rows, cols))
        e0 = jnp.broadcast_to(east[0:1], (rows, cols))
        e1 = jnp.broadcast_to(east[1:2], (rows, cols))
        xm1 = jnp.where(row == 0, w1, pltpu.roll(values, 1, 0))
        xm2 = jnp.where(row == 0, w0, jnp.where(row == 1, w1, pltpu.roll(values, 2, 0)))
        xp1 = jnp.where(row == rows - 1, e0, pltpu.roll(values, rows - 1, 0))
        xp2 = jnp.where(row == rows - 2, e0, jnp.where(row == rows - 1, e1, pltpu.roll(values, rows - 2, 0)))
        ym1 = jnp.where(lane == 0, pltpu.roll(side, cols - 1, 1), pltpu.roll(values, 1, 1))
        ym2 = jnp.where(lane < 2, side, pltpu.roll(values, 2, 1))
        yp1 = jnp.where(lane == cols - 1, pltpu.roll(side, 1, 1), pltpu.roll(values, cols - 1, 1))
        yp2 = jnp.where(lane >= cols - 2, side, pltpu.roll(values, cols - 2, 1))
        return xm2, xm1, xp1, xp2, ym2, ym1, yp1, yp2

    def fourth(m2, m1, p1, p2):
        return (8.0 * (p1 - m1) - (p2 - m2)) / 12.0

    def level(k, carry):
        global_level = chunk * depth_levels + k
        active = (global_level < reach).astype(jnp.float32)
        masked = [state_ref[f, k] * active for f in range(fields)]
        west = [west_ref[f, k] for f in range(fields)]
        east = [east_ref[f, k] for f in range(fields)]
        side = [side_ref[f, k] for f in range(fields)]
        density = -THERMAL * masked[0] + HALINE * masked[1]
        density_w = -THERMAL * west[0] + HALINE * west[1]
        density_e = -THERMAL * east[0] + HALINE * east[1]
        density_s = -THERMAL * side[0] + HALINE * side[1]
        sums_ref[0] = sums_ref[0] + density
        sums_ref[1] = sums_ref[1] + density_s
        sums_ref[2, 0:2] = sums_ref[2, 0:2] + density_w
        sums_ref[2, 2:4] = sums_ref[2, 2:4] + density_e
        scale = PRESSURE_SCALE / levels
        pressure = scale * sums_ref[0]
        pressure_s = scale * sums_ref[1]
        pressure_w = scale * sums_ref[2, 0:2]
        pressure_e = scale * sums_ref[2, 2:4]
        east_vel = masked[2]
        north_vel = masked[3]
        pm2, pm1, pp1, pp2, qm2, qm1, qp1, qp2 = near(pressure, pressure_w, pressure_e, pressure_s)
        extra = [None, None,
                 -fourth(pm2, pm1, pp1, pp2) + coriolis * north_vel,
                 -fourth(qm2, qm1, qp1, qp2) - coriolis * east_vel]
        for f in range(fields):
            xm2, xm1, xp1, xp2, ym2, ym1, yp1, yp2 = near(masked[f], west[f], east[f], side[f])
            lap = xp1 + xm1 + yp1 + ym1 - 4.0 * masked[f]
            tendency = -(east_vel * fourth(xm2, xm1, xp1, xp2) + north_vel * fourth(ym2, ym1, yp1, yp2)) + VISCOSITY * lap
            if extra[f] is not None:
                tendency = tendency + extra[f]
                forcing_ref[f - 2] = forcing_ref[f - 2] + active * tendency
            provisional_ref[f, k] = active * (masked[f] + STEP_TIME * tendency)
        return carry

    @pl.when(chunk == 0)
    def _():
        forcing_ref[...] = jnp.zeros_like(forcing_ref)

    lax.fori_loop(0, depth_levels, level, 0)

    @pl.when(chunk == pl.num_programs(0) - 1)
    def _():
        forcing_ref[...] = forcing_ref[...] / levels


def stencil(state, depth_class, west, east, side, coriolis):
    fields, levels, rows, cols = state.shape
    steps = levels // LEVEL_CHUNK
    big = pl.BlockSpec((fields, LEVEL_CHUNK, rows, cols), lambda c: (0, c, 0, 0))
    rim = pl.BlockSpec((fields, LEVEL_CHUNK, 2, cols), lambda c: (0, c, 0, 0))
    flat = pl.BlockSpec((rows, cols), lambda c: (0, 0))
    return pl.pallas_call(
        stencil_kernel,
        grid=(steps,),
        out_shape=(jax.ShapeDtypeStruct(state.shape, jnp.float32),
                   jax.ShapeDtypeStruct((2, rows, cols), jnp.float32)),
        in_specs=[flat, pl.BlockSpec((8, cols), lambda c: (0, 0)), big, rim, rim, big],
        out_specs=(big, pl.BlockSpec((2, rows, cols), lambda c: (0, 0, 0))),
        scratch_shapes=[pltpu.VMEM((3, rows, cols), jnp.float32)],
        compiler_params=pltpu.CompilerParams(dimension_semantics=("arbitrary",)),
        cost_estimate=pl.CostEstimate(
            flops=60 * state.size, transcendentals=0, bytes_accessed=4 * 3 * state.size
        ),
    )(depth_class, coriolis, state, west, east, side)


def wave_kernel(moving_ref, fixed_ref, coriolis_ref, out_ref):
    rows, cols = moving_ref.shape[1], moving_ref.shape[2]
    column_depth = fixed_ref[2]
    sea_mask = (column_depth > 0.0).astype(jnp.float32)
    force_east = fixed_ref[0]
    force_north = fixed_ref[1]
    coriolis = jnp.broadcast_to(coriolis_ref[0:1, :], (rows, cols))

    def x_slope_rolled(values):
        return (pltpu.roll(values, rows - 1, 0) - pltpu.roll(values, 1, 0)) * 0.5

    def y_slope_rolled(values):
        return (pltpu.roll(values, cols - 1, 1) - pltpu.roll(values, 1, 1)) * 0.5

    out_ref[...] = moving_ref[...]

    def step(index, carry):
        surface = out_ref[0]
        east_old = out_ref[1]
        north_old = out_ref[2]
        surface_mid = sea_mask * (
            surface - WAVE_STEP * (x_slope_rolled(east_old) + y_slope_rolled(north_old))
        )
        east_new = sea_mask * (
            east_old
            + WAVE_STEP
            * (
                -GRAVITY * column_depth * x_slope_rolled(surface_mid)
                + coriolis * north_old
                + force_east
                - BOTTOM_DRAG * east_old
            )
        )
        north_new = sea_mask * (
            north_old
            + WAVE_STEP
            * (
                -GRAVITY * column_depth * y_slope_rolled(surface_mid)
                - coriolis * east_new
                + force_north
                - BOTTOM_DRAG * north_old
            )
        )
        out_ref[0] = surface_mid
        out_ref[1] = east_new
        out_ref[2] = north_new
        return carry

    lax.fori_loop(0, SUB, step, 0)


def local_waves(moving, fixed, coriolis):
    rows, cols = moving.shape[1], moving.shape[2]
    elements = rows * cols
    return pl.pallas_call(
        wave_kernel,
        out_shape=jax.ShapeDtypeStruct(moving.shape, jnp.float32),
        in_specs=[pl.BlockSpec(memory_space=pltpu.VMEM)] * 3,
        out_specs=pl.BlockSpec(memory_space=pltpu.VMEM),
        cost_estimate=pl.CostEstimate(
            flops=SUB * 40 * elements, transcendentals=0, bytes_accessed=4 * 9 * elements
        ),
    )(moving, fixed, coriolis)


def body(state, depth_class, vertical_inverse, height, transport):
    levels = state.shape[1]
    level_block = levels // vertical_inverse.shape[0]
    y_cells = depth_class.shape[1]
    level_ids = lax.broadcasted_iota(jnp.int32, (levels, 1, 1), 0)
    active = (level_ids < depth_class[None] * level_block).astype(jnp.float32)
    west, east = edge_halo(state, active, "gx", 2, 2)
    south, north = edge_halo(state, active, ("gy", "mode"), 3, 2)
    column_blocks = lax.axis_size(("gy", "mode"))
    anchor = lax.axis_index(("gy", "mode")) * y_cells
    coriolis = jnp.broadcast_to(coriolis_row(anchor, y_cells, y_cells * column_blocks), (8, y_cells))
    gap = jnp.zeros(south.shape[:3] + (y_cells - 4,), jnp.float32)
    side = jnp.concatenate([south, gap, north], axis=3)
    provisional, forcing = stencil(state, depth_class, west, east, side, coriolis)
    updated = vertical_solve(state, provisional, active, depth_class, vertical_inverse)
    column_depth = depth_class.astype(jnp.float32) * level_block / levels
    sea_mask = (depth_class > 0).astype(jnp.float32)
    moving = jnp.stack([height, transport[0], transport[1]]) * sea_mask
    fields = jnp.stack([moving[0], moving[1], moving[2], forcing[0], forcing[1], column_depth])
    rim = 2 * SUB
    fields = wide_halo(fields, "gx", 1, rim)
    fields = wide_halo(fields, ("gy", "mode"), 2, rim)
    coriolis_wide = jnp.broadcast_to(
        coriolis_row(anchor - rim, y_cells + 2 * rim, y_cells * column_blocks), (8, y_cells + 2 * rim)
    )
    waves_wide = local_waves(fields[0:3], fields[3:6], coriolis_wide)
    x_cells = depth_class.shape[0]
    waves = waves_wide[:, rim : rim + x_cells, rim : rim + y_cells]
    state_next = finish(updated, waves, active, depth_class, level_block, levels)
    return (state_next, waves[0], waves[1:3])


def solution(mesh):
    placed = (
        P(None, None, "gx", ("gy", "mode")),
        P("gx", ("gy", "mode")),
        P(),
        P("gx", ("gy", "mode")),
        P(None, "gx", ("gy", "mode")),
    )
    return jax.shard_map(
        body,
        mesh=mesh,
        in_specs=placed,
        out_specs=(
            P(None, None, "gx", ("gy", "mode")),
            P("gx", ("gy", "mode")),
            P(None, "gx", ("gy", "mode")),
        ),
        check_vma=False,
    )
```

```python
import jax
import jax.numpy as jnp
from jax import lax
from jax.experimental import pallas as pl
from jax.experimental.pallas import tpu as pltpu
from jax.sharding import PartitionSpec as P

SUB = 32
LEVEL_CHUNK = 8
PACK = 32


THERMAL = 0.8
HALINE = 0.6
PRESSURE_SCALE = 4.0
VISCOSITY = 0.1
STEP_TIME = 0.05
WAVE_STEP = 0.5
GRAVITY = 1.0
BOTTOM_DRAG = 0.05
CORIOLIS_BASE = 0.3
CORIOLIS_SLOPE = 0.4


def coriolis_row(anchor, number, total):
    position = (anchor + lax.broadcasted_iota(jnp.int32, (number,), 0)).astype(jnp.float32)
    return (CORIOLIS_BASE + CORIOLIS_SLOPE * (position + 0.5) / total)[None, :]


def vertical_solve(state, provisional, active, depth_class, inverse):
    levels = state.shape[1]
    classes = inverse.shape[0]
    band = levels // classes
    stacked = jnp.concatenate(
        [inverse[class_index, : band * (class_index + 1)] for class_index in range(classes)], axis=0
    )
    every = jnp.einsum("kl,flxy->fkxy", stacked, provisional, precision=lax.Precision.HIGH)
    starts = [band * class_index * (class_index + 1) // 2 for class_index in range(classes)]
    chosen = [(depth_class == class_index + 1).astype(jnp.float32) for class_index in range(classes)]
    bands = []
    for level_band in range(classes):
        part = jnp.zeros_like(provisional[:, :band])
        for class_index in range(level_band, classes):
            first = starts[class_index] + level_band * band
            part = part + chosen[class_index] * every[:, first : first + band]
        bands.append(part)
    solved = jnp.concatenate(bands, axis=1)
    return active * solved + (1.0 - active) * state


def edge_halo(state, active, axis, dim, width):
    count = lax.axis_size(axis)
    ends = count - 1
    size = state.shape[dim]
    head = lax.slice_in_dim(state, 0, width, axis=dim) * lax.slice_in_dim(active, 0, width, axis=dim - 1)
    tail = lax.slice_in_dim(state, size - width, size, axis=dim) * lax.slice_in_dim(
        active, size - width, size, axis=dim - 1
    )
    before = lax.ppermute(tail, axis, [(i, i + 1) for i in range(ends)])
    after = lax.ppermute(head, axis, [(i + 1, i) for i in range(ends)])
    return before, after


def finish(updated, waves, active, depth_class, level_block, levels):
    counted = jnp.maximum(depth_class * level_block, 1).astype(jnp.float32)
    safe_depth = jnp.maximum(depth_class, 1).astype(jnp.float32) * level_block / levels
    column_means = jnp.sum(active * updated[2:4], axis=1) / counted
    carried = waves[1:3] / safe_depth
    velocity = updated[2:4] + active * (carried - column_means)[:, None]
    return jnp.concatenate([updated[0:2], velocity], axis=0)


def wide_halo(cells, axis, dim, width):
    count = lax.axis_size(axis)
    size = cells.shape[dim]
    before, after = [], []
    remaining, hop = width, 1
    while remaining > 0:
        take = min(size, remaining)
        tail = lax.slice_in_dim(cells, size - take, size, axis=dim)
        head = lax.slice_in_dim(cells, 0, take, axis=dim)
        if hop < count:
            from_before = lax.ppermute(tail, axis, [(i, i + hop) for i in range(count - hop)])
            from_after = lax.ppermute(head, axis, [(i + hop, i) for i in range(count - hop)])
        else:
            from_before = jnp.zeros_like(tail)
            from_after = jnp.zeros_like(head)
        before.insert(0, from_before)
        after.append(from_after)
        remaining -= take
        hop += 1
    return jnp.concatenate(before + [cells] + after, axis=dim)


def stencil_kernel(depth_ref, coriolis_ref, state_ref, west_ref, east_ref, side_ref,
                   provisional_ref, forcing_ref, sums_ref):
    chunk = pl.program_id(0)
    fields, depth_levels, rows, cols = state_ref.shape
    levels = depth_levels * pl.num_programs(0)
    block = levels // 4

    @pl.when(chunk == 0)
    def _():
        sums_ref[...] = jnp.zeros_like(sums_ref)

    row = lax.broadcasted_iota(jnp.int32, (rows, cols), 0)
    lane = lax.broadcasted_iota(jnp.int32, (rows, cols), 1)
    reach = depth_ref[...] * block
    coriolis = coriolis_ref[0:1, :]

    def near(values, west, east, side):
        w0 = jnp.broadcast_to(west[0:1], (rows, cols))
        w1 = jnp.broadcast_to(west[1:2], (rows, cols))
        e0 = jnp.broadcast_to(east[0:1], (rows, cols))
        e1 = jnp.broadcast_to(east[1:2], (rows, cols))
        xm1 = jnp.where(row == 0, w1, pltpu.roll(values, 1, 0))
        xm2 = jnp.where(row == 0, w0, jnp.where(row == 1, w1, pltpu.roll(values, 2, 0)))
        xp1 = jnp.where(row == rows - 1, e0, pltpu.roll(values, rows - 1, 0))
        xp2 = jnp.where(row == rows - 2, e0, jnp.where(row == rows - 1, e1, pltpu.roll(values, rows - 2, 0)))
        ym1 = jnp.where(lane == 0, pltpu.roll(side, cols - 1, 1), pltpu.roll(values, 1, 1))
        ym2 = jnp.where(lane < 2, side, pltpu.roll(values, 2, 1))
        yp1 = jnp.where(lane == cols - 1, pltpu.roll(side, 1, 1), pltpu.roll(values, cols - 1, 1))
        yp2 = jnp.where(lane >= cols - 2, side, pltpu.roll(values, cols - 2, 1))
        return xm2, xm1, xp1, xp2, ym2, ym1, yp1, yp2

    def fourth(m2, m1, p1, p2):
        return (8.0 * (p1 - m1) - (p2 - m2)) / 12.0

    def level(k, carry):
        global_level = chunk * depth_levels + k
        active = (global_level < reach).astype(jnp.float32)
        masked = [state_ref[f, k] * active for f in range(fields)]
        west = [west_ref[f, k] for f in range(fields)]
        east = [east_ref[f, k] for f in range(fields)]
        packed_level = global_level % PACK
        shift = (cols - 2 - 4 * packed_level) % cols
        side = [pltpu.roll(side_ref[f, global_level // PACK], shift, 1) for f in range(fields)]
        density = -THERMAL * masked[0] + HALINE * masked[1]
        density_w = -THERMAL * west[0] + HALINE * west[1]
        density_e = -THERMAL * east[0] + HALINE * east[1]
        density_s = -THERMAL * side[0] + HALINE * side[1]
        sums_ref[0] = sums_ref[0] + density
        sums_ref[1] = sums_ref[1] + density_s
        sums_ref[2, 0:2] = sums_ref[2, 0:2] + density_w
        sums_ref[2, 2:4] = sums_ref[2, 2:4] + density_e
        scale = PRESSURE_SCALE / levels
        pressure = scale * sums_ref[0]
        pressure_s = scale * sums_ref[1]
        pressure_w = scale * sums_ref[2, 0:2]
        pressure_e = scale * sums_ref[2, 2:4]
        east_vel = masked[2]
        north_vel = masked[3]
        pm2, pm1, pp1, pp2, qm2, qm1, qp1, qp2 = near(pressure, pressure_w, pressure_e, pressure_s)
        extra = [None, None,
                 -fourth(pm2, pm1, pp1, pp2) + coriolis * north_vel,
                 -fourth(qm2, qm1, qp1, qp2) - coriolis * east_vel]
        for f in range(fields):
            xm2, xm1, xp1, xp2, ym2, ym1, yp1, yp2 = near(masked[f], west[f], east[f], side[f])
            lap = xp1 + xm1 + yp1 + ym1 - 4.0 * masked[f]
            tendency = -(east_vel * fourth(xm2, xm1, xp1, xp2) + north_vel * fourth(ym2, ym1, yp1, yp2)) + VISCOSITY * lap
            if extra[f] is not None:
                tendency = tendency + extra[f]
                forcing_ref[f - 2] = forcing_ref[f - 2] + active * tendency
            provisional_ref[f, k] = active * (masked[f] + STEP_TIME * tendency)
        return carry

    @pl.when(chunk == 0)
    def _():
        forcing_ref[...] = jnp.zeros_like(forcing_ref)

    lax.fori_loop(0, depth_levels, level, 0)

    @pl.when(chunk == pl.num_programs(0) - 1)
    def _():
        forcing_ref[...] = forcing_ref[...] / levels


def stencil(state, depth_class, west, east, side, coriolis):
    fields, levels, rows, cols = state.shape
    steps = levels // LEVEL_CHUNK
    big = pl.BlockSpec((fields, LEVEL_CHUNK, rows, cols), lambda c: (0, c, 0, 0))
    rim = pl.BlockSpec((fields, LEVEL_CHUNK, 2, cols), lambda c: (0, c, 0, 0))
    flat = pl.BlockSpec((rows, cols), lambda c: (0, 0))
    packed = pl.BlockSpec(side.shape, lambda c: (0, 0, 0, 0))
    return pl.pallas_call(
        stencil_kernel,
        grid=(steps,),
        out_shape=(jax.ShapeDtypeStruct(state.shape, jnp.float32),
                   jax.ShapeDtypeStruct((2, rows, cols), jnp.float32)),
        in_specs=[flat, pl.BlockSpec((8, cols), lambda c: (0, 0)), big, rim, rim, packed],
        out_specs=(big, pl.BlockSpec((2, rows, cols), lambda c: (0, 0, 0))),
        scratch_shapes=[pltpu.VMEM((3, rows, cols), jnp.float32)],
        compiler_params=pltpu.CompilerParams(dimension_semantics=("arbitrary",)),
        cost_estimate=pl.CostEstimate(
            flops=60 * state.size, transcendentals=0, bytes_accessed=4 * 2 * state.size
        ),
    )(depth_class, coriolis, state, west, east, side)


def pack_kernel(depth_ref, state_ref, out_ref):
    block_index = pl.program_id(0)
    fields, depth_levels, rows, cols = state_ref.shape
    block = depth_levels * pl.num_programs(0) // 4
    lane = lax.broadcasted_iota(jnp.int32, (rows, cols), 1)
    reach = depth_ref[...] * block
    packed = [jnp.zeros((rows, cols), jnp.float32) for f in range(fields)]
    for k in range(depth_levels):
        active = (block_index * depth_levels + k < reach).astype(jnp.float32)
        low = 4 * k
        first = (lane == low) | (lane == low + 1)
        second = (lane == low + 2) | (lane == low + 3)
        for f in range(fields):
            masked = state_ref[f, k] * active
            near_end = pltpu.roll(masked, low, 1)
            far_end = pltpu.roll(masked, (low + 4) % cols, 1)
            packed[f] = jnp.where(first, near_end, jnp.where(second, far_end, packed[f]))
    for f in range(fields):
        out_ref[f, 0] = packed[f]


def pack_edges(state, depth_class):
    fields, levels, rows, cols = state.shape
    return pl.pallas_call(
        pack_kernel,
        grid=(levels // PACK,),
        out_shape=jax.ShapeDtypeStruct((fields, levels // PACK, rows, cols), jnp.float32),
        in_specs=[pl.BlockSpec((rows, cols), lambda c: (0, 0)),
                  pl.BlockSpec((fields, PACK, rows, cols), lambda c: (0, c, 0, 0))],
        out_specs=pl.BlockSpec((fields, 1, rows, cols), lambda c: (0, c, 0, 0)),
        cost_estimate=pl.CostEstimate(
            flops=4 * state.size, transcendentals=0, bytes_accessed=4 * state.size
        ),
    )(depth_class, state)


def combine(from_south, from_north):
    lane = lax.broadcasted_iota(jnp.int32, from_south.shape, from_south.ndim - 1)
    return jnp.where(lane % 4 >= 2, from_south, from_north)


def wave_kernel(moving_ref, fixed_ref, coriolis_ref, out_ref):
    rows, cols = moving_ref.shape[1], moving_ref.shape[2]
    column_depth = fixed_ref[2]
    sea_mask = (column_depth > 0.0).astype(jnp.float32)
    force_east = fixed_ref[0]
    force_north = fixed_ref[1]
    coriolis = jnp.broadcast_to(coriolis_ref[0:1, :], (rows, cols))

    def x_slope_rolled(values):
        return (pltpu.roll(values, rows - 1, 0) - pltpu.roll(values, 1, 0)) * 0.5

    def y_slope_rolled(values):
        return (pltpu.roll(values, cols - 1, 1) - pltpu.roll(values, 1, 1)) * 0.5

    out_ref[...] = moving_ref[...]

    def step(index, carry):
        surface = out_ref[0]
        east_old = out_ref[1]
        north_old = out_ref[2]
        surface_mid = sea_mask * (
            surface - WAVE_STEP * (x_slope_rolled(east_old) + y_slope_rolled(north_old))
        )
        east_new = sea_mask * (
            east_old
            + WAVE_STEP
            * (
                -GRAVITY * column_depth * x_slope_rolled(surface_mid)
                + coriolis * north_old
                + force_east
                - BOTTOM_DRAG * east_old
            )
        )
        north_new = sea_mask * (
            north_old
            + WAVE_STEP
            * (
                -GRAVITY * column_depth * y_slope_rolled(surface_mid)
                - coriolis * east_new
                + force_north
                - BOTTOM_DRAG * north_old
            )
        )
        out_ref[0] = surface_mid
        out_ref[1] = east_new
        out_ref[2] = north_new
        return carry

    lax.fori_loop(0, SUB, step, 0)


def local_waves(moving, fixed, coriolis):
    rows, cols = moving.shape[1], moving.shape[2]
    elements = rows * cols
    return pl.pallas_call(
        wave_kernel,
        out_shape=jax.ShapeDtypeStruct(moving.shape, jnp.float32),
        in_specs=[pl.BlockSpec(memory_space=pltpu.VMEM)] * 3,
        out_specs=pl.BlockSpec(memory_space=pltpu.VMEM),
        cost_estimate=pl.CostEstimate(
            flops=SUB * 40 * elements, transcendentals=0, bytes_accessed=4 * 9 * elements
        ),
    )(moving, fixed, coriolis)


def body(state, depth_class, vertical_inverse, height, transport):
    levels = state.shape[1]
    level_block = levels // vertical_inverse.shape[0]
    y_cells = depth_class.shape[1]
    level_ids = lax.broadcasted_iota(jnp.int32, (levels, 1, 1), 0)
    active = (level_ids < depth_class[None] * level_block).astype(jnp.float32)
    west, east = edge_halo(state, active, "gx", 2, 2)
    column_blocks = lax.axis_size(("gy", "mode"))
    anchor = lax.axis_index(("gy", "mode")) * y_cells
    coriolis = jnp.broadcast_to(coriolis_row(anchor, y_cells, y_cells * column_blocks), (8, y_cells))
    edges = pack_edges(state, depth_class)
    y_count = lax.axis_size(("gy", "mode"))
    from_south = lax.ppermute(edges, ("gy", "mode"), [(i, i + 1) for i in range(y_count - 1)])
    from_north = lax.ppermute(edges, ("gy", "mode"), [(i + 1, i) for i in range(y_count - 1)])
    side = combine(from_south, from_north)
    provisional, forcing = stencil(state, depth_class, west, east, side, coriolis)
    updated = vertical_solve(state, provisional, active, depth_class, vertical_inverse)
    column_depth = depth_class.astype(jnp.float32) * level_block / levels
    sea_mask = (depth_class > 0).astype(jnp.float32)
    moving = jnp.stack([height, transport[0], transport[1]]) * sea_mask
    fields = jnp.stack([moving[0], moving[1], moving[2], forcing[0], forcing[1], column_depth])
    rim = 2 * SUB
    fields = wide_halo(fields, "gx", 1, rim)
    fields = wide_halo(fields, ("gy", "mode"), 2, rim)
    coriolis_wide = jnp.broadcast_to(
        coriolis_row(anchor - rim, y_cells + 2 * rim, y_cells * column_blocks), (8, y_cells + 2 * rim)
    )
    waves_wide = local_waves(fields[0:3], fields[3:6], coriolis_wide)
    x_cells = depth_class.shape[0]
    waves = waves_wide[:, rim : rim + x_cells, rim : rim + y_cells]
    state_next = finish(updated, waves, active, depth_class, level_block, levels)
    return (state_next, waves[0], waves[1:3])


def solution(mesh):
    placed = (
        P(None, None, "gx", ("gy", "mode")),
        P("gx", ("gy", "mode")),
        P(),
        P("gx", ("gy", "mode")),
        P(None, "gx", ("gy", "mode")),
    )
    return jax.shard_map(
        body,
        mesh=mesh,
        in_specs=placed,
        out_specs=(
            P(None, None, "gx", ("gy", "mode")),
            P("gx", ("gy", "mode")),
            P(None, "gx", ("gy", "mode")),
        ),
        check_vma=False,
    )
```

```python
import jax
import jax.numpy as jnp
from jax import lax
from jax.experimental import pallas as pl
from jax.experimental.pallas import tpu as pltpu
from jax.sharding import PartitionSpec as P

SUB = 32
LEVEL_CHUNK = 8
PACK = 32


THERMAL = 0.8
HALINE = 0.6
PRESSURE_SCALE = 4.0
VISCOSITY = 0.1
STEP_TIME = 0.05
WAVE_STEP = 0.5
GRAVITY = 1.0
BOTTOM_DRAG = 0.05
CORIOLIS_BASE = 0.3
CORIOLIS_SLOPE = 0.4


def coriolis_row(anchor, number, total):
    position = (anchor + lax.broadcasted_iota(jnp.int32, (number,), 0)).astype(jnp.float32)
    return (CORIOLIS_BASE + CORIOLIS_SLOPE * (position + 0.5) / total)[None, :]


def vertical_solve(state, provisional, active, depth_class, inverse):
    levels = state.shape[1]
    classes = inverse.shape[0]
    band = levels // classes
    stacked = jnp.concatenate(
        [inverse[class_index, : band * (class_index + 1)] for class_index in range(classes)], axis=0
    )
    every = jnp.einsum("kl,flxy->fkxy", stacked, provisional, precision=lax.Precision.HIGH)
    starts = [band * class_index * (class_index + 1) // 2 for class_index in range(classes)]
    chosen = [(depth_class == class_index + 1).astype(jnp.float32) for class_index in range(classes)]
    bands = []
    for level_band in range(classes):
        part = jnp.zeros_like(provisional[:, :band])
        for class_index in range(level_band, classes):
            first = starts[class_index] + level_band * band
            part = part + chosen[class_index] * every[:, first : first + band]
        bands.append(part)
    solved = jnp.concatenate(bands, axis=1)
    return active * solved + (1.0 - active) * state


def edge_halo(state, active, axis, dim, width):
    count = lax.axis_size(axis)
    ends = count - 1
    size = state.shape[dim]
    head = lax.slice_in_dim(state, 0, width, axis=dim) * lax.slice_in_dim(active, 0, width, axis=dim - 1)
    tail = lax.slice_in_dim(state, size - width, size, axis=dim) * lax.slice_in_dim(
        active, size - width, size, axis=dim - 1
    )
    before = lax.ppermute(tail, axis, [(i, i + 1) for i in range(ends)])
    after = lax.ppermute(head, axis, [(i + 1, i) for i in range(ends)])
    return before, after


def finish(updated, waves, active, depth_class, level_block, levels):
    counted = jnp.maximum(depth_class * level_block, 1).astype(jnp.float32)
    safe_depth = jnp.maximum(depth_class, 1).astype(jnp.float32) * level_block / levels
    column_means = jnp.sum(active * updated[2:4], axis=1) / counted
    carried = waves[1:3] / safe_depth
    velocity = updated[2:4] + active * (carried - column_means)[:, None]
    return jnp.concatenate([updated[0:2], velocity], axis=0)


def wide_halo(cells, axis, dim, width):
    count = lax.axis_size(axis)
    size = cells.shape[dim]
    before, after = [], []
    remaining, hop = width, 1
    while remaining > 0:
        take = min(size, remaining)
        tail = lax.slice_in_dim(cells, size - take, size, axis=dim)
        head = lax.slice_in_dim(cells, 0, take, axis=dim)
        if hop < count:
            from_before = lax.ppermute(tail, axis, [(i, i + hop) for i in range(count - hop)])
            from_after = lax.ppermute(head, axis, [(i + hop, i) for i in range(count - hop)])
        else:
            from_before = jnp.zeros_like(tail)
            from_after = jnp.zeros_like(head)
        before.insert(0, from_before)
        after.append(from_after)
        remaining -= take
        hop += 1
    return jnp.concatenate(before + [cells] + after, axis=dim)


def stencil_kernel(depth_ref, coriolis_ref, state_ref, west_ref, east_ref, side_ref,
                   provisional_ref, forcing_ref, sums_ref):
    chunk = pl.program_id(0)
    fields, depth_levels, rows, cols = state_ref.shape
    levels = depth_levels * pl.num_programs(0)
    block = levels // 4

    @pl.when(chunk == 0)
    def _():
        sums_ref[...] = jnp.zeros_like(sums_ref)

    row = lax.broadcasted_iota(jnp.int32, (rows, cols), 0)
    lane = lax.broadcasted_iota(jnp.int32, (rows, cols), 1)
    reach = depth_ref[...] * block
    coriolis = coriolis_ref[0:1, :]

    def near(values, west, east, side):
        w0 = jnp.broadcast_to(west[0:1], (rows, cols))
        w1 = jnp.broadcast_to(west[1:2], (rows, cols))
        e0 = jnp.broadcast_to(east[0:1], (rows, cols))
        e1 = jnp.broadcast_to(east[1:2], (rows, cols))
        xm1 = jnp.where(row == 0, w1, pltpu.roll(values, 1, 0))
        xm2 = jnp.where(row == 0, w0, jnp.where(row == 1, w1, pltpu.roll(values, 2, 0)))
        xp1 = jnp.where(row == rows - 1, e0, pltpu.roll(values, rows - 1, 0))
        xp2 = jnp.where(row == rows - 2, e0, jnp.where(row == rows - 1, e1, pltpu.roll(values, rows - 2, 0)))
        ym1 = jnp.where(lane == 0, pltpu.roll(side, cols - 1, 1), pltpu.roll(values, 1, 1))
        ym2 = jnp.where(lane < 2, side, pltpu.roll(values, 2, 1))
        yp1 = jnp.where(lane == cols - 1, pltpu.roll(side, 1, 1), pltpu.roll(values, cols - 1, 1))
        yp2 = jnp.where(lane >= cols - 2, side, pltpu.roll(values, cols - 2, 1))
        return xm2, xm1, xp1, xp2, ym2, ym1, yp1, yp2

    def fourth(m2, m1, p1, p2):
        return (8.0 * (p1 - m1) - (p2 - m2)) * (1.0 / 12.0)

    def level(k, carry):
        global_level = chunk * depth_levels + k
        active = (global_level < reach).astype(jnp.float32)
        masked = [state_ref[f, k] * active for f in range(fields)]
        west = [west_ref[f, k] for f in range(fields)]
        east = [east_ref[f, k] for f in range(fields)]
        packed_level = global_level % PACK
        shift = (cols - 2 - 4 * packed_level) % cols
        side = [pltpu.roll(side_ref[f, global_level // PACK], shift, 1) for f in range(fields)]
        density = -THERMAL * masked[0] + HALINE * masked[1]
        density_w = -THERMAL * west[0] + HALINE * west[1]
        density_e = -THERMAL * east[0] + HALINE * east[1]
        density_s = -THERMAL * side[0] + HALINE * side[1]
        sums_ref[0] = sums_ref[0] + density
        sums_ref[1] = sums_ref[1] + density_s
        sums_ref[2, 0:2] = sums_ref[2, 0:2] + density_w
        sums_ref[2, 2:4] = sums_ref[2, 2:4] + density_e
        scale = PRESSURE_SCALE / levels
        pressure = scale * sums_ref[0]
        pressure_s = scale * sums_ref[1]
        pressure_w = scale * sums_ref[2, 0:2]
        pressure_e = scale * sums_ref[2, 2:4]
        east_vel = masked[2]
        north_vel = masked[3]
        pm2, pm1, pp1, pp2, qm2, qm1, qp1, qp2 = near(pressure, pressure_w, pressure_e, pressure_s)
        extra = [None, None,
                 -fourth(pm2, pm1, pp1, pp2) + coriolis * north_vel,
                 -fourth(qm2, qm1, qp1, qp2) - coriolis * east_vel]
        for f in range(fields):
            xm2, xm1, xp1, xp2, ym2, ym1, yp1, yp2 = near(masked[f], west[f], east[f], side[f])
            lap = xp1 + xm1 + yp1 + ym1 - 4.0 * masked[f]
            tendency = -(east_vel * fourth(xm2, xm1, xp1, xp2) + north_vel * fourth(ym2, ym1, yp1, yp2)) + VISCOSITY * lap
            if extra[f] is not None:
                tendency = tendency + extra[f]
                forcing_ref[f - 2] = forcing_ref[f - 2] + active * tendency
            provisional_ref[f, k] = active * (masked[f] + STEP_TIME * tendency)
        return carry

    @pl.when(chunk == 0)
    def _():
        forcing_ref[...] = jnp.zeros_like(forcing_ref)

    lax.fori_loop(0, depth_levels, level, 0)

    @pl.when(chunk == pl.num_programs(0) - 1)
    def _():
        forcing_ref[...] = forcing_ref[...] / levels


def stencil(state, depth_class, west, east, side, coriolis):
    fields, levels, rows, cols = state.shape
    steps = levels // LEVEL_CHUNK
    big = pl.BlockSpec((fields, LEVEL_CHUNK, rows, cols), lambda c: (0, c, 0, 0))
    rim = pl.BlockSpec((fields, LEVEL_CHUNK, 2, cols), lambda c: (0, c, 0, 0))
    flat = pl.BlockSpec((rows, cols), lambda c: (0, 0))
    packed = pl.BlockSpec(side.shape, lambda c: (0, 0, 0, 0))
    return pl.pallas_call(
        stencil_kernel,
        grid=(steps,),
        out_shape=(jax.ShapeDtypeStruct(state.shape, jnp.float32),
                   jax.ShapeDtypeStruct((2, rows, cols), jnp.float32)),
        in_specs=[flat, pl.BlockSpec((8, cols), lambda c: (0, 0)), big, rim, rim, packed],
        out_specs=(big, pl.BlockSpec((2, rows, cols), lambda c: (0, 0, 0))),
        scratch_shapes=[pltpu.VMEM((3, rows, cols), jnp.float32)],
        compiler_params=pltpu.CompilerParams(dimension_semantics=("arbitrary",)),
        cost_estimate=pl.CostEstimate(
            flops=60 * state.size, transcendentals=0, bytes_accessed=4 * 2 * state.size
        ),
    )(depth_class, coriolis, state, west, east, side)


def pack_kernel(depth_ref, state_ref, out_ref):
    block_index = pl.program_id(0)
    fields, depth_levels, rows, cols = state_ref.shape
    block = depth_levels * pl.num_programs(0) // 4
    lane = lax.broadcasted_iota(jnp.int32, (rows, cols), 1)
    reach = depth_ref[...] * block
    packed = [jnp.zeros((rows, cols), jnp.float32) for f in range(fields)]
    for k in range(depth_levels):
        active = (block_index * depth_levels + k < reach).astype(jnp.float32)
        low = 4 * k
        first = (lane == low) | (lane == low + 1)
        second = (lane == low + 2) | (lane == low + 3)
        for f in range(fields):
            masked = state_ref[f, k] * active
            near_end = pltpu.roll(masked, low, 1)
            far_end = pltpu.roll(masked, (low + 4) % cols, 1)
            packed[f] = jnp.where(first, near_end, jnp.where(second, far_end, packed[f]))
    for f in range(fields):
        out_ref[f, 0] = packed[f]


def pack_edges(state, depth_class):
    fields, levels, rows, cols = state.shape
    return pl.pallas_call(
        pack_kernel,
        grid=(levels // PACK,),
        out_shape=jax.ShapeDtypeStruct((fields, levels // PACK, rows, cols), jnp.float32),
        in_specs=[pl.BlockSpec((rows, cols), lambda c: (0, 0)),
                  pl.BlockSpec((fields, PACK, rows, cols), lambda c: (0, c, 0, 0))],
        out_specs=pl.BlockSpec((fields, 1, rows, cols), lambda c: (0, c, 0, 0)),
        cost_estimate=pl.CostEstimate(
            flops=4 * state.size, transcendentals=0, bytes_accessed=4 * state.size
        ),
    )(depth_class, state)


def combine(from_south, from_north):
    lane = lax.broadcasted_iota(jnp.int32, from_south.shape, from_south.ndim - 1)
    return jnp.where(lane % 4 >= 2, from_south, from_north)


def wave_kernel(moving_ref, fixed_ref, coriolis_ref, out_ref):
    rows, cols = moving_ref.shape[1], moving_ref.shape[2]
    column_depth = fixed_ref[2]
    sea_mask = (column_depth > 0.0).astype(jnp.float32)
    force_east = fixed_ref[0]
    force_north = fixed_ref[1]
    coriolis = jnp.broadcast_to(coriolis_ref[0:1, :], (rows, cols))

    def x_slope_rolled(values):
        return (pltpu.roll(values, rows - 1, 0) - pltpu.roll(values, 1, 0)) * 0.5

    def y_slope_rolled(values):
        return (pltpu.roll(values, cols - 1, 1) - pltpu.roll(values, 1, 1)) * 0.5

    out_ref[...] = moving_ref[...]

    def step(index, carry):
        surface = out_ref[0]
        east_old = out_ref[1]
        north_old = out_ref[2]
        surface_mid = sea_mask * (
            surface - WAVE_STEP * (x_slope_rolled(east_old) + y_slope_rolled(north_old))
        )
        east_new = sea_mask * (
            east_old
            + WAVE_STEP
            * (
                -GRAVITY * column_depth * x_slope_rolled(surface_mid)
                + coriolis * north_old
                + force_east
                - BOTTOM_DRAG * east_old
            )
        )
        north_new = sea_mask * (
            north_old
            + WAVE_STEP
            * (
                -GRAVITY * column_depth * y_slope_rolled(surface_mid)
                - coriolis * east_new
                + force_north
                - BOTTOM_DRAG * north_old
            )
        )
        out_ref[0] = surface_mid
        out_ref[1] = east_new
        out_ref[2] = north_new
        return carry

    lax.fori_loop(0, SUB, step, 0)


def local_waves(moving, fixed, coriolis):
    rows, cols = moving.shape[1], moving.shape[2]
    elements = rows * cols
    return pl.pallas_call(
        wave_kernel,
        out_shape=jax.ShapeDtypeStruct(moving.shape, jnp.float32),
        in_specs=[pl.BlockSpec(memory_space=pltpu.VMEM)] * 3,
        out_specs=pl.BlockSpec(memory_space=pltpu.VMEM),
        cost_estimate=pl.CostEstimate(
            flops=SUB * 40 * elements, transcendentals=0, bytes_accessed=4 * 9 * elements
        ),
    )(moving, fixed, coriolis)


def body(state, depth_class, vertical_inverse, height, transport):
    levels = state.shape[1]
    level_block = levels // vertical_inverse.shape[0]
    y_cells = depth_class.shape[1]
    level_ids = lax.broadcasted_iota(jnp.int32, (levels, 1, 1), 0)
    active = (level_ids < depth_class[None] * level_block).astype(jnp.float32)
    west, east = edge_halo(state, active, "gx", 2, 2)
    column_blocks = lax.axis_size(("gy", "mode"))
    anchor = lax.axis_index(("gy", "mode")) * y_cells
    coriolis = jnp.broadcast_to(coriolis_row(anchor, y_cells, y_cells * column_blocks), (8, y_cells))
    rim = 2 * SUB
    column_depth = depth_class.astype(jnp.float32) * level_block / levels
    sea_mask = (depth_class > 0).astype(jnp.float32)
    moving = jnp.stack([height, transport[0], transport[1]]) * sea_mask
    early = jnp.concatenate([moving, column_depth[None]], axis=0)
    early = wide_halo(early, "gx", 1, rim)
    early = wide_halo(early, ("gy", "mode"), 2, rim)
    edges = pack_edges(state, depth_class)
    y_count = lax.axis_size(("gy", "mode"))
    from_south = lax.ppermute(edges, ("gy", "mode"), [(i, i + 1) for i in range(y_count - 1)])
    from_north = lax.ppermute(edges, ("gy", "mode"), [(i + 1, i) for i in range(y_count - 1)])
    side = combine(from_south, from_north)
    provisional, forcing = stencil(state, depth_class, west, east, side, coriolis)
    updated = vertical_solve(state, provisional, active, depth_class, vertical_inverse)
    late = wide_halo(forcing, "gx", 1, rim)
    late = wide_halo(late, ("gy", "mode"), 2, rim)
    fields = jnp.concatenate([early[0:3], late, early[3:4]], axis=0)
    coriolis_wide = jnp.broadcast_to(
        coriolis_row(anchor - rim, y_cells + 2 * rim, y_cells * column_blocks), (8, y_cells + 2 * rim)
    )
    waves_wide = local_waves(fields[0:3], fields[3:6], coriolis_wide)
    x_cells = depth_class.shape[0]
    waves = waves_wide[:, rim : rim + x_cells, rim : rim + y_cells]
    state_next = finish(updated, waves, active, depth_class, level_block, levels)
    return (state_next, waves[0], waves[1:3])


def solution(mesh):
    placed = (
        P(None, None, "gx", ("gy", "mode")),
        P("gx", ("gy", "mode")),
        P(),
        P("gx", ("gy", "mode")),
        P(None, "gx", ("gy", "mode")),
    )
    return jax.shard_map(
        body,
        mesh=mesh,
        in_specs=placed,
        out_specs=(
            P(None, None, "gx", ("gy", "mode")),
            P("gx", ("gy", "mode")),
            P(None, "gx", ("gy", "mode")),
        ),
        check_vma=False,
    )
```

```python
import jax
import jax.numpy as jnp
from jax import lax
from jax.experimental import pallas as pl
from jax.experimental.pallas import tpu as pltpu
from jax.sharding import PartitionSpec as P

SUB = 32
LEVEL_CHUNK = 8
PACK = 32


THERMAL = 0.8
HALINE = 0.6
PRESSURE_SCALE = 4.0
VISCOSITY = 0.1
STEP_TIME = 0.05
WAVE_STEP = 0.5
GRAVITY = 1.0
BOTTOM_DRAG = 0.05
CORIOLIS_BASE = 0.3
CORIOLIS_SLOPE = 0.4


def coriolis_row(anchor, number, total):
    position = (anchor + lax.broadcasted_iota(jnp.int32, (number,), 0)).astype(jnp.float32)
    return (CORIOLIS_BASE + CORIOLIS_SLOPE * (position + 0.5) / total)[None, :]


def vertical_solve(state, provisional, active, depth_class, inverse):
    levels = state.shape[1]
    classes = inverse.shape[0]
    band = levels // classes
    stacked = jnp.concatenate(
        [inverse[class_index, : band * (class_index + 1)] for class_index in range(classes)], axis=0
    )
    every = jnp.einsum("kl,flxy->fkxy", stacked, provisional, precision=lax.Precision.HIGH)
    starts = [band * class_index * (class_index + 1) // 2 for class_index in range(classes)]
    chosen = [(depth_class == class_index + 1).astype(jnp.float32) for class_index in range(classes)]
    bands = []
    for level_band in range(classes):
        part = jnp.zeros_like(provisional[:, :band])
        for class_index in range(level_band, classes):
            first = starts[class_index] + level_band * band
            part = part + chosen[class_index] * every[:, first : first + band]
        bands.append(part)
    solved = jnp.concatenate(bands, axis=1)
    return active * solved + (1.0 - active) * state


def edge_halo(state, active, axis, dim, width):
    count = lax.axis_size(axis)
    ends = count - 1
    size = state.shape[dim]
    head = lax.slice_in_dim(state, 0, width, axis=dim) * lax.slice_in_dim(active, 0, width, axis=dim - 1)
    tail = lax.slice_in_dim(state, size - width, size, axis=dim) * lax.slice_in_dim(
        active, size - width, size, axis=dim - 1
    )
    before = lax.ppermute(tail, axis, [(i, i + 1) for i in range(ends)])
    after = lax.ppermute(head, axis, [(i + 1, i) for i in range(ends)])
    return before, after


def wide_halo(cells, axis, dim, width):
    count = lax.axis_size(axis)
    size = cells.shape[dim]
    before, after = [], []
    remaining, hop = width, 1
    while remaining > 0:
        take = min(size, remaining)
        tail = lax.slice_in_dim(cells, size - take, size, axis=dim)
        head = lax.slice_in_dim(cells, 0, take, axis=dim)
        if hop < count:
            from_before = lax.ppermute(tail, axis, [(i, i + hop) for i in range(count - hop)])
            from_after = lax.ppermute(head, axis, [(i + hop, i) for i in range(count - hop)])
        else:
            from_before = jnp.zeros_like(tail)
            from_after = jnp.zeros_like(head)
        before.insert(0, from_before)
        after.append(from_after)
        remaining -= take
        hop += 1
    return jnp.concatenate(before + [cells] + after, axis=dim)


def stencil_kernel(depth_ref, coriolis_ref, state_ref, west_ref, east_ref, side_ref,
                   provisional_ref, forcing_ref, sums_ref):
    chunk = pl.program_id(0)
    fields, depth_levels, rows, cols = state_ref.shape
    levels = depth_levels * pl.num_programs(0)
    block = levels // 4

    @pl.when(chunk == 0)
    def _():
        sums_ref[...] = jnp.zeros_like(sums_ref)

    row = lax.broadcasted_iota(jnp.int32, (rows, cols), 0)
    lane = lax.broadcasted_iota(jnp.int32, (rows, cols), 1)
    reach = depth_ref[...] * block
    coriolis = coriolis_ref[0:1, :]

    def near(values, west, east, side):
        w0 = jnp.broadcast_to(west[0:1], (rows, cols))
        w1 = jnp.broadcast_to(west[1:2], (rows, cols))
        e0 = jnp.broadcast_to(east[0:1], (rows, cols))
        e1 = jnp.broadcast_to(east[1:2], (rows, cols))
        xm1 = jnp.where(row == 0, w1, pltpu.roll(values, 1, 0))
        xm2 = jnp.where(row == 0, w0, jnp.where(row == 1, w1, pltpu.roll(values, 2, 0)))
        xp1 = jnp.where(row == rows - 1, e0, pltpu.roll(values, rows - 1, 0))
        xp2 = jnp.where(row == rows - 2, e0, jnp.where(row == rows - 1, e1, pltpu.roll(values, rows - 2, 0)))
        ym1 = jnp.where(lane == 0, pltpu.roll(side, cols - 1, 1), pltpu.roll(values, 1, 1))
        ym2 = jnp.where(lane < 2, side, pltpu.roll(values, 2, 1))
        yp1 = jnp.where(lane == cols - 1, pltpu.roll(side, 1, 1), pltpu.roll(values, cols - 1, 1))
        yp2 = jnp.where(lane >= cols - 2, side, pltpu.roll(values, cols - 2, 1))
        return xm2, xm1, xp1, xp2, ym2, ym1, yp1, yp2

    def fourth(m2, m1, p1, p2):
        return (8.0 * (p1 - m1) - (p2 - m2)) * (1.0 / 12.0)

    def level(k, carry):
        global_level = chunk * depth_levels + k
        active = (global_level < reach).astype(jnp.float32)
        masked = [state_ref[f, k] * active for f in range(fields)]
        west = [west_ref[f, k] for f in range(fields)]
        east = [east_ref[f, k] for f in range(fields)]
        packed_level = global_level % PACK
        shift = (cols - 2 - 4 * packed_level) % cols
        side = [pltpu.roll(side_ref[f, global_level // PACK], shift, 1) for f in range(fields)]
        density = -THERMAL * masked[0] + HALINE * masked[1]
        density_w = -THERMAL * west[0] + HALINE * west[1]
        density_e = -THERMAL * east[0] + HALINE * east[1]
        density_s = -THERMAL * side[0] + HALINE * side[1]
        sums_ref[0] = sums_ref[0] + density
        sums_ref[1] = sums_ref[1] + density_s
        sums_ref[2, 0:2] = sums_ref[2, 0:2] + density_w
        sums_ref[2, 2:4] = sums_ref[2, 2:4] + density_e
        scale = PRESSURE_SCALE / levels
        pressure = scale * sums_ref[0]
        pressure_s = scale * sums_ref[1]
        pressure_w = scale * sums_ref[2, 0:2]
        pressure_e = scale * sums_ref[2, 2:4]
        east_vel = masked[2]
        north_vel = masked[3]
        pm2, pm1, pp1, pp2, qm2, qm1, qp1, qp2 = near(pressure, pressure_w, pressure_e, pressure_s)
        extra = [None, None,
                 -fourth(pm2, pm1, pp1, pp2) + coriolis * north_vel,
                 -fourth(qm2, qm1, qp1, qp2) - coriolis * east_vel]
        for f in range(fields):
            xm2, xm1, xp1, xp2, ym2, ym1, yp1, yp2 = near(masked[f], west[f], east[f], side[f])
            lap = xp1 + xm1 + yp1 + ym1 - 4.0 * masked[f]
            tendency = -(east_vel * fourth(xm2, xm1, xp1, xp2) + north_vel * fourth(ym2, ym1, yp1, yp2)) + VISCOSITY * lap
            if extra[f] is not None:
                tendency = tendency + extra[f]
                forcing_ref[f - 2] = forcing_ref[f - 2] + active * tendency
            provisional_ref[f, k] = active * (masked[f] + STEP_TIME * tendency)
        return carry

    @pl.when(chunk == 0)
    def _():
        forcing_ref[...] = jnp.zeros_like(forcing_ref)

    lax.fori_loop(0, depth_levels, level, 0)

    @pl.when(chunk == pl.num_programs(0) - 1)
    def _():
        forcing_ref[...] = forcing_ref[...] / levels


def stencil(state, depth_class, west, east, side, coriolis):
    fields, levels, rows, cols = state.shape
    steps = levels // LEVEL_CHUNK
    big = pl.BlockSpec((fields, LEVEL_CHUNK, rows, cols), lambda c: (0, c, 0, 0))
    rim = pl.BlockSpec((fields, LEVEL_CHUNK, 2, cols), lambda c: (0, c, 0, 0))
    flat = pl.BlockSpec((rows, cols), lambda c: (0, 0))
    packed = pl.BlockSpec(side.shape, lambda c: (0, 0, 0, 0))
    return pl.pallas_call(
        stencil_kernel,
        grid=(steps,),
        out_shape=(jax.ShapeDtypeStruct(state.shape, jnp.float32),
                   jax.ShapeDtypeStruct((2, rows, cols), jnp.float32)),
        in_specs=[flat, pl.BlockSpec((8, cols), lambda c: (0, 0)), big, rim, rim, packed],
        out_specs=(big, pl.BlockSpec((2, rows, cols), lambda c: (0, 0, 0))),
        scratch_shapes=[pltpu.VMEM((3, rows, cols), jnp.float32)],
        compiler_params=pltpu.CompilerParams(dimension_semantics=("arbitrary",)),
        cost_estimate=pl.CostEstimate(
            flops=60 * state.size, transcendentals=0, bytes_accessed=4 * 2 * state.size
        ),
    )(depth_class, coriolis, state, west, east, side)


def pack_kernel(depth_ref, state_ref, out_ref):
    block_index = pl.program_id(0)
    fields, depth_levels, rows, cols = state_ref.shape
    block = depth_levels * pl.num_programs(0) // 4
    lane = lax.broadcasted_iota(jnp.int32, (rows, cols), 1)
    reach = depth_ref[...] * block
    packed = [jnp.zeros((rows, cols), jnp.float32) for f in range(fields)]
    for k in range(depth_levels):
        active = (block_index * depth_levels + k < reach).astype(jnp.float32)
        low = 4 * k
        first = (lane == low) | (lane == low + 1)
        second = (lane == low + 2) | (lane == low + 3)
        for f in range(fields):
            masked = state_ref[f, k] * active
            near_end = pltpu.roll(masked, low, 1)
            far_end = pltpu.roll(masked, (low + 4) % cols, 1)
            packed[f] = jnp.where(first, near_end, jnp.where(second, far_end, packed[f]))
    for f in range(fields):
        out_ref[f, 0] = packed[f]


def pack_edges(state, depth_class):
    fields, levels, rows, cols = state.shape
    return pl.pallas_call(
        pack_kernel,
        grid=(levels // PACK,),
        out_shape=jax.ShapeDtypeStruct((fields, levels // PACK, rows, cols), jnp.float32),
        in_specs=[pl.BlockSpec((rows, cols), lambda c: (0, 0)),
                  pl.BlockSpec((fields, PACK, rows, cols), lambda c: (0, c, 0, 0))],
        out_specs=pl.BlockSpec((fields, 1, rows, cols), lambda c: (0, c, 0, 0)),
        cost_estimate=pl.CostEstimate(
            flops=4 * state.size, transcendentals=0, bytes_accessed=4 * state.size
        ),
    )(depth_class, state)


def combine(from_south, from_north):
    lane = lax.broadcasted_iota(jnp.int32, from_south.shape, from_south.ndim - 1)
    return jnp.where(lane % 4 >= 2, from_south, from_north)


def wave_kernel(moving_ref, fixed_ref, coriolis_ref, out_ref, work_ref):
    rows, cols = moving_ref.shape[1], moving_ref.shape[2]
    inner_rows, inner_cols = out_ref.shape[1], out_ref.shape[2]
    rim = (rows - inner_rows) // 2
    groups = 4
    per_group = SUB // groups
    trim = 2 * per_group
    work_ref[...] = moving_ref[...]
    for group in range(groups):
        low = trim * group
        high = rows - trim * group
        span = high - low
        column_depth = fixed_ref[2, low:high]
        sea_mask = (column_depth > 0.0).astype(jnp.float32)
        force_east = fixed_ref[0, low:high]
        force_north = fixed_ref[1, low:high]
        coriolis = jnp.broadcast_to(coriolis_ref[0:1, :], (span, cols))

        def x_slope_rolled(values):
            return (pltpu.roll(values, span - 1, 0) - pltpu.roll(values, 1, 0)) * 0.5

        def y_slope_rolled(values):
            return (pltpu.roll(values, cols - 1, 1) - pltpu.roll(values, 1, 1)) * 0.5

        def step(index, carry):
            surface = work_ref[0, low:high]
            east_old = work_ref[1, low:high]
            north_old = work_ref[2, low:high]
            surface_mid = sea_mask * (
                surface - WAVE_STEP * (x_slope_rolled(east_old) + y_slope_rolled(north_old))
            )
            east_new = sea_mask * (
                east_old
                + WAVE_STEP
                * (
                    -GRAVITY * column_depth * x_slope_rolled(surface_mid)
                    + coriolis * north_old
                    + force_east
                    - BOTTOM_DRAG * east_old
                )
            )
            north_new = sea_mask * (
                north_old
                + WAVE_STEP
                * (
                    -GRAVITY * column_depth * y_slope_rolled(surface_mid)
                    - coriolis * east_new
                    + force_north
                    - BOTTOM_DRAG * north_old
                )
            )
            work_ref[0, low:high] = surface_mid
            work_ref[1, low:high] = east_new
            work_ref[2, low:high] = north_new
            return carry

        lax.fori_loop(0, per_group, step, 0)
    for field in range(3):
        middle = work_ref[field, rim : rim + inner_rows]
        out_ref[field] = pltpu.roll(middle, cols - rim, 1)[:, :inner_cols]


def local_waves(moving, fixed, coriolis, inner_rows, inner_cols):
    rows, cols = moving.shape[1], moving.shape[2]
    elements = rows * cols
    return pl.pallas_call(
        wave_kernel,
        out_shape=jax.ShapeDtypeStruct((3, inner_rows, inner_cols), jnp.float32),
        in_specs=[pl.BlockSpec(memory_space=pltpu.VMEM)] * 3,
        out_specs=pl.BlockSpec(memory_space=pltpu.VMEM),
        scratch_shapes=[pltpu.VMEM(moving.shape, jnp.float32)],
        cost_estimate=pl.CostEstimate(
            flops=SUB * 30 * elements, transcendentals=0, bytes_accessed=4 * 7 * elements
        ),
    )(moving, fixed, coriolis)


def finish_kernel(depth_ref, waves_ref, updated_ref, out_ref):
    field = pl.program_id(0)
    levels = updated_ref.shape[1]
    block = levels // 4
    depth_class = depth_ref[...]

    @pl.when(field < 2)
    def _():
        out_ref[...] = updated_ref[...]

    @pl.when(field >= 2)
    def _():
        reach = depth_class * block
        counted = jnp.maximum(reach, 1).astype(jnp.float32)
        safe_depth = jnp.maximum(depth_class, 1).astype(jnp.float32) * block / levels
        total = jnp.zeros(depth_class.shape, jnp.float32)
        for k in range(levels):
            active = (k < reach).astype(jnp.float32)
            total = total + active * updated_ref[0, k]
        carried = waves_ref[0] / safe_depth
        shift = carried - total / counted
        for k in range(levels):
            active = (k < reach).astype(jnp.float32)
            out_ref[0, k] = updated_ref[0, k] + active * shift


def finish_state(updated, waves, depth_class):
    fields, levels, rows, cols = updated.shape
    whole = pl.BlockSpec((1, levels, rows, cols), lambda f: (f, 0, 0, 0))
    return pl.pallas_call(
        finish_kernel,
        grid=(fields,),
        out_shape=jax.ShapeDtypeStruct(updated.shape, jnp.float32),
        in_specs=[
            pl.BlockSpec((rows, cols), lambda f: (0, 0)),
            pl.BlockSpec((1, rows, cols), lambda f: (jnp.maximum(f - 1, 0), 0, 0)),
            whole,
        ],
        out_specs=whole,
        cost_estimate=pl.CostEstimate(
            flops=4 * updated.size, transcendentals=0, bytes_accessed=4 * 2 * updated.size
        ),
    )(depth_class, waves, updated)


def body(state, depth_class, vertical_inverse, height, transport):
    levels = state.shape[1]
    level_block = levels // vertical_inverse.shape[0]
    y_cells = depth_class.shape[1]
    level_ids = lax.broadcasted_iota(jnp.int32, (levels, 1, 1), 0)
    active = (level_ids < depth_class[None] * level_block).astype(jnp.float32)
    west, east = edge_halo(state, active, "gx", 2, 2)
    column_blocks = lax.axis_size(("gy", "mode"))
    anchor = lax.axis_index(("gy", "mode")) * y_cells
    coriolis = jnp.broadcast_to(coriolis_row(anchor, y_cells, y_cells * column_blocks), (8, y_cells))
    edges = pack_edges(state, depth_class)
    y_count = lax.axis_size(("gy", "mode"))
    from_south = lax.ppermute(edges, ("gy", "mode"), [(i, i + 1) for i in range(y_count - 1)])
    from_north = lax.ppermute(edges, ("gy", "mode"), [(i + 1, i) for i in range(y_count - 1)])
    side = combine(from_south, from_north)
    provisional, forcing = stencil(state, depth_class, west, east, side, coriolis)
    updated = vertical_solve(state, provisional, active, depth_class, vertical_inverse)
    column_depth = depth_class.astype(jnp.float32) * level_block / levels
    sea_mask = (depth_class > 0).astype(jnp.float32)
    moving = jnp.stack([height, transport[0], transport[1]]) * sea_mask
    fields = jnp.stack([moving[0], moving[1], moving[2], forcing[0], forcing[1], column_depth])
    rim = 2 * SUB
    fields = wide_halo(fields, "gx", 1, rim)
    fields = wide_halo(fields, ("gy", "mode"), 2, rim)
    coriolis_wide = jnp.broadcast_to(
        coriolis_row(anchor - rim, y_cells + 2 * rim, y_cells * column_blocks), (8, y_cells + 2 * rim)
    )
    x_cells = depth_class.shape[0]
    waves = local_waves(fields[0:3], fields[3:6], coriolis_wide, x_cells, y_cells)
    state_next = finish_state(updated, waves, depth_class)
    return (state_next, waves[0], waves[1:3])


def solution(mesh):
    placed = (
        P(None, None, "gx", ("gy", "mode")),
        P("gx", ("gy", "mode")),
        P(),
        P("gx", ("gy", "mode")),
        P(None, "gx", ("gy", "mode")),
    )
    return jax.shard_map(
        body,
        mesh=mesh,
        in_specs=placed,
        out_specs=(
            P(None, None, "gx", ("gy", "mode")),
            P("gx", ("gy", "mode")),
            P(None, "gx", ("gy", "mode")),
        ),
        check_vma=False,
    )
```

```python
import jax
import jax.numpy as jnp
from jax import lax
from jax.experimental import pallas as pl
from jax.experimental.pallas import tpu as pltpu
from jax.sharding import PartitionSpec as P

SUB = 32
LEVEL_CHUNK = 8
PACK = 32


THERMAL = 0.8
HALINE = 0.6
PRESSURE_SCALE = 4.0
VISCOSITY = 0.1
STEP_TIME = 0.05
WAVE_STEP = 0.5
GRAVITY = 1.0
BOTTOM_DRAG = 0.05
CORIOLIS_BASE = 0.3
CORIOLIS_SLOPE = 0.4


def coriolis_row(anchor, number, total):
    position = (anchor + lax.broadcasted_iota(jnp.int32, (number,), 0)).astype(jnp.float32)
    return (CORIOLIS_BASE + CORIOLIS_SLOPE * (position + 0.5) / total)[None, :]


def vertical_solve(state, provisional, active, depth_class, inverse):
    levels = state.shape[1]
    classes = inverse.shape[0]
    band = levels // classes
    stacked = jnp.concatenate(
        [inverse[class_index, : band * (class_index + 1)] for class_index in range(classes)], axis=0
    )
    every = jnp.einsum("kl,flxy->fkxy", stacked, provisional, precision=lax.Precision.HIGH)
    starts = [band * class_index * (class_index + 1) // 2 for class_index in range(classes)]
    chosen = [(depth_class == class_index + 1).astype(jnp.float32) for class_index in range(classes)]
    bands = []
    for level_band in range(classes):
        part = jnp.zeros_like(provisional[:, :band])
        for class_index in range(level_band, classes):
            first = starts[class_index] + level_band * band
            part = part + chosen[class_index] * every[:, first : first + band]
        bands.append(part)
    solved = jnp.concatenate(bands, axis=1)
    return active * solved + (1.0 - active) * state


def edge_halo(state, active, axis, dim, width):
    count = lax.axis_size(axis)
    ends = count - 1
    size = state.shape[dim]
    head = lax.slice_in_dim(state, 0, width, axis=dim) * lax.slice_in_dim(active, 0, width, axis=dim - 1)
    tail = lax.slice_in_dim(state, size - width, size, axis=dim) * lax.slice_in_dim(
        active, size - width, size, axis=dim - 1
    )
    before = lax.ppermute(tail, axis, [(i, i + 1) for i in range(ends)])
    after = lax.ppermute(head, axis, [(i + 1, i) for i in range(ends)])
    return before, after


def finish(updated, transport_next, active, depth_class, level_block, levels):
    counted = jnp.maximum(depth_class * level_block, 1).astype(jnp.float32)
    safe_depth = jnp.maximum(depth_class, 1).astype(jnp.float32) * level_block / levels
    column_means = jnp.sum(active * updated[2:4], axis=1) / counted
    carried = transport_next / safe_depth
    velocity = updated[2:4] + active * (carried - column_means)[:, None]
    return jnp.concatenate([updated[0:2], velocity], axis=0)


def wide_halo(cells, axis, dim, width):
    count = lax.axis_size(axis)
    size = cells.shape[dim]
    before, after = [], []
    remaining, hop = width, 1
    while remaining > 0:
        take = min(size, remaining)
        tail = lax.slice_in_dim(cells, size - take, size, axis=dim)
        head = lax.slice_in_dim(cells, 0, take, axis=dim)
        if hop < count:
            from_before = lax.ppermute(tail, axis, [(i, i + hop) for i in range(count - hop)])
            from_after = lax.ppermute(head, axis, [(i + hop, i) for i in range(count - hop)])
        else:
            from_before = jnp.zeros_like(tail)
            from_after = jnp.zeros_like(head)
        before.insert(0, from_before)
        after.append(from_after)
        remaining -= take
        hop += 1
    return jnp.concatenate(before + [cells] + after, axis=dim)


def stencil_kernel(depth_ref, coriolis_ref, state_ref, west_ref, east_ref, side_ref,
                   provisional_ref, forcing_ref, sums_ref):
    chunk = pl.program_id(0)
    fields, depth_levels, rows, cols = state_ref.shape
    levels = depth_levels * pl.num_programs(0)
    block = levels // 4

    @pl.when(chunk == 0)
    def _():
        sums_ref[...] = jnp.zeros_like(sums_ref)

    row = lax.broadcasted_iota(jnp.int32, (rows, cols), 0)
    lane = lax.broadcasted_iota(jnp.int32, (rows, cols), 1)
    reach = depth_ref[...] * block
    coriolis = coriolis_ref[0:1, :]

    def near(values, west, east, side):
        w0 = jnp.broadcast_to(west[0:1], (rows, cols))
        w1 = jnp.broadcast_to(west[1:2], (rows, cols))
        e0 = jnp.broadcast_to(east[0:1], (rows, cols))
        e1 = jnp.broadcast_to(east[1:2], (rows, cols))
        xm1 = jnp.where(row == 0, w1, pltpu.roll(values, 1, 0))
        xm2 = jnp.where(row == 0, w0, jnp.where(row == 1, w1, pltpu.roll(values, 2, 0)))
        xp1 = jnp.where(row == rows - 1, e0, pltpu.roll(values, rows - 1, 0))
        xp2 = jnp.where(row == rows - 2, e0, jnp.where(row == rows - 1, e1, pltpu.roll(values, rows - 2, 0)))
        ym1 = jnp.where(lane == 0, pltpu.roll(side, cols - 1, 1), pltpu.roll(values, 1, 1))
        ym2 = jnp.where(lane < 2, side, pltpu.roll(values, 2, 1))
        yp1 = jnp.where(lane == cols - 1, pltpu.roll(side, 1, 1), pltpu.roll(values, cols - 1, 1))
        yp2 = jnp.where(lane >= cols - 2, side, pltpu.roll(values, cols - 2, 1))
        return xm2, xm1, xp1, xp2, ym2, ym1, yp1, yp2

    def fourth(m2, m1, p1, p2):
        return (8.0 * (p1 - m1) - (p2 - m2)) * (1.0 / 12.0)

    def level(k, carry):
        global_level = chunk * depth_levels + k
        active = (global_level < reach).astype(jnp.float32)
        masked = [state_ref[f, k] * active for f in range(fields)]
        west = [west_ref[f, k] for f in range(fields)]
        east = [east_ref[f, k] for f in range(fields)]
        packed_level = global_level % PACK
        shift = (cols - 2 - 4 * packed_level) % cols
        side = [pltpu.roll(side_ref[f, global_level // PACK], shift, 1) for f in range(fields)]
        density = -THERMAL * masked[0] + HALINE * masked[1]
        density_w = -THERMAL * west[0] + HALINE * west[1]
        density_e = -THERMAL * east[0] + HALINE * east[1]
        density_s = -THERMAL * side[0] + HALINE * side[1]
        sums_ref[0] = sums_ref[0] + density
        sums_ref[1] = sums_ref[1] + density_s
        sums_ref[2, 0:2] = sums_ref[2, 0:2] + density_w
        sums_ref[2, 2:4] = sums_ref[2, 2:4] + density_e
        scale = PRESSURE_SCALE / levels
        pressure = scale * sums_ref[0]
        pressure_s = scale * sums_ref[1]
        pressure_w = scale * sums_ref[2, 0:2]
        pressure_e = scale * sums_ref[2, 2:4]
        east_vel = masked[2]
        north_vel = masked[3]
        pm2, pm1, pp1, pp2, qm2, qm1, qp1, qp2 = near(pressure, pressure_w, pressure_e, pressure_s)
        extra = [None, None,
                 -fourth(pm2, pm1, pp1, pp2) + coriolis * north_vel,
                 -fourth(qm2, qm1, qp1, qp2) - coriolis * east_vel]
        for f in range(fields):
            xm2, xm1, xp1, xp2, ym2, ym1, yp1, yp2 = near(masked[f], west[f], east[f], side[f])
            lap = xp1 + xm1 + yp1 + ym1 - 4.0 * masked[f]
            tendency = -(east_vel * fourth(xm2, xm1, xp1, xp2) + north_vel * fourth(ym2, ym1, yp1, yp2)) + VISCOSITY * lap
            if extra[f] is not None:
                tendency = tendency + extra[f]
                forcing_ref[f - 2] = forcing_ref[f - 2] + active * tendency
            provisional_ref[f, k] = active * (masked[f] + STEP_TIME * tendency)
        return carry

    @pl.when(chunk == 0)
    def _():
        forcing_ref[...] = jnp.zeros_like(forcing_ref)

    lax.fori_loop(0, depth_levels, level, 0)

    @pl.when(chunk == pl.num_programs(0) - 1)
    def _():
        forcing_ref[...] = forcing_ref[...] / levels


def stencil(state, depth_class, west, east, side, coriolis):
    fields, levels, rows, cols = state.shape
    steps = levels // LEVEL_CHUNK
    big = pl.BlockSpec((fields, LEVEL_CHUNK, rows, cols), lambda c: (0, c, 0, 0))
    rim = pl.BlockSpec((fields, LEVEL_CHUNK, 2, cols), lambda c: (0, c, 0, 0))
    flat = pl.BlockSpec((rows, cols), lambda c: (0, 0))
    packed = pl.BlockSpec(side.shape, lambda c: (0, 0, 0, 0))
    return pl.pallas_call(
        stencil_kernel,
        grid=(steps,),
        out_shape=(jax.ShapeDtypeStruct(state.shape, jnp.float32),
                   jax.ShapeDtypeStruct((2, rows, cols), jnp.float32)),
        in_specs=[flat, pl.BlockSpec((8, cols), lambda c: (0, 0)), big, rim, rim, packed],
        out_specs=(big, pl.BlockSpec((2, rows, cols), lambda c: (0, 0, 0))),
        scratch_shapes=[pltpu.VMEM((3, rows, cols), jnp.float32)],
        compiler_params=pltpu.CompilerParams(dimension_semantics=("arbitrary",)),
        cost_estimate=pl.CostEstimate(
            flops=60 * state.size, transcendentals=0, bytes_accessed=4 * 2 * state.size
        ),
    )(depth_class, coriolis, state, west, east, side)


def pack_kernel(depth_ref, state_ref, out_ref):
    block_index = pl.program_id(0)
    fields, depth_levels, rows, cols = state_ref.shape
    block = depth_levels * pl.num_programs(0) // 4
    lane = lax.broadcasted_iota(jnp.int32, (rows, cols), 1)
    reach = depth_ref[...] * block
    packed = [jnp.zeros((rows, cols), jnp.float32) for f in range(fields)]
    for k in range(depth_levels):
        active = (block_index * depth_levels + k < reach).astype(jnp.float32)
        low = 4 * k
        first = (lane == low) | (lane == low + 1)
        second = (lane == low + 2) | (lane == low + 3)
        for f in range(fields):
            masked = state_ref[f, k] * active
            near_end = pltpu.roll(masked, low, 1)
            far_end = pltpu.roll(masked, (low + 4) % cols, 1)
            packed[f] = jnp.where(first, near_end, jnp.where(second, far_end, packed[f]))
    for f in range(fields):
        out_ref[f, 0] = packed[f]


def pack_edges(state, depth_class):
    fields, levels, rows, cols = state.shape
    return pl.pallas_call(
        pack_kernel,
        grid=(levels // PACK,),
        out_shape=jax.ShapeDtypeStruct((fields, levels // PACK, rows, cols), jnp.float32),
        in_specs=[pl.BlockSpec((rows, cols), lambda c: (0, 0)),
                  pl.BlockSpec((fields, PACK, rows, cols), lambda c: (0, c, 0, 0))],
        out_specs=pl.BlockSpec((fields, 1, rows, cols), lambda c: (0, c, 0, 0)),
        cost_estimate=pl.CostEstimate(
            flops=4 * state.size, transcendentals=0, bytes_accessed=4 * state.size
        ),
    )(depth_class, state)


def combine(from_south, from_north):
    lane = lax.broadcasted_iota(jnp.int32, from_south.shape, from_south.ndim - 1)
    return jnp.where(lane % 4 >= 2, from_south, from_north)


def wave_kernel(moving_ref, fixed_ref, coriolis_ref, height_ref, transport_ref, work_ref):
    rows, cols = moving_ref.shape[1], moving_ref.shape[2]
    inner_rows, inner_cols = height_ref.shape[0], height_ref.shape[1]
    rim = (rows - inner_rows) // 2
    groups = 4
    per_group = SUB // groups
    trim = 2 * per_group
    work_ref[...] = moving_ref[...]
    for group in range(groups):
        low = trim * group
        high = rows - trim * group
        span = high - low
        column_depth = fixed_ref[2, low:high]
        sea_mask = (column_depth > 0.0).astype(jnp.float32)
        force_east = fixed_ref[0, low:high]
        force_north = fixed_ref[1, low:high]
        coriolis = jnp.broadcast_to(coriolis_ref[0:1, :], (span, cols))

        def x_slope_rolled(values):
            return (pltpu.roll(values, span - 1, 0) - pltpu.roll(values, 1, 0)) * 0.5

        def y_slope_rolled(values):
            return (pltpu.roll(values, cols - 1, 1) - pltpu.roll(values, 1, 1)) * 0.5

        def step(index, carry):
            surface = work_ref[0, low:high]
            east_old = work_ref[1, low:high]
            north_old = work_ref[2, low:high]
            surface_mid = sea_mask * (
                surface - WAVE_STEP * (x_slope_rolled(east_old) + y_slope_rolled(north_old))
            )
            east_new = sea_mask * (
                east_old
                + WAVE_STEP
                * (
                    -GRAVITY * column_depth * x_slope_rolled(surface_mid)
                    + coriolis * north_old
                    + force_east
                    - BOTTOM_DRAG * east_old
                )
            )
            north_new = sea_mask * (
                north_old
                + WAVE_STEP
                * (
                    -GRAVITY * column_depth * y_slope_rolled(surface_mid)
                    - coriolis * east_new
                    + force_north
                    - BOTTOM_DRAG * north_old
                )
            )
            work_ref[0, low:high] = surface_mid
            work_ref[1, low:high] = east_new
            work_ref[2, low:high] = north_new
            return carry

        lax.fori_loop(0, per_group, step, 0)
    for field in range(3):
        middle = work_ref[field, rim : rim + inner_rows]
        inner = pltpu.roll(middle, cols - rim, 1)[:, :inner_cols]
        if field == 0:
            height_ref[...] = inner
        else:
            transport_ref[field - 1] = inner


def local_waves(moving, fixed, coriolis, inner_rows, inner_cols):
    rows, cols = moving.shape[1], moving.shape[2]
    elements = rows * cols
    return pl.pallas_call(
        wave_kernel,
        out_shape=(
            jax.ShapeDtypeStruct((inner_rows, inner_cols), jnp.float32),
            jax.ShapeDtypeStruct((2, inner_rows, inner_cols), jnp.float32),
        ),
        in_specs=[pl.BlockSpec(memory_space=pltpu.VMEM)] * 3,
        out_specs=(pl.BlockSpec(memory_space=pltpu.VMEM), pl.BlockSpec(memory_space=pltpu.VMEM)),
        scratch_shapes=[pltpu.VMEM(moving.shape, jnp.float32)],
        cost_estimate=pl.CostEstimate(
            flops=SUB * 30 * elements, transcendentals=0, bytes_accessed=4 * 7 * elements
        ),
    )(moving, fixed, coriolis)


def body(state, depth_class, vertical_inverse, height, transport):
    levels = state.shape[1]
    level_block = levels // vertical_inverse.shape[0]
    y_cells = depth_class.shape[1]
    level_ids = lax.broadcasted_iota(jnp.int32, (levels, 1, 1), 0)
    active = (level_ids < depth_class[None] * level_block).astype(jnp.float32)
    west, east = edge_halo(state, active, "gx", 2, 2)
    column_blocks = lax.axis_size(("gy", "mode"))
    anchor = lax.axis_index(("gy", "mode")) * y_cells
    coriolis = jnp.broadcast_to(coriolis_row(anchor, y_cells, y_cells * column_blocks), (8, y_cells))
    edges = pack_edges(state, depth_class)
    y_count = lax.axis_size(("gy", "mode"))
    from_south = lax.ppermute(edges, ("gy", "mode"), [(i, i + 1) for i in range(y_count - 1)])
    from_north = lax.ppermute(edges, ("gy", "mode"), [(i + 1, i) for i in range(y_count - 1)])
    side = combine(from_south, from_north)
    provisional, forcing = stencil(state, depth_class, west, east, side, coriolis)
    updated = vertical_solve(state, provisional, active, depth_class, vertical_inverse)
    column_depth = depth_class.astype(jnp.float32) * level_block / levels
    sea_mask = (depth_class > 0).astype(jnp.float32)
    moving = jnp.stack([height, transport[0], transport[1]]) * sea_mask
    fields = jnp.stack([moving[0], moving[1], moving[2], forcing[0], forcing[1], column_depth])
    rim = 2 * SUB
    fields = wide_halo(fields, "gx", 1, rim)
    fields = wide_halo(fields, ("gy", "mode"), 2, rim)
    coriolis_wide = jnp.broadcast_to(
        coriolis_row(anchor - rim, y_cells + 2 * rim, y_cells * column_blocks), (8, y_cells + 2 * rim)
    )
    x_cells = depth_class.shape[0]
    height_next, transport_next = local_waves(fields[0:3], fields[3:6], coriolis_wide, x_cells, y_cells)
    state_next = finish(updated, transport_next, active, depth_class, level_block, levels)
    return (state_next, height_next, transport_next)


def solution(mesh):
    placed = (
        P(None, None, "gx", ("gy", "mode")),
        P("gx", ("gy", "mode")),
        P(),
        P("gx", ("gy", "mode")),
        P(None, "gx", ("gy", "mode")),
    )
    return jax.shard_map(
        body,
        mesh=mesh,
        in_specs=placed,
        out_specs=(
            P(None, None, "gx", ("gy", "mode")),
            P("gx", ("gy", "mode")),
            P(None, "gx", ("gy", "mode")),
        ),
        check_vma=False,
    )
```

```python
import jax
import numpy as np
import jax.numpy as jnp
from jax import lax
from jax.experimental import pallas as pl
from jax.experimental.pallas import tpu as pltpu
from jax.sharding import PartitionSpec as P

SUB = 32
LEVEL_CHUNK = 8
PACK = 32


THERMAL = 0.8
HALINE = 0.6
PRESSURE_SCALE = 4.0
VISCOSITY = 0.1
STEP_TIME = 0.05
WAVE_STEP = 0.5
GRAVITY = 1.0
BOTTOM_DRAG = 0.05
CORIOLIS_BASE = 0.3
CORIOLIS_SLOPE = 0.4


def coriolis_row(anchor, number, total):
    position = (anchor + lax.broadcasted_iota(jnp.int32, (number,), 0)).astype(jnp.float32)
    return (CORIOLIS_BASE + CORIOLIS_SLOPE * (position + 0.5) / total)[None, :]


def vertical_solve(state, provisional, active, depth_class, inverse):
    levels = state.shape[1]
    classes = inverse.shape[0]
    band = levels // classes
    rows_used = np.concatenate(
        [class_index * levels + np.arange(band * (class_index + 1)) for class_index in range(classes)]
    )
    stacked = jnp.take(inverse.reshape(classes * levels, inverse.shape[2]), rows_used, axis=0)
    every = jnp.einsum("kl,flxy->fkxy", stacked, provisional, precision=lax.Precision.HIGH)
    starts = [band * class_index * (class_index + 1) // 2 for class_index in range(classes)]
    chosen = [(depth_class == class_index + 1).astype(jnp.float32) for class_index in range(classes)]
    bands = []
    for level_band in range(classes):
        part = jnp.zeros_like(provisional[:, :band])
        for class_index in range(level_band, classes):
            first = starts[class_index] + level_band * band
            part = part + chosen[class_index] * every[:, first : first + band]
        bands.append(part)
    solved = jnp.concatenate(bands, axis=1)
    return active * solved + (1.0 - active) * state


def finish(updated, transport_next, active, depth_class, level_block, levels):
    counted = jnp.maximum(depth_class * level_block, 1).astype(jnp.float32)
    safe_depth = jnp.maximum(depth_class, 1).astype(jnp.float32) * level_block / levels
    column_means = jnp.sum(active * updated[2:4], axis=1) / counted
    carried = transport_next / safe_depth
    velocity = updated[2:4] + active * (carried - column_means)[:, None]
    return jnp.concatenate([updated[0:2], velocity], axis=0)


def wide_halo(cells, axis, dim, width):
    count = lax.axis_size(axis)
    size = cells.shape[dim]
    before, after = [], []
    remaining, hop = width, 1
    while remaining > 0:
        take = min(size, remaining)
        tail = lax.slice_in_dim(cells, size - take, size, axis=dim)
        head = lax.slice_in_dim(cells, 0, take, axis=dim)
        if hop < count:
            from_before = lax.ppermute(tail, axis, [(i, i + hop) for i in range(count - hop)])
            from_after = lax.ppermute(head, axis, [(i + hop, i) for i in range(count - hop)])
        else:
            from_before = jnp.zeros_like(tail)
            from_after = jnp.zeros_like(head)
        before.insert(0, from_before)
        after.append(from_after)
        remaining -= take
        hop += 1
    return jnp.concatenate(before + [cells] + after, axis=dim)


def stencil_kernel(depth_ref, coriolis_ref, state_ref, west_ref, east_ref, side_ref,
                   provisional_ref, forcing_ref, sums_ref):
    chunk = pl.program_id(0)
    fields, depth_levels, rows, cols = state_ref.shape
    levels = depth_levels * pl.num_programs(0)
    block = levels // 4

    @pl.when(chunk == 0)
    def _():
        sums_ref[...] = jnp.zeros_like(sums_ref)

    row = lax.broadcasted_iota(jnp.int32, (rows, cols), 0)
    lane = lax.broadcasted_iota(jnp.int32, (rows, cols), 1)
    reach = depth_ref[...] * block
    coriolis = coriolis_ref[0:1, :]

    def near(values, west, east, side):
        w0 = jnp.broadcast_to(west[0:1], (rows, cols))
        w1 = jnp.broadcast_to(west[1:2], (rows, cols))
        e0 = jnp.broadcast_to(east[0:1], (rows, cols))
        e1 = jnp.broadcast_to(east[1:2], (rows, cols))
        xm1 = jnp.where(row == 0, w1, pltpu.roll(values, 1, 0))
        xm2 = jnp.where(row == 0, w0, jnp.where(row == 1, w1, pltpu.roll(values, 2, 0)))
        xp1 = jnp.where(row == rows - 1, e0, pltpu.roll(values, rows - 1, 0))
        xp2 = jnp.where(row == rows - 2, e0, jnp.where(row == rows - 1, e1, pltpu.roll(values, rows - 2, 0)))
        ym1 = jnp.where(lane == 0, pltpu.roll(side, cols - 1, 1), pltpu.roll(values, 1, 1))
        ym2 = jnp.where(lane < 2, side, pltpu.roll(values, 2, 1))
        yp1 = jnp.where(lane == cols - 1, pltpu.roll(side, 1, 1), pltpu.roll(values, cols - 1, 1))
        yp2 = jnp.where(lane >= cols - 2, side, pltpu.roll(values, cols - 2, 1))
        return xm2, xm1, xp1, xp2, ym2, ym1, yp1, yp2

    def fourth(m2, m1, p1, p2):
        return (8.0 * (p1 - m1) - (p2 - m2)) * (1.0 / 12.0)

    def level(k, carry):
        global_level = chunk * depth_levels + k
        active = (global_level < reach).astype(jnp.float32)
        masked = [state_ref[f, k] * active for f in range(fields)]
        west = [west_ref[f, k] for f in range(fields)]
        east = [east_ref[f, k] for f in range(fields)]
        packed_level = global_level % PACK
        shift = (cols - 2 - 4 * packed_level) % cols
        side = [pltpu.roll(side_ref[f, global_level // PACK], shift, 1) for f in range(fields)]
        density = -THERMAL * masked[0] + HALINE * masked[1]
        density_w = -THERMAL * west[0] + HALINE * west[1]
        density_e = -THERMAL * east[0] + HALINE * east[1]
        density_s = -THERMAL * side[0] + HALINE * side[1]
        sums_ref[0] = sums_ref[0] + density
        sums_ref[1] = sums_ref[1] + density_s
        sums_ref[2, 0:2] = sums_ref[2, 0:2] + density_w
        sums_ref[2, 2:4] = sums_ref[2, 2:4] + density_e
        scale = PRESSURE_SCALE / levels
        pressure = scale * sums_ref[0]
        pressure_s = scale * sums_ref[1]
        pressure_w = scale * sums_ref[2, 0:2]
        pressure_e = scale * sums_ref[2, 2:4]
        east_vel = masked[2]
        north_vel = masked[3]
        pm2, pm1, pp1, pp2, qm2, qm1, qp1, qp2 = near(pressure, pressure_w, pressure_e, pressure_s)
        extra = [None, None,
                 -fourth(pm2, pm1, pp1, pp2) + coriolis * north_vel,
                 -fourth(qm2, qm1, qp1, qp2) - coriolis * east_vel]
        for f in range(fields):
            xm2, xm1, xp1, xp2, ym2, ym1, yp1, yp2 = near(masked[f], west[f], east[f], side[f])
            lap = xp1 + xm1 + yp1 + ym1 - 4.0 * masked[f]
            tendency = -(east_vel * fourth(xm2, xm1, xp1, xp2) + north_vel * fourth(ym2, ym1, yp1, yp2)) + VISCOSITY * lap
            if extra[f] is not None:
                tendency = tendency + extra[f]
                forcing_ref[f - 2] = forcing_ref[f - 2] + active * tendency
            provisional_ref[f, k] = active * (masked[f] + STEP_TIME * tendency)
        return carry

    @pl.when(chunk == 0)
    def _():
        forcing_ref[...] = jnp.zeros_like(forcing_ref)

    lax.fori_loop(0, depth_levels, level, 0)

    @pl.when(chunk == pl.num_programs(0) - 1)
    def _():
        forcing_ref[...] = forcing_ref[...] / levels


def stencil(state, depth_class, west, east, side, coriolis):
    fields, levels, rows, cols = state.shape
    steps = levels // LEVEL_CHUNK
    big = pl.BlockSpec((fields, LEVEL_CHUNK, rows, cols), lambda c: (0, c, 0, 0))
    rim = pl.BlockSpec((fields, LEVEL_CHUNK, 2, cols), lambda c: (0, c, 0, 0))
    flat = pl.BlockSpec((rows, cols), lambda c: (0, 0))
    packed = pl.BlockSpec(side.shape, lambda c: (0, 0, 0, 0))
    return pl.pallas_call(
        stencil_kernel,
        grid=(steps,),
        out_shape=(jax.ShapeDtypeStruct(state.shape, jnp.float32),
                   jax.ShapeDtypeStruct((2, rows, cols), jnp.float32)),
        in_specs=[flat, pl.BlockSpec((1, cols), lambda c: (0, 0)), big, rim, rim, packed],
        out_specs=(big, pl.BlockSpec((2, rows, cols), lambda c: (0, 0, 0))),
        scratch_shapes=[pltpu.VMEM((3, rows, cols), jnp.float32)],
        compiler_params=pltpu.CompilerParams(dimension_semantics=("arbitrary",)),
        cost_estimate=pl.CostEstimate(
            flops=60 * state.size, transcendentals=0, bytes_accessed=4 * 2 * state.size
        ),
    )(depth_class, coriolis, state, west, east, side)


def pack_kernel(depth_ref, state_ref, out_ref, head_ref, tail_ref):
    block_index = pl.program_id(0)
    fields, depth_levels, rows, cols = state_ref.shape
    block = depth_levels * pl.num_programs(0) // 4
    lane = lax.broadcasted_iota(jnp.int32, (rows, cols), 1)
    reach = depth_ref[...] * block
    packed = [jnp.zeros((rows, cols), jnp.float32) for f in range(fields)]
    for k in range(depth_levels):
        active = (block_index * depth_levels + k < reach).astype(jnp.float32)
        low = 4 * k
        first = (lane == low) | (lane == low + 1)
        second = (lane == low + 2) | (lane == low + 3)
        for f in range(fields):
            masked = state_ref[f, k] * active
            head_ref[f, k] = masked[0:2]
            tail_ref[f, k] = masked[rows - 2 : rows]
            near_end = pltpu.roll(masked, low, 1)
            far_end = pltpu.roll(masked, (low + 4) % cols, 1)
            packed[f] = jnp.where(first, near_end, jnp.where(second, far_end, packed[f]))
    for f in range(fields):
        out_ref[f, 0] = packed[f]


def pack_edges(state, depth_class):
    fields, levels, rows, cols = state.shape
    rim = pl.BlockSpec((fields, PACK, 2, cols), lambda c: (0, c, 0, 0))
    return pl.pallas_call(
        pack_kernel,
        grid=(levels // PACK,),
        out_shape=(
            jax.ShapeDtypeStruct((fields, levels // PACK, rows, cols), jnp.float32),
            jax.ShapeDtypeStruct((fields, levels, 2, cols), jnp.float32),
            jax.ShapeDtypeStruct((fields, levels, 2, cols), jnp.float32),
        ),
        in_specs=[pl.BlockSpec((rows, cols), lambda c: (0, 0)),
                  pl.BlockSpec((fields, PACK, rows, cols), lambda c: (0, c, 0, 0))],
        out_specs=(pl.BlockSpec((fields, 1, rows, cols), lambda c: (0, c, 0, 0)), rim, rim),
        cost_estimate=pl.CostEstimate(
            flops=4 * state.size, transcendentals=0, bytes_accessed=4 * state.size
        ),
    )(depth_class, state)


def combine(from_south, from_north):
    lane = lax.broadcasted_iota(jnp.int32, from_south.shape, from_south.ndim - 1)
    return jnp.where(lane % 4 >= 2, from_south, from_north)


def wave_kernel(moving_ref, fixed_ref, coriolis_ref, height_ref, transport_ref, work_ref):
    rows, cols = moving_ref.shape[1], moving_ref.shape[2]
    inner_rows, inner_cols = height_ref.shape[0], height_ref.shape[1]
    rim = (rows - inner_rows) // 2
    groups = 4
    per_group = SUB // groups
    trim = 2 * per_group
    work_ref[...] = moving_ref[...]
    for group in range(groups):
        low = trim * group
        high = rows - trim * group
        span = high - low
        column_depth = fixed_ref[2, low:high]
        sea_mask = (column_depth > 0.0).astype(jnp.float32)
        force_east = fixed_ref[0, low:high]
        force_north = fixed_ref[1, low:high]
        coriolis = jnp.broadcast_to(coriolis_ref[0:1, :], (span, cols))

        def x_slope_rolled(values):
            return (pltpu.roll(values, span - 1, 0) - pltpu.roll(values, 1, 0)) * 0.5

        def y_slope_rolled(values):
            return (pltpu.roll(values, cols - 1, 1) - pltpu.roll(values, 1, 1)) * 0.5

        def step(index, carry):
            surface = work_ref[0, low:high]
            east_old = work_ref[1, low:high]
            north_old = work_ref[2, low:high]
            surface_mid = sea_mask * (
                surface - WAVE_STEP * (x_slope_rolled(east_old) + y_slope_rolled(north_old))
            )
            east_new = sea_mask * (
                east_old
                + WAVE_STEP
                * (
                    -GRAVITY * column_depth * x_slope_rolled(surface_mid)
                    + coriolis * north_old
                    + force_east
                    - BOTTOM_DRAG * east_old
                )
            )
            north_new = sea_mask * (
                north_old
                + WAVE_STEP
                * (
                    -GRAVITY * column_depth * y_slope_rolled(surface_mid)
                    - coriolis * east_new
                    + force_north
                    - BOTTOM_DRAG * north_old
                )
            )
            work_ref[0, low:high] = surface_mid
            work_ref[1, low:high] = east_new
            work_ref[2, low:high] = north_new
            return carry

        lax.fori_loop(0, per_group, step, 0)
    for field in range(3):
        middle = work_ref[field, rim : rim + inner_rows]
        inner = pltpu.roll(middle, cols - rim, 1)[:, :inner_cols]
        if field == 0:
            height_ref[...] = inner
        else:
            transport_ref[field - 1] = inner


def local_waves(moving, fixed, coriolis, inner_rows, inner_cols):
    rows, cols = moving.shape[1], moving.shape[2]
    elements = rows * cols
    return pl.pallas_call(
        wave_kernel,
        out_shape=(
            jax.ShapeDtypeStruct((inner_rows, inner_cols), jnp.float32),
            jax.ShapeDtypeStruct((2, inner_rows, inner_cols), jnp.float32),
        ),
        in_specs=[pl.BlockSpec(memory_space=pltpu.VMEM)] * 3,
        out_specs=(pl.BlockSpec(memory_space=pltpu.VMEM), pl.BlockSpec(memory_space=pltpu.VMEM)),
        scratch_shapes=[pltpu.VMEM(moving.shape, jnp.float32)],
        cost_estimate=pl.CostEstimate(
            flops=SUB * 30 * elements, transcendentals=0, bytes_accessed=4 * 7 * elements
        ),
    )(moving, fixed, coriolis)


def body(state, depth_class, vertical_inverse, height, transport):
    levels = state.shape[1]
    level_block = levels // vertical_inverse.shape[0]
    y_cells = depth_class.shape[1]
    level_ids = lax.broadcasted_iota(jnp.int32, (levels, 1, 1), 0)
    active = (level_ids < depth_class[None] * level_block).astype(jnp.float32)
    column_blocks = lax.axis_size(("gy", "mode"))
    anchor = lax.axis_index(("gy", "mode")) * y_cells
    coriolis = coriolis_row(anchor, y_cells, y_cells * column_blocks)
    edges, head, tail = pack_edges(state, depth_class)
    x_count = lax.axis_size("gx")
    west = lax.ppermute(tail, "gx", [(i, i + 1) for i in range(x_count - 1)])
    east = lax.ppermute(head, "gx", [(i + 1, i) for i in range(x_count - 1)])
    y_count = lax.axis_size(("gy", "mode"))
    from_south = lax.ppermute(edges, ("gy", "mode"), [(i, i + 1) for i in range(y_count - 1)])
    from_north = lax.ppermute(edges, ("gy", "mode"), [(i + 1, i) for i in range(y_count - 1)])
    side = combine(from_south, from_north)
    provisional, forcing = stencil(state, depth_class, west, east, side, coriolis)
    updated = vertical_solve(state, provisional, active, depth_class, vertical_inverse)
    column_depth = depth_class.astype(jnp.float32) * level_block / levels
    sea_mask = (depth_class > 0).astype(jnp.float32)
    moving = jnp.stack([height, transport[0], transport[1]]) * sea_mask
    fields = jnp.stack([moving[0], moving[1], moving[2], forcing[0], forcing[1], column_depth])
    rim = 2 * SUB
    fields = wide_halo(fields, "gx", 1, rim)
    fields = wide_halo(fields, ("gy", "mode"), 2, rim)
    coriolis_wide = coriolis_row(anchor - rim, y_cells + 2 * rim, y_cells * column_blocks)
    x_cells = depth_class.shape[0]
    height_next, transport_next = local_waves(fields[0:3], fields[3:6], coriolis_wide, x_cells, y_cells)
    state_next = finish(updated, transport_next, active, depth_class, level_block, levels)
    return (state_next, height_next, transport_next)


def solution(mesh):
    placed = (
        P(None, None, "gx", ("gy", "mode")),
        P("gx", ("gy", "mode")),
        P(),
        P("gx", ("gy", "mode")),
        P(None, "gx", ("gy", "mode")),
    )
    return jax.shard_map(
        body,
        mesh=mesh,
        in_specs=placed,
        out_specs=(
            P(None, None, "gx", ("gy", "mode")),
            P("gx", ("gy", "mode")),
            P(None, "gx", ("gy", "mode")),
        ),
        check_vma=False,
    )
```

```python
import jax
import numpy as np
import jax.numpy as jnp
from jax import lax
from jax.experimental import pallas as pl
from jax.experimental.pallas import tpu as pltpu
from jax.sharding import PartitionSpec as P

SUB = 32
LEVEL_CHUNK = 8
PACK = 32


THERMAL = 0.8
HALINE = 0.6
PRESSURE_SCALE = 4.0
VISCOSITY = 0.1
STEP_TIME = 0.05
WAVE_STEP = 0.5
GRAVITY = 1.0
BOTTOM_DRAG = 0.05
CORIOLIS_BASE = 0.3
CORIOLIS_SLOPE = 0.4


def coriolis_row(anchor, number, total):
    position = (anchor + lax.broadcasted_iota(jnp.int32, (number,), 0)).astype(jnp.float32)
    return (CORIOLIS_BASE + CORIOLIS_SLOPE * (position + 0.5) / total)[None, :]


def vertical_solve(state, provisional, active, depth_class, inverse):
    levels = state.shape[1]
    classes = inverse.shape[0]
    band = levels // classes
    rows_used = np.concatenate(
        [class_index * levels + np.arange(band * (class_index + 1)) for class_index in range(classes)]
    )
    stacked = jnp.take(inverse.reshape(classes * levels, inverse.shape[2]), rows_used, axis=0)
    every = jnp.einsum("kl,flxy->fkxy", stacked, provisional, precision=lax.Precision.HIGH)
    starts = [band * class_index * (class_index + 1) // 2 for class_index in range(classes)]
    chosen = [(depth_class == class_index + 1).astype(jnp.float32) for class_index in range(classes)]
    bands = []
    for level_band in range(classes):
        part = jnp.zeros_like(provisional[:, :band])
        for class_index in range(level_band, classes):
            first = starts[class_index] + level_band * band
            part = part + chosen[class_index] * every[:, first : first + band]
        bands.append(part)
    solved = jnp.concatenate(bands, axis=1)
    return active * solved + (1.0 - active) * state


def finish(updated, transport_next, active, depth_class, level_block, levels):
    counted = jnp.maximum(depth_class * level_block, 1).astype(jnp.float32)
    safe_depth = jnp.maximum(depth_class, 1).astype(jnp.float32) * level_block / levels
    column_means = jnp.sum(active * updated[2:4], axis=1) / counted
    carried = transport_next / safe_depth
    velocity = updated[2:4] + active * (carried - column_means)[:, None]
    return jnp.concatenate([updated[0:2], velocity], axis=0)


def wide_halo(cells, axis, dim, width):
    count = lax.axis_size(axis)
    size = cells.shape[dim]
    before, after = [], []
    remaining, hop = width, 1
    while remaining > 0:
        take = min(size, remaining)
        tail = lax.slice_in_dim(cells, size - take, size, axis=dim)
        head = lax.slice_in_dim(cells, 0, take, axis=dim)
        if hop < count:
            from_before = lax.ppermute(tail, axis, [(i, i + hop) for i in range(count - hop)])
            from_after = lax.ppermute(head, axis, [(i + hop, i) for i in range(count - hop)])
        else:
            from_before = jnp.zeros_like(tail)
            from_after = jnp.zeros_like(head)
        before.insert(0, from_before)
        after.append(from_after)
        remaining -= take
        hop += 1
    return jnp.concatenate(before + [cells] + after, axis=dim)


def stencil_kernel(depth_ref, coriolis_ref, state_ref, west_ref, east_ref, side_ref,
                   provisional_ref, forcing_ref, sums_ref):
    chunk = pl.program_id(0)
    fields, depth_levels, rows, cols = state_ref.shape
    levels = depth_levels * pl.num_programs(0)
    block = levels // 4

    @pl.when(chunk == 0)
    def _():
        sums_ref[...] = jnp.zeros_like(sums_ref)

    row = lax.broadcasted_iota(jnp.int32, (rows, cols), 0)
    lane = lax.broadcasted_iota(jnp.int32, (rows, cols), 1)
    reach = depth_ref[...] * block
    coriolis = coriolis_ref[0:1, :]

    def near(values, west, east, side):
        w0 = jnp.broadcast_to(west[0:1], (rows, cols))
        w1 = jnp.broadcast_to(west[1:2], (rows, cols))
        e0 = jnp.broadcast_to(east[0:1], (rows, cols))
        e1 = jnp.broadcast_to(east[1:2], (rows, cols))
        xm1 = jnp.where(row == 0, w1, pltpu.roll(values, 1, 0))
        xm2 = jnp.where(row == 0, w0, jnp.where(row == 1, w1, pltpu.roll(values, 2, 0)))
        xp1 = jnp.where(row == rows - 1, e0, pltpu.roll(values, rows - 1, 0))
        xp2 = jnp.where(row == rows - 2, e0, jnp.where(row == rows - 1, e1, pltpu.roll(values, rows - 2, 0)))
        ym1 = jnp.where(lane == 0, pltpu.roll(side, cols - 1, 1), pltpu.roll(values, 1, 1))
        ym2 = jnp.where(lane < 2, side, pltpu.roll(values, 2, 1))
        yp1 = jnp.where(lane == cols - 1, pltpu.roll(side, 1, 1), pltpu.roll(values, cols - 1, 1))
        yp2 = jnp.where(lane >= cols - 2, side, pltpu.roll(values, cols - 2, 1))
        return xm2, xm1, xp1, xp2, ym2, ym1, yp1, yp2

    def fourth(m2, m1, p1, p2):
        return (8.0 * (p1 - m1) - (p2 - m2)) * (1.0 / 12.0)

    def level(k, carry):
        global_level = chunk * depth_levels + k
        active = (global_level < reach).astype(jnp.float32)
        masked = [state_ref[f, k] * active for f in range(fields)]
        west = [west_ref[f, k] for f in range(fields)]
        east = [east_ref[f, k] for f in range(fields)]
        packed_level = global_level % PACK
        shift = (cols - 2 - 4 * packed_level) % cols
        side = [pltpu.roll(side_ref[f, global_level // PACK], shift, 1) for f in range(fields)]
        density = -THERMAL * masked[0] + HALINE * masked[1]
        density_w = -THERMAL * west[0] + HALINE * west[1]
        density_e = -THERMAL * east[0] + HALINE * east[1]
        density_s = -THERMAL * side[0] + HALINE * side[1]
        sums_ref[0] = sums_ref[0] + density
        sums_ref[1] = sums_ref[1] + density_s
        sums_ref[2, 0:2] = sums_ref[2, 0:2] + density_w
        sums_ref[2, 2:4] = sums_ref[2, 2:4] + density_e
        scale = PRESSURE_SCALE / levels
        pressure = scale * sums_ref[0]
        pressure_s = scale * sums_ref[1]
        pressure_w = scale * sums_ref[2, 0:2]
        pressure_e = scale * sums_ref[2, 2:4]
        east_vel = masked[2]
        north_vel = masked[3]
        pm2, pm1, pp1, pp2, qm2, qm1, qp1, qp2 = near(pressure, pressure_w, pressure_e, pressure_s)
        extra = [None, None,
                 -fourth(pm2, pm1, pp1, pp2) + coriolis * north_vel,
                 -fourth(qm2, qm1, qp1, qp2) - coriolis * east_vel]
        for f in range(fields):
            xm2, xm1, xp1, xp2, ym2, ym1, yp1, yp2 = near(masked[f], west[f], east[f], side[f])
            lap = xp1 + xm1 + yp1 + ym1 - 4.0 * masked[f]
            tendency = -(east_vel * fourth(xm2, xm1, xp1, xp2) + north_vel * fourth(ym2, ym1, yp1, yp2)) + VISCOSITY * lap
            if extra[f] is not None:
                tendency = tendency + extra[f]
                forcing_ref[f - 2] = forcing_ref[f - 2] + active * tendency
            provisional_ref[f, k] = active * (masked[f] + STEP_TIME * tendency)
        return carry

    @pl.when(chunk == 0)
    def _():
        forcing_ref[...] = jnp.zeros_like(forcing_ref)

    lax.fori_loop(0, depth_levels, level, 0)

    @pl.when(chunk == pl.num_programs(0) - 1)
    def _():
        forcing_ref[...] = forcing_ref[...] / levels


def stencil(state, depth_class, west, east, side, coriolis):
    fields, levels, rows, cols = state.shape
    steps = levels // LEVEL_CHUNK
    big = pl.BlockSpec((fields, LEVEL_CHUNK, rows, cols), lambda c: (0, c, 0, 0))
    rim = pl.BlockSpec((fields, LEVEL_CHUNK, 2, cols), lambda c: (0, c, 0, 0))
    flat = pl.BlockSpec((rows, cols), lambda c: (0, 0))
    packed = pl.BlockSpec(side.shape, lambda c: (0, 0, 0, 0))
    return pl.pallas_call(
        stencil_kernel,
        grid=(steps,),
        out_shape=(jax.ShapeDtypeStruct(state.shape, jnp.float32),
                   jax.ShapeDtypeStruct((2, rows, cols), jnp.float32)),
        in_specs=[flat, pl.BlockSpec((1, cols), lambda c: (0, 0)), big, rim, rim, packed],
        out_specs=(big, pl.BlockSpec((2, rows, cols), lambda c: (0, 0, 0))),
        scratch_shapes=[pltpu.VMEM((3, rows, cols), jnp.float32)],
        compiler_params=pltpu.CompilerParams(dimension_semantics=("arbitrary",)),
        cost_estimate=pl.CostEstimate(
            flops=60 * state.size, transcendentals=0, bytes_accessed=4 * 2 * state.size
        ),
    )(depth_class, coriolis, state, west, east, side)


def pack_kernel(depth_ref, state_ref, after_ref, out_ref):
    block_index = pl.program_id(0)
    fields, depth_levels, rows, cols = state_ref.shape
    block = depth_levels * pl.num_programs(0) // 4
    lane = lax.broadcasted_iota(jnp.int32, (rows, cols), 1)
    reach = depth_ref[...] * block
    packed = [jnp.zeros((rows, cols), jnp.float32) for f in range(fields)]
    for k in range(depth_levels):
        active = (block_index * depth_levels + k < reach).astype(jnp.float32)
        low = 4 * k
        first = (lane == low) | (lane == low + 1)
        second = (lane == low + 2) | (lane == low + 3)
        for f in range(fields):
            masked = state_ref[f, k] * active
            near_end = pltpu.roll(masked, low, 1)
            far_end = pltpu.roll(masked, (low + 4) % cols, 1)
            packed[f] = jnp.where(first, near_end, jnp.where(second, far_end, packed[f]))
    for f in range(fields):
        out_ref[f, 0] = packed[f]


def pack_edges(state, depth_class, after):
    fields, levels, rows, cols = state.shape
    return pl.pallas_call(
        pack_kernel,
        grid=(levels // PACK,),
        out_shape=jax.ShapeDtypeStruct((fields, levels // PACK, rows, cols), jnp.float32),
        in_specs=[pl.BlockSpec((rows, cols), lambda c: (0, 0)),
                  pl.BlockSpec((fields, PACK, rows, cols), lambda c: (0, c, 0, 0)),
                  pl.BlockSpec(memory_space=pl.ANY)],
        out_specs=pl.BlockSpec((fields, 1, rows, cols), lambda c: (0, c, 0, 0)),
        cost_estimate=pl.CostEstimate(
            flops=4 * state.size, transcendentals=0, bytes_accessed=4 * state.size
        ),
    )(depth_class, state, after)


def rim_kernel(depth_top_ref, depth_bottom_ref, top_ref, bottom_ref, head_ref, tail_ref):
    fields, levels = top_ref.shape[0], top_ref.shape[1]
    block = levels // 4
    reach_top = depth_top_ref[0:2] * block
    reach_bottom = depth_bottom_ref[6:8] * block

    def level(k, carry):
        for f in range(fields):
            head_ref[f, k] = top_ref[f, k, 0:2] * (k < reach_top).astype(jnp.float32)
            tail_ref[f, k] = bottom_ref[f, k, 6:8] * (k < reach_bottom).astype(jnp.float32)
        return carry

    lax.fori_loop(0, levels, level, 0)


def rim_rows(state, depth_class):
    fields, levels, rows, cols = state.shape
    last = rows // 8 - 1
    return pl.pallas_call(
        rim_kernel,
        out_shape=(
            jax.ShapeDtypeStruct((fields, levels, 2, cols), jnp.float32),
            jax.ShapeDtypeStruct((fields, levels, 2, cols), jnp.float32),
        ),
        grid=(1,),
        in_specs=[
            pl.BlockSpec((8, cols), lambda i: (0, 0)),
            pl.BlockSpec((8, cols), lambda i: (last, 0)),
            pl.BlockSpec((fields, levels, 8, cols), lambda i: (0, 0, 0, 0)),
            pl.BlockSpec((fields, levels, 8, cols), lambda i: (0, 0, last, 0)),
        ],
        out_specs=(
            pl.BlockSpec((fields, levels, 2, cols), lambda i: (0, 0, 0, 0)),
            pl.BlockSpec((fields, levels, 2, cols), lambda i: (0, 0, 0, 0)),
        ),
        cost_estimate=pl.CostEstimate(
            flops=fields * levels * 4 * cols, transcendentals=0,
            bytes_accessed=4 * fields * levels * 20 * cols,
        ),
    )(depth_class, depth_class, state, state)


def combine(from_south, from_north):
    lane = lax.broadcasted_iota(jnp.int32, from_south.shape, from_south.ndim - 1)
    return jnp.where(lane % 4 >= 2, from_south, from_north)


def wave_kernel(moving_ref, fixed_ref, coriolis_ref, height_ref, transport_ref, work_ref):
    rows, cols = moving_ref.shape[1], moving_ref.shape[2]
    inner_rows, inner_cols = height_ref.shape[0], height_ref.shape[1]
    rim = (rows - inner_rows) // 2
    groups = 4
    per_group = SUB // groups
    trim = 2 * per_group
    work_ref[...] = moving_ref[...]
    for group in range(groups):
        low = trim * group
        high = rows - trim * group
        span = high - low
        column_depth = fixed_ref[2, low:high]
        sea_mask = (column_depth > 0.0).astype(jnp.float32)
        force_east = fixed_ref[0, low:high]
        force_north = fixed_ref[1, low:high]
        coriolis = jnp.broadcast_to(coriolis_ref[0:1, :], (span, cols))

        def x_slope_rolled(values):
            return (pltpu.roll(values, span - 1, 0) - pltpu.roll(values, 1, 0)) * 0.5

        def y_slope_rolled(values):
            return (pltpu.roll(values, cols - 1, 1) - pltpu.roll(values, 1, 1)) * 0.5

        def step(index, carry):
            surface = work_ref[0, low:high]
            east_old = work_ref[1, low:high]
            north_old = work_ref[2, low:high]
            surface_mid = sea_mask * (
                surface - WAVE_STEP * (x_slope_rolled(east_old) + y_slope_rolled(north_old))
            )
            east_new = sea_mask * (
                east_old
                + WAVE_STEP
                * (
                    -GRAVITY * column_depth * x_slope_rolled(surface_mid)
                    + coriolis * north_old
                    + force_east
                    - BOTTOM_DRAG * east_old
                )
            )
            north_new = sea_mask * (
                north_old
                + WAVE_STEP
                * (
                    -GRAVITY * column_depth * y_slope_rolled(surface_mid)
                    - coriolis * east_new
                    + force_north
                    - BOTTOM_DRAG * north_old
                )
            )
            work_ref[0, low:high] = surface_mid
            work_ref[1, low:high] = east_new
            work_ref[2, low:high] = north_new
            return carry

        lax.fori_loop(0, per_group, step, 0)
    for field in range(3):
        middle = work_ref[field, rim : rim + inner_rows]
        inner = pltpu.roll(middle, cols - rim, 1)[:, :inner_cols]
        if field == 0:
            height_ref[...] = inner
        else:
            transport_ref[field - 1] = inner


def local_waves(moving, fixed, coriolis, inner_rows, inner_cols):
    rows, cols = moving.shape[1], moving.shape[2]
    elements = rows * cols
    return pl.pallas_call(
        wave_kernel,
        out_shape=(
            jax.ShapeDtypeStruct((inner_rows, inner_cols), jnp.float32),
            jax.ShapeDtypeStruct((2, inner_rows, inner_cols), jnp.float32),
        ),
        in_specs=[pl.BlockSpec(memory_space=pltpu.VMEM)] * 3,
        out_specs=(pl.BlockSpec(memory_space=pltpu.VMEM), pl.BlockSpec(memory_space=pltpu.VMEM)),
        scratch_shapes=[pltpu.VMEM(moving.shape, jnp.float32)],
        cost_estimate=pl.CostEstimate(
            flops=SUB * 30 * elements, transcendentals=0, bytes_accessed=4 * 7 * elements
        ),
    )(moving, fixed, coriolis)


def body(state, depth_class, vertical_inverse, height, transport):
    levels = state.shape[1]
    level_block = levels // vertical_inverse.shape[0]
    y_cells = depth_class.shape[1]
    level_ids = lax.broadcasted_iota(jnp.int32, (levels, 1, 1), 0)
    active = (level_ids < depth_class[None] * level_block).astype(jnp.float32)
    column_blocks = lax.axis_size(("gy", "mode"))
    anchor = lax.axis_index(("gy", "mode")) * y_cells
    coriolis = coriolis_row(anchor, y_cells, y_cells * column_blocks)
    head, tail = rim_rows(state, depth_class)
    x_count = lax.axis_size("gx")
    west = lax.ppermute(tail, "gx", [(i, i + 1) for i in range(x_count - 1)])
    east = lax.ppermute(head, "gx", [(i + 1, i) for i in range(x_count - 1)])
    edges = pack_edges(state, depth_class, head)
    y_count = lax.axis_size(("gy", "mode"))
    from_south = lax.ppermute(edges, ("gy", "mode"), [(i, i + 1) for i in range(y_count - 1)])
    from_north = lax.ppermute(edges, ("gy", "mode"), [(i + 1, i) for i in range(y_count - 1)])
    side = combine(from_south, from_north)
    provisional, forcing = stencil(state, depth_class, west, east, side, coriolis)
    updated = vertical_solve(state, provisional, active, depth_class, vertical_inverse)
    column_depth = depth_class.astype(jnp.float32) * level_block / levels
    sea_mask = (depth_class > 0).astype(jnp.float32)
    moving = jnp.stack([height, transport[0], transport[1]]) * sea_mask
    fields = jnp.stack([moving[0], moving[1], moving[2], forcing[0], forcing[1], column_depth])
    rim = 2 * SUB
    fields = wide_halo(fields, "gx", 1, rim)
    fields = wide_halo(fields, ("gy", "mode"), 2, rim)
    coriolis_wide = coriolis_row(anchor - rim, y_cells + 2 * rim, y_cells * column_blocks)
    x_cells = depth_class.shape[0]
    height_next, transport_next = local_waves(fields[0:3], fields[3:6], coriolis_wide, x_cells, y_cells)
    state_next = finish(updated, transport_next, active, depth_class, level_block, levels)
    return (state_next, height_next, transport_next)


def solution(mesh):
    placed = (
        P(None, None, "gx", ("gy", "mode")),
        P("gx", ("gy", "mode")),
        P(),
        P("gx", ("gy", "mode")),
        P(None, "gx", ("gy", "mode")),
    )
    return jax.shard_map(
        body,
        mesh=mesh,
        in_specs=placed,
        out_specs=(
            P(None, None, "gx", ("gy", "mode")),
            P("gx", ("gy", "mode")),
            P(None, "gx", ("gy", "mode")),
        ),
        check_vma=False,
    )
```

```python
import jax
import numpy as np
import jax.numpy as jnp
from jax import lax
from jax.experimental import pallas as pl
from jax.experimental.pallas import tpu as pltpu
from jax.sharding import PartitionSpec as P

SUB = 32
LEVEL_CHUNK = 16
PACK = 32


THERMAL = 0.8
HALINE = 0.6
PRESSURE_SCALE = 4.0
VISCOSITY = 0.1
STEP_TIME = 0.05
WAVE_STEP = 0.5
GRAVITY = 1.0
BOTTOM_DRAG = 0.05
CORIOLIS_BASE = 0.3
CORIOLIS_SLOPE = 0.4


def coriolis_row(anchor, number, total):
    position = (anchor + lax.broadcasted_iota(jnp.int32, (number,), 0)).astype(jnp.float32)
    return (CORIOLIS_BASE + CORIOLIS_SLOPE * (position + 0.5) / total)[None, :]


def vertical_solve(state, provisional, active, depth_class, inverse):
    levels = state.shape[1]
    classes = inverse.shape[0]
    band = levels // classes
    rows_used = np.concatenate(
        [class_index * levels + np.arange(band * (class_index + 1)) for class_index in range(classes)]
    )
    stacked = jnp.take(inverse.reshape(classes * levels, inverse.shape[2]), rows_used, axis=0)
    every = jnp.einsum("kl,flxy->fkxy", stacked, provisional, precision=lax.Precision.HIGH)
    starts = [band * class_index * (class_index + 1) // 2 for class_index in range(classes)]
    chosen = [(depth_class == class_index + 1).astype(jnp.float32) for class_index in range(classes)]
    bands = []
    for level_band in range(classes):
        part = jnp.zeros_like(provisional[:, :band])
        for class_index in range(level_band, classes):
            first = starts[class_index] + level_band * band
            part = part + chosen[class_index] * every[:, first : first + band]
        bands.append(part)
    solved = jnp.concatenate(bands, axis=1)
    return active * solved + (1.0 - active) * state


def finish(updated, transport_next, active, depth_class, level_block, levels):
    counted = jnp.maximum(depth_class * level_block, 1).astype(jnp.float32)
    safe_depth = jnp.maximum(depth_class, 1).astype(jnp.float32) * level_block / levels
    column_means = jnp.sum(active * updated[2:4], axis=1) / counted
    carried = transport_next / safe_depth
    velocity = updated[2:4] + active * (carried - column_means)[:, None]
    return jnp.concatenate([updated[0:2], velocity], axis=0)


def wide_halo(cells, axis, dim, width):
    count = lax.axis_size(axis)
    size = cells.shape[dim]
    before, after = [], []
    remaining, hop = width, 1
    while remaining > 0:
        take = min(size, remaining)
        tail = lax.slice_in_dim(cells, size - take, size, axis=dim)
        head = lax.slice_in_dim(cells, 0, take, axis=dim)
        if hop < count:
            from_before = lax.ppermute(tail, axis, [(i, i + hop) for i in range(count - hop)])
            from_after = lax.ppermute(head, axis, [(i + hop, i) for i in range(count - hop)])
        else:
            from_before = jnp.zeros_like(tail)
            from_after = jnp.zeros_like(head)
        before.insert(0, from_before)
        after.append(from_after)
        remaining -= take
        hop += 1
    return jnp.concatenate(before + [cells] + after, axis=dim)


def stencil_kernel(depth_ref, coriolis_ref, state_ref, west_ref, east_ref, side_ref,
                   provisional_ref, forcing_ref, sums_ref):
    chunk = pl.program_id(0)
    fields, depth_levels, rows, cols = state_ref.shape
    levels = depth_levels * pl.num_programs(0)
    block = levels // 4

    @pl.when(chunk == 0)
    def _():
        sums_ref[...] = jnp.zeros_like(sums_ref)

    row = lax.broadcasted_iota(jnp.int32, (rows, cols), 0)
    lane = lax.broadcasted_iota(jnp.int32, (rows, cols), 1)
    reach = depth_ref[...] * block
    coriolis = coriolis_ref[0:1, :]

    def near(values, west, east, side):
        w0 = jnp.broadcast_to(west[0:1], (rows, cols))
        w1 = jnp.broadcast_to(west[1:2], (rows, cols))
        e0 = jnp.broadcast_to(east[0:1], (rows, cols))
        e1 = jnp.broadcast_to(east[1:2], (rows, cols))
        xm1 = jnp.where(row == 0, w1, pltpu.roll(values, 1, 0))
        xm2 = jnp.where(row == 0, w0, jnp.where(row == 1, w1, pltpu.roll(values, 2, 0)))
        xp1 = jnp.where(row == rows - 1, e0, pltpu.roll(values, rows - 1, 0))
        xp2 = jnp.where(row == rows - 2, e0, jnp.where(row == rows - 1, e1, pltpu.roll(values, rows - 2, 0)))
        ym1 = jnp.where(lane == 0, pltpu.roll(side, cols - 1, 1), pltpu.roll(values, 1, 1))
        ym2 = jnp.where(lane < 2, side, pltpu.roll(values, 2, 1))
        yp1 = jnp.where(lane == cols - 1, pltpu.roll(side, 1, 1), pltpu.roll(values, cols - 1, 1))
        yp2 = jnp.where(lane >= cols - 2, side, pltpu.roll(values, cols - 2, 1))
        return xm2, xm1, xp1, xp2, ym2, ym1, yp1, yp2

    def fourth(m2, m1, p1, p2):
        return (8.0 * (p1 - m1) - (p2 - m2)) * (1.0 / 12.0)

    def level(k, carry):
        global_level = chunk * depth_levels + k
        active = (global_level < reach).astype(jnp.float32)
        masked = [state_ref[f, k] * active for f in range(fields)]
        west = [west_ref[f, k] for f in range(fields)]
        east = [east_ref[f, k] for f in range(fields)]
        packed_level = global_level % PACK
        shift = (cols - 2 - 4 * packed_level) % cols
        side = [pltpu.roll(side_ref[f, global_level // PACK], shift, 1) for f in range(fields)]
        density = -THERMAL * masked[0] + HALINE * masked[1]
        density_w = -THERMAL * west[0] + HALINE * west[1]
        density_e = -THERMAL * east[0] + HALINE * east[1]
        density_s = -THERMAL * side[0] + HALINE * side[1]
        sums_ref[0] = sums_ref[0] + density
        sums_ref[1] = sums_ref[1] + density_s
        sums_ref[2, 0:2] = sums_ref[2, 0:2] + density_w
        sums_ref[2, 2:4] = sums_ref[2, 2:4] + density_e
        scale = PRESSURE_SCALE / levels
        pressure = scale * sums_ref[0]
        pressure_s = scale * sums_ref[1]
        pressure_w = scale * sums_ref[2, 0:2]
        pressure_e = scale * sums_ref[2, 2:4]
        east_vel = masked[2]
        north_vel = masked[3]
        pm2, pm1, pp1, pp2, qm2, qm1, qp1, qp2 = near(pressure, pressure_w, pressure_e, pressure_s)
        extra = [None, None,
                 -fourth(pm2, pm1, pp1, pp2) + coriolis * north_vel,
                 -fourth(qm2, qm1, qp1, qp2) - coriolis * east_vel]
        for f in range(fields):
            xm2, xm1, xp1, xp2, ym2, ym1, yp1, yp2 = near(masked[f], west[f], east[f], side[f])
            lap = xp1 + xm1 + yp1 + ym1 - 4.0 * masked[f]
            tendency = -(east_vel * fourth(xm2, xm1, xp1, xp2) + north_vel * fourth(ym2, ym1, yp1, yp2)) + VISCOSITY * lap
            if extra[f] is not None:
                tendency = tendency + extra[f]
                forcing_ref[f - 2] = forcing_ref[f - 2] + active * tendency
            provisional_ref[f, k] = active * (masked[f] + STEP_TIME * tendency)
        return carry

    @pl.when(chunk == 0)
    def _():
        forcing_ref[...] = jnp.zeros_like(forcing_ref)

    lax.fori_loop(0, depth_levels, level, 0)

    @pl.when(chunk == pl.num_programs(0) - 1)
    def _():
        forcing_ref[...] = forcing_ref[...] / levels


def stencil(state, depth_class, west, east, side, coriolis):
    fields, levels, rows, cols = state.shape
    steps = levels // LEVEL_CHUNK
    big = pl.BlockSpec((fields, LEVEL_CHUNK, rows, cols), lambda c: (0, c, 0, 0))
    rim = pl.BlockSpec((fields, LEVEL_CHUNK, 2, cols), lambda c: (0, c, 0, 0))
    flat = pl.BlockSpec((rows, cols), lambda c: (0, 0))
    packed = pl.BlockSpec(side.shape, lambda c: (0, 0, 0, 0))
    return pl.pallas_call(
        stencil_kernel,
        grid=(steps,),
        out_shape=(jax.ShapeDtypeStruct(state.shape, jnp.float32),
                   jax.ShapeDtypeStruct((2, rows, cols), jnp.float32)),
        in_specs=[flat, pl.BlockSpec((1, cols), lambda c: (0, 0)), big, rim, rim, packed],
        out_specs=(big, pl.BlockSpec((2, rows, cols), lambda c: (0, 0, 0))),
        scratch_shapes=[pltpu.VMEM((3, rows, cols), jnp.float32)],
        compiler_params=pltpu.CompilerParams(dimension_semantics=("arbitrary",)),
        cost_estimate=pl.CostEstimate(
            flops=60 * state.size, transcendentals=0, bytes_accessed=4 * 2 * state.size
        ),
    )(depth_class, coriolis, state, west, east, side)


def pack_kernel(depth_ref, state_ref, out_ref, head_ref, tail_ref):
    block_index = pl.program_id(0)
    fields, depth_levels, rows, cols = state_ref.shape
    block = depth_levels * pl.num_programs(0) // 4
    lane = lax.broadcasted_iota(jnp.int32, (rows, cols), 1)
    reach = depth_ref[...] * block
    packed = [jnp.zeros((rows, cols), jnp.float32) for f in range(fields)]
    for k in range(depth_levels):
        active = (block_index * depth_levels + k < reach).astype(jnp.float32)
        low = 4 * k
        first = (lane == low) | (lane == low + 1)
        second = (lane == low + 2) | (lane == low + 3)
        for f in range(fields):
            masked = state_ref[f, k] * active
            head_ref[f, k] = masked[0:2]
            tail_ref[f, k] = masked[rows - 2 : rows]
            near_end = pltpu.roll(masked, low, 1)
            far_end = pltpu.roll(masked, (low + 4) % cols, 1)
            packed[f] = jnp.where(first, near_end, jnp.where(second, far_end, packed[f]))
    for f in range(fields):
        out_ref[f, 0] = packed[f]


def pack_edges(state, depth_class):
    fields, levels, rows, cols = state.shape
    rim = pl.BlockSpec((fields, PACK, 2, cols), lambda c: (0, c, 0, 0))
    return pl.pallas_call(
        pack_kernel,
        grid=(levels // PACK,),
        out_shape=(
            jax.ShapeDtypeStruct((fields, levels // PACK, rows, cols), jnp.float32),
            jax.ShapeDtypeStruct((fields, levels, 2, cols), jnp.float32),
            jax.ShapeDtypeStruct((fields, levels, 2, cols), jnp.float32),
        ),
        in_specs=[pl.BlockSpec((rows, cols), lambda c: (0, 0)),
                  pl.BlockSpec((fields, PACK, rows, cols), lambda c: (0, c, 0, 0))],
        out_specs=(pl.BlockSpec((fields, 1, rows, cols), lambda c: (0, c, 0, 0)), rim, rim),
        cost_estimate=pl.CostEstimate(
            flops=4 * state.size, transcendentals=0, bytes_accessed=4 * state.size
        ),
    )(depth_class, state)


def combine(from_south, from_north):
    lane = lax.broadcasted_iota(jnp.int32, from_south.shape, from_south.ndim - 1)
    return jnp.where(lane % 4 >= 2, from_south, from_north)


def wave_kernel(moving_ref, fixed_ref, coriolis_ref, height_ref, transport_ref, work_ref):
    rows, cols = moving_ref.shape[1], moving_ref.shape[2]
    inner_rows, inner_cols = height_ref.shape[0], height_ref.shape[1]
    rim = (rows - inner_rows) // 2
    groups = 8
    per_group = SUB // groups
    trim = 2 * per_group
    work_ref[...] = moving_ref[...]
    for group in range(groups):
        low = trim * group
        high = rows - trim * group
        span = high - low
        column_depth = fixed_ref[2, low:high]
        sea_mask = (column_depth > 0.0).astype(jnp.float32)
        force_east = fixed_ref[0, low:high]
        force_north = fixed_ref[1, low:high]
        coriolis = jnp.broadcast_to(coriolis_ref[0:1, :], (span, cols))

        def x_slope_rolled(values):
            return (pltpu.roll(values, span - 1, 0) - pltpu.roll(values, 1, 0)) * 0.5

        def y_slope_rolled(values):
            return (pltpu.roll(values, cols - 1, 1) - pltpu.roll(values, 1, 1)) * 0.5

        def step(index, carry):
            surface = work_ref[0, low:high]
            east_old = work_ref[1, low:high]
            north_old = work_ref[2, low:high]
            surface_mid = sea_mask * (
                surface - WAVE_STEP * (x_slope_rolled(east_old) + y_slope_rolled(north_old))
            )
            east_new = sea_mask * (
                east_old
                + WAVE_STEP
                * (
                    -GRAVITY * column_depth * x_slope_rolled(surface_mid)
                    + coriolis * north_old
                    + force_east
                    - BOTTOM_DRAG * east_old
                )
            )
            north_new = sea_mask * (
                north_old
                + WAVE_STEP
                * (
                    -GRAVITY * column_depth * y_slope_rolled(surface_mid)
                    - coriolis * east_new
                    + force_north
                    - BOTTOM_DRAG * north_old
                )
            )
            work_ref[0, low:high] = surface_mid
            work_ref[1, low:high] = east_new
            work_ref[2, low:high] = north_new
            return carry

        lax.fori_loop(0, per_group, step, 0)
    for field in range(3):
        middle = work_ref[field, rim : rim + inner_rows]
        inner = pltpu.roll(middle, cols - rim, 1)[:, :inner_cols]
        if field == 0:
            height_ref[...] = inner
        else:
            transport_ref[field - 1] = inner


def local_waves(moving, fixed, coriolis, inner_rows, inner_cols):
    rows, cols = moving.shape[1], moving.shape[2]
    elements = rows * cols
    return pl.pallas_call(
        wave_kernel,
        out_shape=(
            jax.ShapeDtypeStruct((inner_rows, inner_cols), jnp.float32),
            jax.ShapeDtypeStruct((2, inner_rows, inner_cols), jnp.float32),
        ),
        in_specs=[pl.BlockSpec(memory_space=pltpu.VMEM)] * 3,
        out_specs=(pl.BlockSpec(memory_space=pltpu.VMEM), pl.BlockSpec(memory_space=pltpu.VMEM)),
        scratch_shapes=[pltpu.VMEM(moving.shape, jnp.float32)],
        cost_estimate=pl.CostEstimate(
            flops=SUB * 30 * elements, transcendentals=0, bytes_accessed=4 * 7 * elements
        ),
    )(moving, fixed, coriolis)


def body(state, depth_class, vertical_inverse, height, transport):
    levels = state.shape[1]
    level_block = levels // vertical_inverse.shape[0]
    y_cells = depth_class.shape[1]
    level_ids = lax.broadcasted_iota(jnp.int32, (levels, 1, 1), 0)
    active = (level_ids < depth_class[None] * level_block).astype(jnp.float32)
    column_blocks = lax.axis_size(("gy", "mode"))
    anchor = lax.axis_index(("gy", "mode")) * y_cells
    coriolis = coriolis_row(anchor, y_cells, y_cells * column_blocks)
    edges, head, tail = pack_edges(state, depth_class)
    x_count = lax.axis_size("gx")
    west = lax.ppermute(tail, "gx", [(i, i + 1) for i in range(x_count - 1)])
    east = lax.ppermute(head, "gx", [(i + 1, i) for i in range(x_count - 1)])
    y_count = lax.axis_size(("gy", "mode"))
    from_south = lax.ppermute(edges, ("gy", "mode"), [(i, i + 1) for i in range(y_count - 1)])
    from_north = lax.ppermute(edges, ("gy", "mode"), [(i + 1, i) for i in range(y_count - 1)])
    side = combine(from_south, from_north)
    provisional, forcing = stencil(state, depth_class, west, east, side, coriolis)
    updated = vertical_solve(state, provisional, active, depth_class, vertical_inverse)
    column_depth = depth_class.astype(jnp.float32) * level_block / levels
    sea_mask = (depth_class > 0).astype(jnp.float32)
    moving = jnp.stack([height, transport[0], transport[1]]) * sea_mask
    fields = jnp.stack([moving[0], moving[1], moving[2], forcing[0], forcing[1], column_depth])
    rim = 2 * SUB
    fields = wide_halo(fields, "gx", 1, rim)
    fields = wide_halo(fields, ("gy", "mode"), 2, rim)
    coriolis_wide = coriolis_row(anchor - rim, y_cells + 2 * rim, y_cells * column_blocks)
    x_cells = depth_class.shape[0]
    height_next, transport_next = local_waves(fields[0:3], fields[3:6], coriolis_wide, x_cells, y_cells)
    state_next = finish(updated, transport_next, active, depth_class, level_block, levels)
    return (state_next, height_next, transport_next)


def solution(mesh):
    placed = (
        P(None, None, "gx", ("gy", "mode")),
        P("gx", ("gy", "mode")),
        P(),
        P("gx", ("gy", "mode")),
        P(None, "gx", ("gy", "mode")),
    )
    return jax.shard_map(
        body,
        mesh=mesh,
        in_specs=placed,
        out_specs=(
            P(None, None, "gx", ("gy", "mode")),
            P("gx", ("gy", "mode")),
            P(None, "gx", ("gy", "mode")),
        ),
        check_vma=False,
    )
```

```python
import jax
import numpy as np
import jax.numpy as jnp
from jax import lax
from jax.experimental import pallas as pl
from jax.experimental.pallas import tpu as pltpu
from jax.sharding import PartitionSpec as P

SUB = 32
LEVEL_CHUNK = 16
PACK = 32


THERMAL = 0.8
HALINE = 0.6
PRESSURE_SCALE = 4.0
VISCOSITY = 0.1
STEP_TIME = 0.05
WAVE_STEP = 0.5
GRAVITY = 1.0
BOTTOM_DRAG = 0.05
CORIOLIS_BASE = 0.3
CORIOLIS_SLOPE = 0.4


def coriolis_row(anchor, number, total):
    position = (anchor + lax.broadcasted_iota(jnp.int32, (number,), 0)).astype(jnp.float32)
    return (CORIOLIS_BASE + CORIOLIS_SLOPE * (position + 0.5) / total)[None, :]


def vertical_solve(state, provisional, active, depth_class, inverse):
    levels = state.shape[1]
    classes = inverse.shape[0]
    band = levels // classes
    rows_used = np.concatenate(
        [class_index * levels + np.arange(band * (class_index + 1)) for class_index in range(classes)]
    )
    stacked = jnp.take(inverse.reshape(classes * levels, inverse.shape[2]), rows_used, axis=0)
    every = jnp.einsum("kl,flxy->fkxy", stacked, provisional, precision=lax.Precision.HIGH)
    starts = [band * class_index * (class_index + 1) // 2 for class_index in range(classes)]
    chosen = [(depth_class == class_index + 1).astype(jnp.float32) for class_index in range(classes)]
    bands = []
    for level_band in range(classes):
        part = jnp.zeros_like(provisional[:, :band])
        for class_index in range(level_band, classes):
            first = starts[class_index] + level_band * band
            part = part + chosen[class_index] * every[:, first : first + band]
        bands.append(part)
    solved = jnp.concatenate(bands, axis=1)
    return active * solved + (1.0 - active) * state


def finish(updated, transport_next, active, depth_class, level_block, levels):
    counted = jnp.maximum(depth_class * level_block, 1).astype(jnp.float32)
    safe_depth = jnp.maximum(depth_class, 1).astype(jnp.float32) * level_block / levels
    column_means = jnp.sum(active * updated[2:4], axis=1) / counted
    carried = transport_next / safe_depth
    velocity = updated[2:4] + active * (carried - column_means)[:, None]
    return jnp.concatenate([updated[0:2], velocity], axis=0)


def wide_halo(cells, axis, dim, width):
    count = lax.axis_size(axis)
    size = cells.shape[dim]
    before, after = [], []
    remaining, hop = width, 1
    while remaining > 0:
        take = min(size, remaining)
        tail = lax.slice_in_dim(cells, size - take, size, axis=dim)
        head = lax.slice_in_dim(cells, 0, take, axis=dim)
        if hop < count:
            from_before = lax.ppermute(tail, axis, [(i, i + hop) for i in range(count - hop)])
            from_after = lax.ppermute(head, axis, [(i + hop, i) for i in range(count - hop)])
        else:
            from_before = jnp.zeros_like(tail)
            from_after = jnp.zeros_like(head)
        before.insert(0, from_before)
        after.append(from_after)
        remaining -= take
        hop += 1
    return jnp.concatenate(before + [cells] + after, axis=dim)


def stencil_kernel(depth_ref, coriolis_ref, state_ref, west_ref, east_ref, side_ref,
                   provisional_ref, forcing_ref, sums_ref):
    chunk = pl.program_id(0)
    fields, depth_levels, rows, cols = state_ref.shape
    levels = depth_levels * pl.num_programs(0)
    block = levels // 4

    @pl.when(chunk == 0)
    def _():
        sums_ref[...] = jnp.zeros_like(sums_ref)

    row = lax.broadcasted_iota(jnp.int32, (rows, cols), 0)
    lane = lax.broadcasted_iota(jnp.int32, (rows, cols), 1)
    reach = depth_ref[...] * block
    coriolis = coriolis_ref[0:1, :]

    def near(values, west, east, side):
        w0 = jnp.broadcast_to(west[0:1], (rows, cols))
        w1 = jnp.broadcast_to(west[1:2], (rows, cols))
        e0 = jnp.broadcast_to(east[0:1], (rows, cols))
        e1 = jnp.broadcast_to(east[1:2], (rows, cols))
        xm1 = jnp.where(row == 0, w1, pltpu.roll(values, 1, 0))
        xm2 = jnp.where(row == 0, w0, jnp.where(row == 1, w1, pltpu.roll(values, 2, 0)))
        xp1 = jnp.where(row == rows - 1, e0, pltpu.roll(values, rows - 1, 0))
        xp2 = jnp.where(row == rows - 2, e0, jnp.where(row == rows - 1, e1, pltpu.roll(values, rows - 2, 0)))
        ym1 = jnp.where(lane == 0, pltpu.roll(side, cols - 1, 1), pltpu.roll(values, 1, 1))
        ym2 = jnp.where(lane < 2, side, pltpu.roll(values, 2, 1))
        yp1 = jnp.where(lane == cols - 1, pltpu.roll(side, 1, 1), pltpu.roll(values, cols - 1, 1))
        yp2 = jnp.where(lane >= cols - 2, side, pltpu.roll(values, cols - 2, 1))
        return xm2, xm1, xp1, xp2, ym2, ym1, yp1, yp2

    def fourth(m2, m1, p1, p2):
        return (8.0 * (p1 - m1) - (p2 - m2)) * (1.0 / 12.0)

    def level(k, carry):
        global_level = chunk * depth_levels + k
        active = (global_level < reach).astype(jnp.float32)
        masked = [state_ref[f, k] * active for f in range(fields)]
        west = [west_ref[f, k] for f in range(fields)]
        east = [east_ref[f, k] for f in range(fields)]
        packed_level = global_level % PACK
        shift = (cols - 2 - 4 * packed_level) % cols
        side = [pltpu.roll(side_ref[f, global_level // PACK], shift, 1) for f in range(fields)]
        density = -THERMAL * masked[0] + HALINE * masked[1]
        density_w = -THERMAL * west[0] + HALINE * west[1]
        density_e = -THERMAL * east[0] + HALINE * east[1]
        density_s = -THERMAL * side[0] + HALINE * side[1]
        sums_ref[0] = sums_ref[0] + density
        sums_ref[1] = sums_ref[1] + density_s
        sums_ref[2, 0:2] = sums_ref[2, 0:2] + density_w
        sums_ref[2, 2:4] = sums_ref[2, 2:4] + density_e
        scale = PRESSURE_SCALE / levels
        pressure = scale * sums_ref[0]
        pressure_s = scale * sums_ref[1]
        pressure_w = scale * sums_ref[2, 0:2]
        pressure_e = scale * sums_ref[2, 2:4]
        east_vel = masked[2]
        north_vel = masked[3]
        pm2, pm1, pp1, pp2, qm2, qm1, qp1, qp2 = near(pressure, pressure_w, pressure_e, pressure_s)
        extra = [None, None,
                 -fourth(pm2, pm1, pp1, pp2) + coriolis * north_vel,
                 -fourth(qm2, qm1, qp1, qp2) - coriolis * east_vel]
        for f in range(fields):
            xm2, xm1, xp1, xp2, ym2, ym1, yp1, yp2 = near(masked[f], west[f], east[f], side[f])
            lap = xp1 + xm1 + yp1 + ym1 - 4.0 * masked[f]
            tendency = -(east_vel * fourth(xm2, xm1, xp1, xp2) + north_vel * fourth(ym2, ym1, yp1, yp2)) + VISCOSITY * lap
            if extra[f] is not None:
                tendency = tendency + extra[f]
                forcing_ref[f - 2] = forcing_ref[f - 2] + active * tendency
            provisional_ref[f, k] = active * (masked[f] + STEP_TIME * tendency)
        return carry

    @pl.when(chunk == 0)
    def _():
        forcing_ref[...] = jnp.zeros_like(forcing_ref)

    lax.fori_loop(0, depth_levels, level, 0, unroll=4)

    @pl.when(chunk == pl.num_programs(0) - 1)
    def _():
        forcing_ref[...] = forcing_ref[...] / levels


def stencil(state, depth_class, west, east, side, coriolis):
    fields, levels, rows, cols = state.shape
    steps = levels // LEVEL_CHUNK
    big = pl.BlockSpec((fields, LEVEL_CHUNK, rows, cols), lambda c: (0, c, 0, 0))
    rim = pl.BlockSpec((fields, LEVEL_CHUNK, 2, cols), lambda c: (0, c, 0, 0))
    flat = pl.BlockSpec((rows, cols), lambda c: (0, 0))
    packed = pl.BlockSpec(side.shape, lambda c: (0, 0, 0, 0))
    return pl.pallas_call(
        stencil_kernel,
        grid=(steps,),
        out_shape=(jax.ShapeDtypeStruct(state.shape, jnp.float32),
                   jax.ShapeDtypeStruct((2, rows, cols), jnp.float32)),
        in_specs=[flat, pl.BlockSpec((1, cols), lambda c: (0, 0)), big, rim, rim, packed],
        out_specs=(big, pl.BlockSpec((2, rows, cols), lambda c: (0, 0, 0))),
        scratch_shapes=[pltpu.VMEM((3, rows, cols), jnp.float32)],
        compiler_params=pltpu.CompilerParams(dimension_semantics=("arbitrary",)),
        cost_estimate=pl.CostEstimate(
            flops=60 * state.size, transcendentals=0, bytes_accessed=4 * 2 * state.size
        ),
    )(depth_class, coriolis, state, west, east, side)


def pack_kernel(depth_ref, state_ref, out_ref, head_ref, tail_ref):
    block_index = pl.program_id(0)
    fields, depth_levels, rows, cols = state_ref.shape
    block = depth_levels * pl.num_programs(0) // 4
    lane = lax.broadcasted_iota(jnp.int32, (rows, cols), 1)
    reach = depth_ref[...] * block
    packed = [jnp.zeros((rows, cols), jnp.float32) for f in range(fields)]
    for k in range(depth_levels):
        active = (block_index * depth_levels + k < reach).astype(jnp.float32)
        low = 4 * k
        first = (lane == low) | (lane == low + 1)
        second = (lane == low + 2) | (lane == low + 3)
        for f in range(fields):
            masked = state_ref[f, k] * active
            head_ref[f, k] = masked[0:2]
            tail_ref[f, k] = masked[rows - 2 : rows]
            near_end = pltpu.roll(masked, low, 1)
            far_end = pltpu.roll(masked, (low + 4) % cols, 1)
            packed[f] = jnp.where(first, near_end, jnp.where(second, far_end, packed[f]))
    for f in range(fields):
        out_ref[f, 0] = packed[f]


def pack_edges(state, depth_class):
    fields, levels, rows, cols = state.shape
    rim = pl.BlockSpec((fields, PACK, 2, cols), lambda c: (0, c, 0, 0))
    return pl.pallas_call(
        pack_kernel,
        grid=(levels // PACK,),
        out_shape=(
            jax.ShapeDtypeStruct((fields, levels // PACK, rows, cols), jnp.float32),
            jax.ShapeDtypeStruct((fields, levels, 2, cols), jnp.float32),
            jax.ShapeDtypeStruct((fields, levels, 2, cols), jnp.float32),
        ),
        in_specs=[pl.BlockSpec((rows, cols), lambda c: (0, 0)),
                  pl.BlockSpec((fields, PACK, rows, cols), lambda c: (0, c, 0, 0))],
        out_specs=(pl.BlockSpec((fields, 1, rows, cols), lambda c: (0, c, 0, 0)), rim, rim),
        cost_estimate=pl.CostEstimate(
            flops=4 * state.size, transcendentals=0, bytes_accessed=4 * state.size
        ),
    )(depth_class, state)


def combine(from_south, from_north):
    lane = lax.broadcasted_iota(jnp.int32, from_south.shape, from_south.ndim - 1)
    return jnp.where(lane % 4 >= 2, from_south, from_north)


def wave_kernel(moving_ref, fixed_ref, coriolis_ref, height_ref, transport_ref, work_ref):
    rows, cols = moving_ref.shape[1], moving_ref.shape[2]
    inner_rows, inner_cols = height_ref.shape[0], height_ref.shape[1]
    rim = (rows - inner_rows) // 2
    groups = 8
    per_group = SUB // groups
    trim = 2 * per_group
    work_ref[...] = moving_ref[...]
    for group in range(groups):
        low = trim * group
        high = rows - trim * group
        span = high - low
        column_depth = fixed_ref[2, low:high]
        sea_mask = (column_depth > 0.0).astype(jnp.float32)
        force_east = fixed_ref[0, low:high]
        force_north = fixed_ref[1, low:high]
        coriolis = jnp.broadcast_to(coriolis_ref[0:1, :], (span, cols))

        def x_slope_rolled(values):
            return (pltpu.roll(values, span - 1, 0) - pltpu.roll(values, 1, 0)) * 0.5

        def y_slope_rolled(values):
            return (pltpu.roll(values, cols - 1, 1) - pltpu.roll(values, 1, 1)) * 0.5

        def step(index, carry):
            surface = work_ref[0, low:high]
            east_old = work_ref[1, low:high]
            north_old = work_ref[2, low:high]
            surface_mid = sea_mask * (
                surface - WAVE_STEP * (x_slope_rolled(east_old) + y_slope_rolled(north_old))
            )
            east_new = sea_mask * (
                east_old
                + WAVE_STEP
                * (
                    -GRAVITY * column_depth * x_slope_rolled(surface_mid)
                    + coriolis * north_old
                    + force_east
                    - BOTTOM_DRAG * east_old
                )
            )
            north_new = sea_mask * (
                north_old
                + WAVE_STEP
                * (
                    -GRAVITY * column_depth * y_slope_rolled(surface_mid)
                    - coriolis * east_new
                    + force_north
                    - BOTTOM_DRAG * north_old
                )
            )
            work_ref[0, low:high] = surface_mid
            work_ref[1, low:high] = east_new
            work_ref[2, low:high] = north_new
            return carry

        lax.fori_loop(0, per_group, step, 0)
    for field in range(3):
        middle = work_ref[field, rim : rim + inner_rows]
        inner = pltpu.roll(middle, cols - rim, 1)[:, :inner_cols]
        if field == 0:
            height_ref[...] = inner
        else:
            transport_ref[field - 1] = inner


def local_waves(moving, fixed, coriolis, inner_rows, inner_cols):
    rows, cols = moving.shape[1], moving.shape[2]
    elements = rows * cols
    return pl.pallas_call(
        wave_kernel,
        out_shape=(
            jax.ShapeDtypeStruct((inner_rows, inner_cols), jnp.float32),
            jax.ShapeDtypeStruct((2, inner_rows, inner_cols), jnp.float32),
        ),
        in_specs=[pl.BlockSpec(memory_space=pltpu.VMEM)] * 3,
        out_specs=(pl.BlockSpec(memory_space=pltpu.VMEM), pl.BlockSpec(memory_space=pltpu.VMEM)),
        scratch_shapes=[pltpu.VMEM(moving.shape, jnp.float32)],
        cost_estimate=pl.CostEstimate(
            flops=SUB * 30 * elements, transcendentals=0, bytes_accessed=4 * 7 * elements
        ),
    )(moving, fixed, coriolis)


def body(state, depth_class, vertical_inverse, height, transport):
    levels = state.shape[1]
    level_block = levels // vertical_inverse.shape[0]
    y_cells = depth_class.shape[1]
    level_ids = lax.broadcasted_iota(jnp.int32, (levels, 1, 1), 0)
    active = (level_ids < depth_class[None] * level_block).astype(jnp.float32)
    column_blocks = lax.axis_size(("gy", "mode"))
    anchor = lax.axis_index(("gy", "mode")) * y_cells
    coriolis = coriolis_row(anchor, y_cells, y_cells * column_blocks)
    edges, head, tail = pack_edges(state, depth_class)
    x_count = lax.axis_size("gx")
    west = lax.ppermute(tail, "gx", [(i, i + 1) for i in range(x_count - 1)])
    east = lax.ppermute(head, "gx", [(i + 1, i) for i in range(x_count - 1)])
    y_count = lax.axis_size(("gy", "mode"))
    from_south = lax.ppermute(edges, ("gy", "mode"), [(i, i + 1) for i in range(y_count - 1)])
    from_north = lax.ppermute(edges, ("gy", "mode"), [(i + 1, i) for i in range(y_count - 1)])
    side = combine(from_south, from_north)
    provisional, forcing = stencil(state, depth_class, west, east, side, coriolis)
    updated = vertical_solve(state, provisional, active, depth_class, vertical_inverse)
    column_depth = depth_class.astype(jnp.float32) * level_block / levels
    sea_mask = (depth_class > 0).astype(jnp.float32)
    moving = jnp.stack([height, transport[0], transport[1]]) * sea_mask
    fields = jnp.stack([moving[0], moving[1], moving[2], forcing[0], forcing[1], column_depth])
    rim = 2 * SUB
    fields = wide_halo(fields, "gx", 1, rim)
    fields = wide_halo(fields, ("gy", "mode"), 2, rim)
    coriolis_wide = coriolis_row(anchor - rim, y_cells + 2 * rim, y_cells * column_blocks)
    x_cells = depth_class.shape[0]
    height_next, transport_next = local_waves(fields[0:3], fields[3:6], coriolis_wide, x_cells, y_cells)
    state_next = finish(updated, transport_next, active, depth_class, level_block, levels)
    return (state_next, height_next, transport_next)


def solution(mesh):
    placed = (
        P(None, None, "gx", ("gy", "mode")),
        P("gx", ("gy", "mode")),
        P(),
        P("gx", ("gy", "mode")),
        P(None, "gx", ("gy", "mode")),
    )
    return jax.shard_map(
        body,
        mesh=mesh,
        in_specs=placed,
        out_specs=(
            P(None, None, "gx", ("gy", "mode")),
            P("gx", ("gy", "mode")),
            P(None, "gx", ("gy", "mode")),
        ),
        check_vma=False,
    )
```

```python
import jax
import numpy as np
import jax.numpy as jnp
from jax import lax
from jax.experimental import pallas as pl
from jax.experimental.pallas import tpu as pltpu
from jax.sharding import PartitionSpec as P

SUB = 32
LEVEL_CHUNK = 16
PACK = 32


THERMAL = 0.8
HALINE = 0.6
PRESSURE_SCALE = 4.0
VISCOSITY = 0.1
STEP_TIME = 0.05
WAVE_STEP = 0.5
GRAVITY = 1.0
BOTTOM_DRAG = 0.05
CORIOLIS_BASE = 0.3
CORIOLIS_SLOPE = 0.4


def coriolis_row(anchor, number, total):
    position = (anchor + lax.broadcasted_iota(jnp.int32, (number,), 0)).astype(jnp.float32)
    return (CORIOLIS_BASE + CORIOLIS_SLOPE * (position + 0.5) / total)[None, :]


def vertical_solve(state, provisional, active, depth_class, inverse):
    levels = state.shape[1]
    classes = inverse.shape[0]
    band = levels // classes
    rows_used = np.concatenate(
        [class_index * levels + np.arange(band * (class_index + 1)) for class_index in range(classes)]
    )
    stacked = jnp.take(inverse.reshape(classes * levels, inverse.shape[2]), rows_used, axis=0)
    every = jnp.einsum("kl,flxy->fkxy", stacked, provisional, precision=lax.Precision.HIGH)
    starts = [band * class_index * (class_index + 1) // 2 for class_index in range(classes)]
    chosen = [(depth_class == class_index + 1).astype(jnp.float32) for class_index in range(classes)]
    bands = []
    for level_band in range(classes):
        part = jnp.zeros_like(provisional[:, :band])
        for class_index in range(level_band, classes):
            first = starts[class_index] + level_band * band
            part = part + chosen[class_index] * every[:, first : first + band]
        bands.append(part)
    solved = jnp.concatenate(bands, axis=1)
    return active * solved + (1.0 - active) * state


def finish(updated, transport_next, active, depth_class, level_block, levels):
    counted = jnp.maximum(depth_class * level_block, 1).astype(jnp.float32)
    safe_depth = jnp.maximum(depth_class, 1).astype(jnp.float32) * level_block / levels
    column_means = jnp.sum(active * updated[2:4], axis=1) / counted
    carried = transport_next / safe_depth
    velocity = updated[2:4] + active * (carried - column_means)[:, None]
    return jnp.concatenate([updated[0:2], velocity], axis=0)


def wide_halo(cells, axis, dim, width):
    count = lax.axis_size(axis)
    size = cells.shape[dim]
    before, after = [], []
    remaining, hop = width, 1
    while remaining > 0:
        take = min(size, remaining)
        tail = lax.slice_in_dim(cells, size - take, size, axis=dim)
        head = lax.slice_in_dim(cells, 0, take, axis=dim)
        if hop < count:
            from_before = lax.ppermute(tail, axis, [(i, i + hop) for i in range(count - hop)])
            from_after = lax.ppermute(head, axis, [(i + hop, i) for i in range(count - hop)])
        else:
            from_before = jnp.zeros_like(tail)
            from_after = jnp.zeros_like(head)
        before.insert(0, from_before)
        after.append(from_after)
        remaining -= take
        hop += 1
    return jnp.concatenate(before + [cells] + after, axis=dim)


def stencil_kernel(depth_ref, coriolis_ref, state_ref, west_ref, east_ref, side_ref,
                   provisional_ref, forcing_ref, sums_ref):
    chunk = pl.program_id(0)
    fields, depth_levels, rows, cols = state_ref.shape
    levels = depth_levels * pl.num_programs(0)
    block = levels // 4

    @pl.when(chunk == 0)
    def _():
        sums_ref[...] = jnp.zeros_like(sums_ref)

    row = lax.broadcasted_iota(jnp.int32, (rows, cols), 0)
    lane = lax.broadcasted_iota(jnp.int32, (rows, cols), 1)
    reach = depth_ref[...] * block
    coriolis = coriolis_ref[0:1, :]

    def near(values, west, east, side):
        w0 = jnp.broadcast_to(west[0:1], (rows, cols))
        w1 = jnp.broadcast_to(west[1:2], (rows, cols))
        e0 = jnp.broadcast_to(east[0:1], (rows, cols))
        e1 = jnp.broadcast_to(east[1:2], (rows, cols))
        xm1 = jnp.where(row == 0, w1, pltpu.roll(values, 1, 0))
        xm2 = jnp.where(row == 0, w0, jnp.where(row == 1, w1, pltpu.roll(values, 2, 0)))
        xp1 = jnp.where(row == rows - 1, e0, pltpu.roll(values, rows - 1, 0))
        xp2 = jnp.where(row == rows - 2, e0, jnp.where(row == rows - 1, e1, pltpu.roll(values, rows - 2, 0)))
        ym1 = jnp.where(lane == 0, pltpu.roll(side, cols - 1, 1), pltpu.roll(values, 1, 1))
        ym2 = jnp.where(lane < 2, side, pltpu.roll(values, 2, 1))
        yp1 = jnp.where(lane == cols - 1, pltpu.roll(side, 1, 1), pltpu.roll(values, cols - 1, 1))
        yp2 = jnp.where(lane >= cols - 2, side, pltpu.roll(values, cols - 2, 1))
        return xm2, xm1, xp1, xp2, ym2, ym1, yp1, yp2

    def fourth(m2, m1, p1, p2):
        return (8.0 * (p1 - m1) - (p2 - m2)) * (1.0 / 12.0)

    def level(k, carry):
        global_level = chunk * depth_levels + k
        active = (global_level < reach).astype(jnp.float32)
        masked = [state_ref[f, k] * active for f in range(fields)]
        west = [west_ref[f, k] for f in range(fields)]
        east = [east_ref[f, k] for f in range(fields)]
        packed_level = global_level % PACK
        shift = (cols - 2 - 4 * packed_level) % cols
        side = [pltpu.roll(side_ref[f, global_level // PACK], shift, 1) for f in range(fields)]
        density = -THERMAL * masked[0] + HALINE * masked[1]
        density_w = -THERMAL * west[0] + HALINE * west[1]
        density_e = -THERMAL * east[0] + HALINE * east[1]
        density_s = -THERMAL * side[0] + HALINE * side[1]
        sums_ref[0] = sums_ref[0] + density
        sums_ref[1] = sums_ref[1] + density_s
        sums_ref[2, 0:2] = sums_ref[2, 0:2] + density_w
        sums_ref[2, 2:4] = sums_ref[2, 2:4] + density_e
        scale = PRESSURE_SCALE / levels
        pressure = scale * sums_ref[0]
        pressure_s = scale * sums_ref[1]
        pressure_w = scale * sums_ref[2, 0:2]
        pressure_e = scale * sums_ref[2, 2:4]
        east_vel = masked[2]
        north_vel = masked[3]
        pm2, pm1, pp1, pp2, qm2, qm1, qp1, qp2 = near(pressure, pressure_w, pressure_e, pressure_s)
        extra = [None, None,
                 -fourth(pm2, pm1, pp1, pp2) + coriolis * north_vel,
                 -fourth(qm2, qm1, qp1, qp2) - coriolis * east_vel]
        for f in range(fields):
            xm2, xm1, xp1, xp2, ym2, ym1, yp1, yp2 = near(masked[f], west[f], east[f], side[f])
            lap = xp1 + xm1 + yp1 + ym1 - 4.0 * masked[f]
            tendency = -(east_vel * fourth(xm2, xm1, xp1, xp2) + north_vel * fourth(ym2, ym1, yp1, yp2)) + VISCOSITY * lap
            if extra[f] is not None:
                tendency = tendency + extra[f]
                forcing_ref[f - 2] = forcing_ref[f - 2] + active * tendency
            provisional_ref[f, k] = active * (masked[f] + STEP_TIME * tendency)
        return carry

    @pl.when(chunk == 0)
    def _():
        forcing_ref[...] = jnp.zeros_like(forcing_ref)

    lax.fori_loop(0, depth_levels, level, 0, unroll=4)

    @pl.when(chunk == pl.num_programs(0) - 1)
    def _():
        forcing_ref[...] = forcing_ref[...] / levels


def stencil(state, depth_class, west, east, side, coriolis):
    fields, levels, rows, cols = state.shape
    steps = levels // LEVEL_CHUNK
    big = pl.BlockSpec((fields, LEVEL_CHUNK, rows, cols), lambda c: (0, c, 0, 0))
    rim = pl.BlockSpec((fields, LEVEL_CHUNK, 2, cols), lambda c: (0, c, 0, 0))
    flat = pl.BlockSpec((rows, cols), lambda c: (0, 0))
    packed = pl.BlockSpec(side.shape, lambda c: (0, 0, 0, 0))
    return pl.pallas_call(
        stencil_kernel,
        grid=(steps,),
        out_shape=(jax.ShapeDtypeStruct(state.shape, jnp.float32),
                   jax.ShapeDtypeStruct((2, rows, cols), jnp.float32)),
        in_specs=[flat, pl.BlockSpec((1, cols), lambda c: (0, 0)), big, rim, rim, packed],
        out_specs=(big, pl.BlockSpec((2, rows, cols), lambda c: (0, 0, 0))),
        scratch_shapes=[pltpu.VMEM((3, rows, cols), jnp.float32)],
        compiler_params=pltpu.CompilerParams(dimension_semantics=("arbitrary",)),
        cost_estimate=pl.CostEstimate(
            flops=60 * state.size, transcendentals=0, bytes_accessed=4 * 2 * state.size
        ),
    )(depth_class, coriolis, state, west, east, side)


def pack_kernel(depth_ref, state_ref, out_ref, head_ref, tail_ref):
    block_index = pl.program_id(0)
    fields, depth_levels, rows, cols = state_ref.shape
    block = depth_levels * pl.num_programs(0) // 4
    lane = lax.broadcasted_iota(jnp.int32, (rows, cols), 1)
    reach = depth_ref[...] * block
    packed = [jnp.zeros((rows, cols), jnp.float32) for f in range(fields)]
    for k in range(depth_levels):
        active = (block_index * depth_levels + k < reach).astype(jnp.float32)
        low = 4 * k
        first = (lane == low) | (lane == low + 1)
        second = (lane == low + 2) | (lane == low + 3)
        for f in range(fields):
            masked = state_ref[f, k] * active
            head_ref[f, k] = masked[0:2]
            tail_ref[f, k] = masked[rows - 2 : rows]
            near_end = pltpu.roll(masked, low, 1)
            far_end = pltpu.roll(masked, (low + 4) % cols, 1)
            packed[f] = jnp.where(first, near_end, jnp.where(second, far_end, packed[f]))
    for f in range(fields):
        out_ref[f, 0] = packed[f]


def pack_edges(state, depth_class):
    fields, levels, rows, cols = state.shape
    rim = pl.BlockSpec((fields, PACK, 2, cols), lambda c: (0, c, 0, 0))
    return pl.pallas_call(
        pack_kernel,
        grid=(levels // PACK,),
        out_shape=(
            jax.ShapeDtypeStruct((fields, levels // PACK, rows, cols), jnp.float32),
            jax.ShapeDtypeStruct((fields, levels, 2, cols), jnp.float32),
            jax.ShapeDtypeStruct((fields, levels, 2, cols), jnp.float32),
        ),
        in_specs=[pl.BlockSpec((rows, cols), lambda c: (0, 0)),
                  pl.BlockSpec((fields, PACK, rows, cols), lambda c: (0, c, 0, 0))],
        out_specs=(pl.BlockSpec((fields, 1, rows, cols), lambda c: (0, c, 0, 0)), rim, rim),
        cost_estimate=pl.CostEstimate(
            flops=4 * state.size, transcendentals=0, bytes_accessed=4 * state.size
        ),
    )(depth_class, state)


def combine(from_south, from_north):
    lane = lax.broadcasted_iota(jnp.int32, from_south.shape, from_south.ndim - 1)
    return jnp.where(lane % 4 >= 2, from_south, from_north)


def wave_kernel(moving_ref, fixed_ref, coriolis_ref, height_ref, transport_ref, work_ref):
    rows, cols = moving_ref.shape[1], moving_ref.shape[2]
    inner_rows, inner_cols = height_ref.shape[0], height_ref.shape[1]
    rim = (rows - inner_rows) // 2
    groups = 8
    per_group = SUB // groups
    trim = 2 * per_group
    work_ref[...] = moving_ref[...]
    for group in range(groups):
        low = trim * group
        high = rows - trim * group
        span = high - low
        column_depth = fixed_ref[2, low:high]
        sea_mask = (column_depth > 0.0).astype(jnp.float32)
        force_east = fixed_ref[0, low:high]
        force_north = fixed_ref[1, low:high]
        coriolis = jnp.broadcast_to(coriolis_ref[0:1, :], (span, cols))

        def x_slope_rolled(values):
            return (pltpu.roll(values, span - 1, 0) - pltpu.roll(values, 1, 0)) * 0.5

        def y_slope_rolled(values):
            return (pltpu.roll(values, cols - 1, 1) - pltpu.roll(values, 1, 1)) * 0.5

        def step(index, carry):
            surface = work_ref[0, low:high]
            east_old = work_ref[1, low:high]
            north_old = work_ref[2, low:high]
            surface_mid = sea_mask * (
                surface - WAVE_STEP * (x_slope_rolled(east_old) + y_slope_rolled(north_old))
            )
            east_new = sea_mask * (
                east_old
                + WAVE_STEP
                * (
                    -GRAVITY * column_depth * x_slope_rolled(surface_mid)
                    + coriolis * north_old
                    + force_east
                    - BOTTOM_DRAG * east_old
                )
            )
            north_new = sea_mask * (
                north_old
                + WAVE_STEP
                * (
                    -GRAVITY * column_depth * y_slope_rolled(surface_mid)
                    - coriolis * east_new
                    + force_north
                    - BOTTOM_DRAG * north_old
                )
            )
            work_ref[0, low:high] = surface_mid
            work_ref[1, low:high] = east_new
            work_ref[2, low:high] = north_new
            return carry

        lax.fori_loop(0, per_group, step, 0, unroll=True)
    for field in range(3):
        middle = work_ref[field, rim : rim + inner_rows]
        inner = pltpu.roll(middle, cols - rim, 1)[:, :inner_cols]
        if field == 0:
            height_ref[...] = inner
        else:
            transport_ref[field - 1] = inner


def local_waves(moving, fixed, coriolis, inner_rows, inner_cols):
    rows, cols = moving.shape[1], moving.shape[2]
    elements = rows * cols
    return pl.pallas_call(
        wave_kernel,
        out_shape=(
            jax.ShapeDtypeStruct((inner_rows, inner_cols), jnp.float32),
            jax.ShapeDtypeStruct((2, inner_rows, inner_cols), jnp.float32),
        ),
        in_specs=[pl.BlockSpec(memory_space=pltpu.VMEM)] * 3,
        out_specs=(pl.BlockSpec(memory_space=pltpu.VMEM), pl.BlockSpec(memory_space=pltpu.VMEM)),
        scratch_shapes=[pltpu.VMEM(moving.shape, jnp.float32)],
        cost_estimate=pl.CostEstimate(
            flops=SUB * 30 * elements, transcendentals=0, bytes_accessed=4 * 7 * elements
        ),
    )(moving, fixed, coriolis)


def body(state, depth_class, vertical_inverse, height, transport):
    levels = state.shape[1]
    level_block = levels // vertical_inverse.shape[0]
    y_cells = depth_class.shape[1]
    level_ids = lax.broadcasted_iota(jnp.int32, (levels, 1, 1), 0)
    active = (level_ids < depth_class[None] * level_block).astype(jnp.float32)
    column_blocks = lax.axis_size(("gy", "mode"))
    anchor = lax.axis_index(("gy", "mode")) * y_cells
    coriolis = coriolis_row(anchor, y_cells, y_cells * column_blocks)
    edges, head, tail = pack_edges(state, depth_class)
    x_count = lax.axis_size("gx")
    west = lax.ppermute(tail, "gx", [(i, i + 1) for i in range(x_count - 1)])
    east = lax.ppermute(head, "gx", [(i + 1, i) for i in range(x_count - 1)])
    y_count = lax.axis_size(("gy", "mode"))
    from_south = lax.ppermute(edges, ("gy", "mode"), [(i, i + 1) for i in range(y_count - 1)])
    from_north = lax.ppermute(edges, ("gy", "mode"), [(i + 1, i) for i in range(y_count - 1)])
    side = combine(from_south, from_north)
    provisional, forcing = stencil(state, depth_class, west, east, side, coriolis)
    updated = vertical_solve(state, provisional, active, depth_class, vertical_inverse)
    column_depth = depth_class.astype(jnp.float32) * level_block / levels
    sea_mask = (depth_class > 0).astype(jnp.float32)
    moving = jnp.stack([height, transport[0], transport[1]]) * sea_mask
    fields = jnp.stack([moving[0], moving[1], moving[2], forcing[0], forcing[1], column_depth])
    rim = 2 * SUB
    fields = wide_halo(fields, "gx", 1, rim)
    fields = wide_halo(fields, ("gy", "mode"), 2, rim)
    coriolis_wide = coriolis_row(anchor - rim, y_cells + 2 * rim, y_cells * column_blocks)
    x_cells = depth_class.shape[0]
    height_next, transport_next = local_waves(fields[0:3], fields[3:6], coriolis_wide, x_cells, y_cells)
    state_next = finish(updated, transport_next, active, depth_class, level_block, levels)
    return (state_next, height_next, transport_next)


def solution(mesh):
    placed = (
        P(None, None, "gx", ("gy", "mode")),
        P("gx", ("gy", "mode")),
        P(),
        P("gx", ("gy", "mode")),
        P(None, "gx", ("gy", "mode")),
    )
    return jax.shard_map(
        body,
        mesh=mesh,
        in_specs=placed,
        out_specs=(
            P(None, None, "gx", ("gy", "mode")),
            P("gx", ("gy", "mode")),
            P(None, "gx", ("gy", "mode")),
        ),
        check_vma=False,
    )
```

```python
import jax
import numpy as np
import jax.numpy as jnp
from jax import lax
from jax.experimental import pallas as pl
from jax.experimental.pallas import tpu as pltpu
from jax.sharding import PartitionSpec as P

SUB = 32
LEVEL_CHUNK = 16
PACK = 32


THERMAL = 0.8
HALINE = 0.6
PRESSURE_SCALE = 4.0
VISCOSITY = 0.1
STEP_TIME = 0.05
WAVE_STEP = 0.5
GRAVITY = 1.0
BOTTOM_DRAG = 0.05
CORIOLIS_BASE = 0.3
CORIOLIS_SLOPE = 0.4


def coriolis_row(anchor, number, total):
    position = (anchor + lax.broadcasted_iota(jnp.int32, (number,), 0)).astype(jnp.float32)
    return (CORIOLIS_BASE + CORIOLIS_SLOPE * (position + 0.5) / total)[None, :]


def vertical_solve(state, provisional, active, depth_class, inverse):
    levels = state.shape[1]
    classes = inverse.shape[0]
    band = levels // classes
    rows_used = np.concatenate(
        [class_index * levels + np.arange(band * (class_index + 1)) for class_index in range(classes)]
    )
    stacked = jnp.take(inverse.reshape(classes * levels, inverse.shape[2]), rows_used, axis=0)
    every = jnp.einsum("kl,flxy->fkxy", stacked, provisional, precision=lax.Precision.HIGH)
    starts = [band * class_index * (class_index + 1) // 2 for class_index in range(classes)]
    chosen = [(depth_class == class_index + 1).astype(jnp.float32) for class_index in range(classes)]
    bands = []
    for level_band in range(classes):
        part = jnp.zeros_like(provisional[:, :band])
        for class_index in range(level_band, classes):
            first = starts[class_index] + level_band * band
            part = part + chosen[class_index] * every[:, first : first + band]
        bands.append(part)
    solved = jnp.concatenate(bands, axis=1)
    return active * solved + (1.0 - active) * state


def finish(updated, transport_next, active, depth_class, level_block, levels):
    counted = jnp.maximum(depth_class * level_block, 1).astype(jnp.float32)
    safe_depth = jnp.maximum(depth_class, 1).astype(jnp.float32) * level_block / levels
    column_means = jnp.sum(active * updated[2:4], axis=1) / counted
    carried = transport_next / safe_depth
    velocity = updated[2:4] + active * (carried - column_means)[:, None]
    return jnp.concatenate([updated[0:2], velocity], axis=0)


def wide_halo(cells, axis, dim, width):
    count = lax.axis_size(axis)
    size = cells.shape[dim]
    before, after = [], []
    remaining, hop = width, 1
    while remaining > 0:
        take = min(size, remaining)
        tail = lax.slice_in_dim(cells, size - take, size, axis=dim)
        head = lax.slice_in_dim(cells, 0, take, axis=dim)
        if hop < count:
            from_before = lax.ppermute(tail, axis, [(i, i + hop) for i in range(count - hop)])
            from_after = lax.ppermute(head, axis, [(i + hop, i) for i in range(count - hop)])
        else:
            from_before = jnp.zeros_like(tail)
            from_after = jnp.zeros_like(head)
        before.insert(0, from_before)
        after.append(from_after)
        remaining -= take
        hop += 1
    return jnp.concatenate(before + [cells] + after, axis=dim)


def stencil_kernel(depth_ref, coriolis_ref, state_ref, west_ref, east_ref, side_ref,
                   provisional_ref, forcing_ref, sums_ref):
    chunk = pl.program_id(0)
    fields, depth_levels, rows, cols = state_ref.shape
    levels = depth_levels * pl.num_programs(0)
    block = levels // 4

    @pl.when(chunk == 0)
    def _():
        sums_ref[...] = jnp.zeros_like(sums_ref)

    row = lax.broadcasted_iota(jnp.int32, (rows, cols), 0)
    lane = lax.broadcasted_iota(jnp.int32, (rows, cols), 1)
    reach = depth_ref[...] * block
    coriolis = coriolis_ref[0:1, :]

    def near(values, west, east, side):
        w0 = jnp.broadcast_to(west[0:1], (rows, cols))
        w1 = jnp.broadcast_to(west[1:2], (rows, cols))
        e0 = jnp.broadcast_to(east[0:1], (rows, cols))
        e1 = jnp.broadcast_to(east[1:2], (rows, cols))
        xm1 = jnp.where(row == 0, w1, pltpu.roll(values, 1, 0))
        xm2 = jnp.where(row == 0, w0, jnp.where(row == 1, w1, pltpu.roll(values, 2, 0)))
        xp1 = jnp.where(row == rows - 1, e0, pltpu.roll(values, rows - 1, 0))
        xp2 = jnp.where(row == rows - 2, e0, jnp.where(row == rows - 1, e1, pltpu.roll(values, rows - 2, 0)))
        ym1 = jnp.where(lane == 0, pltpu.roll(side, cols - 1, 1), pltpu.roll(values, 1, 1))
        ym2 = jnp.where(lane < 2, side, pltpu.roll(values, 2, 1))
        yp1 = jnp.where(lane == cols - 1, pltpu.roll(side, 1, 1), pltpu.roll(values, cols - 1, 1))
        yp2 = jnp.where(lane >= cols - 2, side, pltpu.roll(values, cols - 2, 1))
        return xm2, xm1, xp1, xp2, ym2, ym1, yp1, yp2

    def fourth(m2, m1, p1, p2):
        return (8.0 * (p1 - m1) - (p2 - m2)) * (1.0 / 12.0)

    def level(k, carry):
        global_level = chunk * depth_levels + k
        active = (global_level < reach).astype(jnp.float32)
        masked = [state_ref[f, k] * active for f in range(fields)]
        west = [west_ref[f, k] for f in range(fields)]
        east = [east_ref[f, k] for f in range(fields)]
        packed_level = global_level % PACK
        shift = (cols - 2 - 4 * packed_level) % cols
        side = [pltpu.roll(side_ref[f, global_level // PACK], shift, 1) for f in range(fields)]
        density = -THERMAL * masked[0] + HALINE * masked[1]
        density_w = -THERMAL * west[0] + HALINE * west[1]
        density_e = -THERMAL * east[0] + HALINE * east[1]
        density_s = -THERMAL * side[0] + HALINE * side[1]
        sums_ref[0] = sums_ref[0] + density
        sums_ref[1] = sums_ref[1] + density_s
        sums_ref[2, 0:2] = sums_ref[2, 0:2] + density_w
        sums_ref[2, 2:4] = sums_ref[2, 2:4] + density_e
        scale = PRESSURE_SCALE / levels
        pressure = scale * sums_ref[0]
        pressure_s = scale * sums_ref[1]
        pressure_w = scale * sums_ref[2, 0:2]
        pressure_e = scale * sums_ref[2, 2:4]
        east_vel = masked[2]
        north_vel = masked[3]
        pm2, pm1, pp1, pp2, qm2, qm1, qp1, qp2 = near(pressure, pressure_w, pressure_e, pressure_s)
        extra = [None, None,
                 -fourth(pm2, pm1, pp1, pp2) + coriolis * north_vel,
                 -fourth(qm2, qm1, qp1, qp2) - coriolis * east_vel]
        for f in range(fields):
            xm2, xm1, xp1, xp2, ym2, ym1, yp1, yp2 = near(masked[f], west[f], east[f], side[f])
            lap = xp1 + xm1 + yp1 + ym1 - 4.0 * masked[f]
            tendency = -(east_vel * fourth(xm2, xm1, xp1, xp2) + north_vel * fourth(ym2, ym1, yp1, yp2)) + VISCOSITY * lap
            if extra[f] is not None:
                tendency = tendency + extra[f]
                forcing_ref[f - 2] = forcing_ref[f - 2] + active * tendency
            provisional_ref[f, k] = active * (masked[f] + STEP_TIME * tendency)
        return carry

    @pl.when(chunk == 0)
    def _():
        forcing_ref[...] = jnp.zeros_like(forcing_ref)

    lax.fori_loop(0, depth_levels, level, 0, unroll=True)

    @pl.when(chunk == pl.num_programs(0) - 1)
    def _():
        forcing_ref[...] = forcing_ref[...] / levels


def stencil(state, depth_class, west, east, side, coriolis):
    fields, levels, rows, cols = state.shape
    steps = levels // LEVEL_CHUNK
    big = pl.BlockSpec((fields, LEVEL_CHUNK, rows, cols), lambda c: (0, c, 0, 0))
    rim = pl.BlockSpec((fields, LEVEL_CHUNK, 2, cols), lambda c: (0, c, 0, 0))
    flat = pl.BlockSpec((rows, cols), lambda c: (0, 0))
    packed = pl.BlockSpec(side.shape, lambda c: (0, 0, 0, 0))
    return pl.pallas_call(
        stencil_kernel,
        grid=(steps,),
        out_shape=(jax.ShapeDtypeStruct(state.shape, jnp.float32),
                   jax.ShapeDtypeStruct((2, rows, cols), jnp.float32)),
        in_specs=[flat, pl.BlockSpec((1, cols), lambda c: (0, 0)), big, rim, rim, packed],
        out_specs=(big, pl.BlockSpec((2, rows, cols), lambda c: (0, 0, 0))),
        scratch_shapes=[pltpu.VMEM((3, rows, cols), jnp.float32)],
        compiler_params=pltpu.CompilerParams(dimension_semantics=("arbitrary",)),
        cost_estimate=pl.CostEstimate(
            flops=60 * state.size, transcendentals=0, bytes_accessed=4 * 2 * state.size
        ),
    )(depth_class, coriolis, state, west, east, side)


def pack_kernel(depth_ref, state_ref, out_ref, head_ref, tail_ref):
    block_index = pl.program_id(0)
    fields, depth_levels, rows, cols = state_ref.shape
    block = depth_levels * pl.num_programs(0) // 4
    lane = lax.broadcasted_iota(jnp.int32, (rows, cols), 1)
    reach = depth_ref[...] * block
    packed = [jnp.zeros((rows, cols), jnp.float32) for f in range(fields)]
    for k in range(depth_levels):
        active = (block_index * depth_levels + k < reach).astype(jnp.float32)
        low = 4 * k
        first = (lane == low) | (lane == low + 1)
        second = (lane == low + 2) | (lane == low + 3)
        for f in range(fields):
            masked = state_ref[f, k] * active
            head_ref[f, k] = masked[0:2]
            tail_ref[f, k] = masked[rows - 2 : rows]
            near_end = pltpu.roll(masked, low, 1)
            far_end = pltpu.roll(masked, (low + 4) % cols, 1)
            packed[f] = jnp.where(first, near_end, jnp.where(second, far_end, packed[f]))
    for f in range(fields):
        out_ref[f, 0] = packed[f]


def pack_edges(state, depth_class):
    fields, levels, rows, cols = state.shape
    rim = pl.BlockSpec((fields, PACK, 2, cols), lambda c: (0, c, 0, 0))
    return pl.pallas_call(
        pack_kernel,
        grid=(levels // PACK,),
        out_shape=(
            jax.ShapeDtypeStruct((fields, levels // PACK, rows, cols), jnp.float32),
            jax.ShapeDtypeStruct((fields, levels, 2, cols), jnp.float32),
            jax.ShapeDtypeStruct((fields, levels, 2, cols), jnp.float32),
        ),
        in_specs=[pl.BlockSpec((rows, cols), lambda c: (0, 0)),
                  pl.BlockSpec((fields, PACK, rows, cols), lambda c: (0, c, 0, 0))],
        out_specs=(pl.BlockSpec((fields, 1, rows, cols), lambda c: (0, c, 0, 0)), rim, rim),
        cost_estimate=pl.CostEstimate(
            flops=4 * state.size, transcendentals=0, bytes_accessed=4 * state.size
        ),
    )(depth_class, state)


def combine(from_south, from_north):
    lane = lax.broadcasted_iota(jnp.int32, from_south.shape, from_south.ndim - 1)
    return jnp.where(lane % 4 >= 2, from_south, from_north)


def wave_kernel(moving_ref, fixed_ref, coriolis_ref, height_ref, transport_ref, work_ref):
    rows, cols = moving_ref.shape[1], moving_ref.shape[2]
    inner_rows, inner_cols = height_ref.shape[0], height_ref.shape[1]
    rim = (rows - inner_rows) // 2
    groups = 8
    per_group = SUB // groups
    trim = 2 * per_group
    work_ref[...] = moving_ref[...]
    for group in range(groups):
        low = trim * group
        high = rows - trim * group
        span = high - low
        column_depth = fixed_ref[2, low:high]
        sea_mask = (column_depth > 0.0).astype(jnp.float32)
        force_east = fixed_ref[0, low:high]
        force_north = fixed_ref[1, low:high]
        coriolis = jnp.broadcast_to(coriolis_ref[0:1, :], (span, cols))

        def x_slope_rolled(values):
            return (pltpu.roll(values, span - 1, 0) - pltpu.roll(values, 1, 0)) * 0.5

        def y_slope_rolled(values):
            return (pltpu.roll(values, cols - 1, 1) - pltpu.roll(values, 1, 1)) * 0.5

        def step(index, carry):
            surface = work_ref[0, low:high]
            east_old = work_ref[1, low:high]
            north_old = work_ref[2, low:high]
            surface_mid = sea_mask * (
                surface - WAVE_STEP * (x_slope_rolled(east_old) + y_slope_rolled(north_old))
            )
            east_new = sea_mask * (
                east_old
                + WAVE_STEP
                * (
                    -GRAVITY * column_depth * x_slope_rolled(surface_mid)
                    + coriolis * north_old
                    + force_east
                    - BOTTOM_DRAG * east_old
                )
            )
            north_new = sea_mask * (
                north_old
                + WAVE_STEP
                * (
                    -GRAVITY * column_depth * y_slope_rolled(surface_mid)
                    - coriolis * east_new
                    + force_north
                    - BOTTOM_DRAG * north_old
                )
            )
            work_ref[0, low:high] = surface_mid
            work_ref[1, low:high] = east_new
            work_ref[2, low:high] = north_new
            return carry

        lax.fori_loop(0, per_group, step, 0, unroll=True)
    for field in range(3):
        middle = work_ref[field, rim : rim + inner_rows]
        inner = pltpu.roll(middle, cols - rim, 1)[:, :inner_cols]
        if field == 0:
            height_ref[...] = inner
        else:
            transport_ref[field - 1] = inner


def local_waves(moving, fixed, coriolis, inner_rows, inner_cols):
    rows, cols = moving.shape[1], moving.shape[2]
    elements = rows * cols
    return pl.pallas_call(
        wave_kernel,
        out_shape=(
            jax.ShapeDtypeStruct((inner_rows, inner_cols), jnp.float32),
            jax.ShapeDtypeStruct((2, inner_rows, inner_cols), jnp.float32),
        ),
        in_specs=[pl.BlockSpec(memory_space=pltpu.VMEM)] * 3,
        out_specs=(pl.BlockSpec(memory_space=pltpu.VMEM), pl.BlockSpec(memory_space=pltpu.VMEM)),
        scratch_shapes=[pltpu.VMEM(moving.shape, jnp.float32)],
        cost_estimate=pl.CostEstimate(
            flops=SUB * 30 * elements, transcendentals=0, bytes_accessed=4 * 7 * elements
        ),
    )(moving, fixed, coriolis)


def body(state, depth_class, vertical_inverse, height, transport):
    levels = state.shape[1]
    level_block = levels // vertical_inverse.shape[0]
    y_cells = depth_class.shape[1]
    level_ids = lax.broadcasted_iota(jnp.int32, (levels, 1, 1), 0)
    active = (level_ids < depth_class[None] * level_block).astype(jnp.float32)
    column_blocks = lax.axis_size(("gy", "mode"))
    anchor = lax.axis_index(("gy", "mode")) * y_cells
    coriolis = coriolis_row(anchor, y_cells, y_cells * column_blocks)
    edges, head, tail = pack_edges(state, depth_class)
    x_count = lax.axis_size("gx")
    west = lax.ppermute(tail, "gx", [(i, i + 1) for i in range(x_count - 1)])
    east = lax.ppermute(head, "gx", [(i + 1, i) for i in range(x_count - 1)])
    y_count = lax.axis_size(("gy", "mode"))
    from_south = lax.ppermute(edges, ("gy", "mode"), [(i, i + 1) for i in range(y_count - 1)])
    from_north = lax.ppermute(edges, ("gy", "mode"), [(i + 1, i) for i in range(y_count - 1)])
    side = combine(from_south, from_north)
    provisional, forcing = stencil(state, depth_class, west, east, side, coriolis)
    updated = vertical_solve(state, provisional, active, depth_class, vertical_inverse)
    column_depth = depth_class.astype(jnp.float32) * level_block / levels
    sea_mask = (depth_class > 0).astype(jnp.float32)
    moving = jnp.stack([height, transport[0], transport[1]]) * sea_mask
    fields = jnp.stack([moving[0], moving[1], moving[2], forcing[0], forcing[1], column_depth])
    rim = 2 * SUB
    fields = wide_halo(fields, "gx", 1, rim)
    fields = wide_halo(fields, ("gy", "mode"), 2, rim)
    coriolis_wide = coriolis_row(anchor - rim, y_cells + 2 * rim, y_cells * column_blocks)
    x_cells = depth_class.shape[0]
    height_next, transport_next = local_waves(fields[0:3], fields[3:6], coriolis_wide, x_cells, y_cells)
    state_next = finish(updated, transport_next, active, depth_class, level_block, levels)
    return (state_next, height_next, transport_next)


def solution(mesh):
    placed = (
        P(None, None, "gx", ("gy", "mode")),
        P("gx", ("gy", "mode")),
        P(),
        P("gx", ("gy", "mode")),
        P(None, "gx", ("gy", "mode")),
    )
    return jax.shard_map(
        body,
        mesh=mesh,
        in_specs=placed,
        out_specs=(
            P(None, None, "gx", ("gy", "mode")),
            P("gx", ("gy", "mode")),
            P(None, "gx", ("gy", "mode")),
        ),
        check_vma=False,
    )
```
